128 devices in a mesh: fsdp: 16 (over z, x_lo, core), seq: 8 (over x_hi, y).
Axes of the slice: x: 4 (x_hi: 2, x_lo: 2; x = x_hi * 2 + x_lo), y: 4, z: 4, core: 2. Of those that a mesh axis runs over, the one named last changes fastest.
Arguments:
- hidden_in: bfloat16 [64, 5, 1536], P('fsdp'), may hold values from -6 to 6
- norm_gain: float32 [1536], replicated, may hold values from 0.1 to 1.9
- w_qkv: bfloat16 [1536, 3, 24, 64], P(None, None, 'seq', 'fsdp'), may hold values from -0.15625 to 0.15625
- w_forget: bfloat16 [1536, 24], replicated, may hold values from -0.15625 to 0.15625
- forget_bias: float32 [24], replicated, may hold values from 1 to 5
- cache_keys: bfloat16 [64, 4096, 1536], P('fsdp', 'seq')
- cache_values: bfloat16 [64, 4096, 1536], P('fsdp', 'seq'), may hold values from -6 to 6
- cache_forget: float32 [64, 24, 4096], P('fsdp', None, 'seq')
- cache_lengths: int32 [64], P('fsdp'), may hold values from 128 to 4096, as said below
- piece_map: int32 [64, 8], P('fsdp'), may hold values from 0 to 7, each once within a row
- draft_counts: int32 [64], P('fsdp'), may hold values from 1 to 4
Outputs:
- verified: bfloat16 [64, 5, 1536], P('fsdp', None, 'seq')
The draws below stay inside these ranges and needn't reach their ends.
Inputs may be any that keep to these rules, and one draw needn't show every extreme that they name: `cache_lengths`: 16 requests drawn at random have lengths from 3841 to 4096, one exactly 4096; the others have lengths from 128 to 256, one exactly 128.
All inputs are finite; a program needn't handle non-finite values.
Results may differ from the reference program's by a relative error of at most 0.012.
The reference program's roundings to bfloat16 on the way count: a program that leaves them out, or rounds other values in their place, can miss the bound.
Values may be sent and summed in bfloat16 or wider, within the bound.
No kernel may reach another device: no remote copies, remote signals or barrier semaphores. Data moves between devices by JAX's collectives and lax.ppermute only.
A program may use at most 128 MiB of HBM per device.

```python
import math
import jax
import jax.numpy as jnp
from jax import lax

D = 1536
HEAD_TOTAL = 24
HEAD_DIM = 64
DRAFT = 4
NEW = 5
PIECE_POSITIONS = 512
REQUEST_TOTAL = 64
CACHE_POSITIONS = 4096
N_SEQ = 8


def draw_cache_keys(key, part):
    earlier = jax.random.fold_in(key, 0)
    inner_width = HEAD_TOTAL * HEAD_DIM
    table_entries = jax.random.normal(earlier, (REQUEST_TOTAL, N_SEQ, PIECE_POSITIONS, inner_width), jnp.float32)
    return table_entries.reshape(REQUEST_TOTAL, CACHE_POSITIONS, inner_width).astype(jnp.bfloat16)


def draw_cache_forget(key, part):
    random_subkeys = jax.random.split(key, 5)
    rate_low = math.log(1.0 / (16.0 * CACHE_POSITIONS))
    rate_high = math.log(1.0 / 30.0)
    forget_decay = jnp.exp(jax.random.uniform(random_subkeys[0], (REQUEST_TOTAL, HEAD_TOTAL, 1, 1), jnp.float32, rate_low, rate_high))
    device_multiplier = jnp.exp(jax.random.uniform(random_subkeys[1], (REQUEST_TOTAL, HEAD_TOTAL, N_SEQ, 1), jnp.float32, math.log(0.5), math.log(2.0)))
    random_noise = jax.random.uniform(random_subkeys[2], (REQUEST_TOTAL, HEAD_TOTAL, N_SEQ, PIECE_POSITIONS), jnp.float32, 0.5, 1.5)
    spike_events = jax.random.bernoulli(random_subkeys[3], 3.0 / CACHE_POSITIONS, (REQUEST_TOTAL, HEAD_TOTAL, N_SEQ, PIECE_POSITIONS))
    spike_penalty = jax.random.uniform(random_subkeys[4], (REQUEST_TOTAL, HEAD_TOTAL, N_SEQ, PIECE_POSITIONS), jnp.float32, 0.2, 0.5)
    table_entries = -forget_decay * device_multiplier * random_noise + jnp.where(spike_events, jnp.log1p(-spike_penalty), 0.0)
    return table_entries.reshape(REQUEST_TOTAL, HEAD_TOTAL, CACHE_POSITIONS).astype(jnp.float32)


def draw_cache_lengths(key, part):
    earlier, second, third = jax.random.split(key, 3)
    request_rank = jax.random.permutation(earlier, REQUEST_TOTAL)
    long_len = CACHE_POSITIONS - jax.random.randint(second, (REQUEST_TOTAL,), 0, PIECE_POSITIONS // 2)
    short_len = jax.random.randint(third, (REQUEST_TOTAL,), PIECE_POSITIONS // 4, PIECE_POSITIONS // 2 + 1)
    lengths = jnp.where(request_rank == 0, CACHE_POSITIONS, jnp.where(request_rank < REQUEST_TOTAL // 4, long_len, jnp.where(request_rank == REQUEST_TOTAL // 4, PIECE_POSITIONS // 4, short_len)))
    return lengths.astype(jnp.int32)


def touch_ends(drawn, own_key, smallest, high):
    shape = drawn.shape
    index_at = [jax.random.randint(jax.random.fold_in(own_key, axis), (), 0, shape[axis]) for axis in range(len(shape))]
    drawn = drawn.at[tuple(index_at)].set(smallest)
    longest = shape.index(max(shape))
    index_at[longest] = (index_at[longest] + 1) % shape[longest]
    return drawn.at[tuple(index_at)].set(high)


def shard_levels(rng, shape, shards, low, high):
    level = 1.0
    for axis_at, shards_of in shards:
        steps = jax.random.uniform(jax.random.fold_in(jax.random.fold_in(rng, 6), axis_at), (shards_of,), jnp.float32, low / len(shards), high / len(shards))
        level = level * jnp.repeat(jnp.exp(steps), shape[axis_at] // shards_of).reshape((-1,) + (1,) * (len(shape) - 1 - axis_at))
    return level


def gaussian(rng, shape, spread, bound, shards=(), kind=jnp.bfloat16):
    entries = jax.random.normal(rng, shape, jnp.float32) * spread
    if len(shards) > 0:
        entries = shard_levels(rng, shape, shards, -0.22, 0.18) * entries
    return jnp.clip(entries, min=-bound, max=bound).astype(kind)


def setup_inputs(seed: int = 0) -> dict:
    splits = jax.random.split(jax.random.key(seed), 12)
    hidden_in = gaussian(splits[0], (REQUEST_TOTAL, NEW, D), 1.0, 6.0, ((0, 16),))
    norm_gain = jnp.clip(1.0 + 0.18 * jax.random.normal(splits[1], (D,), jnp.float32), 0.1, 1.9)
    w_qkv = gaussian(splits[2], (D, 3, HEAD_TOTAL, HEAD_DIM), D ** -0.5, 0.15625, ((2, 8), (3, 16)))
    w_forget = gaussian(splits[3], (D, HEAD_TOTAL), D ** -0.5, 0.15625)
    forget_bias = jnp.clip(jax.random.uniform(splits[4], (HEAD_TOTAL,), jnp.float32, 1.0, 5.0), 1.0, 5.0)
    cache_keys = draw_cache_keys(jax.random.fold_in(splits[11], 71), 0)
    cache_values = gaussian(splits[6], (REQUEST_TOTAL, CACHE_POSITIONS, HEAD_TOTAL * HEAD_DIM), 1.0, 6.0, ((0, 16), (1, 8)))
    cache_forget = draw_cache_forget(jax.random.fold_in(splits[11], 71), 0)
    cache_lengths = draw_cache_lengths(jax.random.fold_in(splits[11], 71), 0)
    piece_map = jax.vmap(lambda own: jax.random.permutation(own, N_SEQ))(jax.random.split(splits[9], REQUEST_TOTAL)).reshape((REQUEST_TOTAL, N_SEQ)).astype(jnp.int32)
    draft_counts = touch_ends(jax.random.randint(splits[10], (REQUEST_TOTAL,), 1, DRAFT + 1), jax.random.fold_in(splits[10], 1), 1, DRAFT).astype(jnp.int32)
    return {"hidden_in": hidden_in, "norm_gain": norm_gain, "w_qkv": w_qkv, "w_forget": w_forget, "forget_bias": forget_bias, "cache_keys": cache_keys, "cache_values": cache_values, "cache_forget": cache_forget, "cache_lengths": cache_lengths, "piece_map": piece_map, "draft_counts": draft_counts}


norm_eps = 1e-06
neg_fill = -1e+30

def normalize(rows, gain):
    values = rows.astype(jnp.float32)
    mean_sq = lax.optimization_barrier(jnp.mean(values * values, axis=-1, keepdims=True))
    return (values * lax.rsqrt(mean_sq + norm_eps) * gain).astype(jnp.bfloat16)

def reference(hidden_in, norm_gain, w_qkv, w_forget, forget_bias, cache_keys, cache_values, cache_forget, cache_lengths, piece_map, draft_counts):
    inner_width = HEAD_TOTAL * HEAD_DIM
    normed = normalize(hidden_in, norm_gain).reshape(REQUEST_TOTAL * NEW, D)
    projected = jnp.dot(normed, w_qkv.reshape(D, 3 * inner_width), preferred_element_type=jnp.float32).astype(jnp.bfloat16)
    projected = projected.reshape(REQUEST_TOTAL, NEW, 3, HEAD_TOTAL, HEAD_DIM)
    gate_logit = jnp.dot(normed, w_forget, preferred_element_type=jnp.float32).reshape(REQUEST_TOTAL, NEW, HEAD_TOTAL) + forget_bias
    prefix = jnp.cumsum(jax.nn.log_sigmoid(gate_logit), axis=1)
    logit_scale = HEAD_DIM ** (-0.5)
    step_ids = jnp.arange(NEW, dtype=jnp.int32)
    causal = step_ids[None, :] <= step_ids[:, None]

    def per_request(request_items):
        projected_row, prefix_row, key_rows, value_rows, forget_rows, length, piece_order, draft_count = request_items
        query_rows_all = projected_row[:, 0].astype(jnp.float32)
        fresh_keys = projected_row[:, 1].astype(jnp.float32)
        fresh_values = projected_row[:, 2].astype(jnp.float32)
        key_history = key_rows.reshape(N_SEQ, PIECE_POSITIONS, inner_width)[piece_order].reshape(CACHE_POSITIONS, HEAD_TOTAL, HEAD_DIM).astype(jnp.float32)
        value_history = value_rows.reshape(N_SEQ, PIECE_POSITIONS, inner_width)[piece_order].reshape(CACHE_POSITIONS, HEAD_TOTAL, HEAD_DIM).astype(jnp.float32)
        forget_log = forget_rows.reshape(HEAD_TOTAL, N_SEQ, PIECE_POSITIONS)[:, piece_order].reshape(HEAD_TOTAL, CACHE_POSITIONS)
        live_mask = jnp.arange(CACHE_POSITIONS, dtype=jnp.int32) < length
        masked = jnp.where(live_mask[None, :], forget_log, 0.0)
        trailing_part = lax.optimization_barrier(jnp.sum(masked, axis=-1, keepdims=True)) - jnp.cumsum(masked, axis=-1)
        prefix_transposed = prefix_row.T
        cache_logits = jnp.einsum('cuv,kuv->uck', query_rows_all, key_history) * logit_scale + trailing_part[:, None, :] + prefix_transposed[:, :, None]
        fresh_logits = jnp.einsum('ufq,lfq->ful', query_rows_all, fresh_keys) * logit_scale + prefix_transposed[:, :, None] - prefix_transposed[:, None, :]
        cache_logits = jnp.where(live_mask[None, None, :], cache_logits, neg_fill)
        fresh_logits = jnp.where(causal[None], fresh_logits, neg_fill)
        row_max = jnp.maximum(lax.optimization_barrier(jnp.max(cache_logits, axis=-1)), lax.optimization_barrier(jnp.max(fresh_logits, axis=-1)))
        cache_weights = jnp.where(live_mask[None, None, :], jnp.exp(cache_logits - row_max[..., None]), 0.0)
        new_weights = jnp.where(causal[None], jnp.exp(fresh_logits - row_max[..., None]), 0.0)
        total_sum = lax.optimization_barrier(jnp.sum(cache_weights, axis=-1)) + lax.optimization_barrier(jnp.sum(new_weights, axis=-1))
        cache_rounded = lax.optimization_barrier(cache_weights.astype(jnp.bfloat16)).astype(jnp.float32)
        fresh_rounded = lax.optimization_barrier(new_weights.astype(jnp.bfloat16)).astype(jnp.float32)
        blend_weights = jnp.einsum('slb,bsf->slf', cache_rounded, value_history) + jnp.einsum('zyv,vzs->zys', fresh_rounded, fresh_values)
        result = blend_weights / total_sum[..., None]
        live_rows = step_ids <= draft_count
        result = jnp.where(live_rows[None, :, None], result, 0.0)
        return jnp.transpose(result, (1, 0, 2)).reshape(NEW, inner_width).astype(jnp.bfloat16)
    return lax.map(per_request, (projected, prefix, cache_keys, cache_values, cache_forget, cache_lengths, piece_map, draft_counts))
```

```python
import jax
import jax.numpy as jnp
from jax import lax
from jax.sharding import PartitionSpec as P

HEAD_DIM = 64


norm_eps = 1e-06
neg_fill = -1e30


def normalize(rows, gain):
    values = rows.astype(jnp.float32)
    mean_sq = jnp.mean(values * values, axis=-1, keepdims=True)
    return (values * lax.rsqrt(mean_sq + norm_eps) * gain).astype(jnp.bfloat16)


def body(
    hidden_in,
    norm_gain,
    w_qkv,
    w_forget,
    forget_bias,
    cache_keys,
    cache_values,
    cache_forget,
    cache_lengths,
    piece_map,
    draft_counts,
):
    req_count, new_count, width = hidden_in.shape
    head_count = w_forget.shape[1]
    seq_count = lax.axis_size("seq")
    own_heads = w_qkv.shape[2]
    own_width = own_heads * HEAD_DIM
    piece_len = cache_forget.shape[2]
    logit_scale = HEAD_DIM ** (-0.5)
    seq_index = lax.axis_index("seq")
    head_start = seq_index * own_heads
    normed = normalize(hidden_in, norm_gain).reshape(req_count * new_count, width)
    gate_logit = (
        jnp.dot(normed, w_forget, preferred_element_type=jnp.float32).reshape(
            req_count, new_count, head_count
        )
        + forget_bias
    )
    prefix = jnp.cumsum(jax.nn.log_sigmoid(gate_logit), axis=1)
    projected = jnp.einsum(
        "nd,dchk->nchk",
        normed,
        lax.all_gather(w_qkv, "fsdp", axis=3, tiled=True),
        preferred_element_type=jnp.float32,
    ).astype(jnp.bfloat16)
    own_part = projected.reshape(req_count * new_count, 3, own_width)
    own_query = jnp.broadcast_to(own_part[None, :, 0], (seq_count, req_count * new_count, own_width))
    query_blocks = lax.all_to_all(own_query, "seq", 0, 0, tiled=True)
    query_rows_all = (
        query_blocks.reshape(seq_count, req_count, new_count, own_heads, HEAD_DIM)
        .transpose(1, 2, 0, 3, 4)
        .reshape(req_count, new_count, head_count, HEAD_DIM)
    )
    slot_ids = jnp.arange(seq_count, dtype=jnp.int32)
    holders = piece_map[:, :, None] == slot_ids[None, None, :]
    piece_of_slot = jnp.sum(jnp.where(holders, slot_ids[None, :, None], 0), axis=1)
    own_piece = jnp.sum(jnp.where(piece_map == seq_index, slot_ids[None, :], 0), axis=1)
    positions = own_piece[:, None] * piece_len + jnp.arange(piece_len, dtype=jnp.int32)[None, :]
    live_mask = positions < cache_lengths[:, None]
    masked = jnp.where(live_mask[:, None, :], cache_forget, 0.0)
    piece_total = jnp.sum(masked, axis=-1)
    trailing_part = piece_total[..., None] - jnp.cumsum(masked, axis=-1)
    key_rows = cache_keys.reshape(req_count, piece_len, head_count, HEAD_DIM)
    value_rows = cache_values.reshape(req_count, piece_len, head_count, HEAD_DIM)
    prefix_transposed = jnp.transpose(prefix, (0, 2, 1))
    scores = (
        jnp.einsum("rmhd,rthd->rhmt", query_rows_all, key_rows, preferred_element_type=jnp.float32)
        * logit_scale
    )
    scores = scores + trailing_part[:, :, None, :] + prefix_transposed[..., None]
    key_live = live_mask[:, None, None, :]
    row_max = jnp.max(jnp.where(key_live, scores, neg_fill), axis=-1)
    attn_weights = jnp.where(key_live, jnp.exp(scores - row_max[..., None]), 0.0)
    weight_sum = jnp.sum(attn_weights, axis=-1)
    accum = jnp.einsum(
        "rhmt,rthd->rhmd",
        attn_weights.astype(jnp.bfloat16),
        value_rows,
        preferred_element_type=jnp.float32,
    )
    packed = jnp.concatenate(
        [
            accum,
            row_max[..., None],
            weight_sum[..., None],
            jnp.broadcast_to(piece_total[:, :, None, None], (req_count, head_count, new_count, 1)),
        ],
        axis=-1,
    )
    packed = packed.reshape(req_count, seq_count, own_heads, new_count, HEAD_DIM + 3).transpose(
        1, 0, 2, 3, 4
    )
    parts = lax.all_to_all(packed, "seq", 0, 0, tiled=True)
    part_acc = parts[..., :HEAD_DIM]
    part_max = parts[..., HEAD_DIM]
    part_sum = parts[..., HEAD_DIM + 1]
    part_total = parts[..., 0, HEAD_DIM + 2]
    later_piece = (piece_of_slot.T[None, :, :] > piece_of_slot.T[:, None, :])[..., None]
    later_sum = jnp.sum(jnp.where(later_piece, part_total[None], 0.0), axis=1)
    part_max = part_max + later_sum[..., None]
    cache_max = jnp.max(part_max, axis=0)
    factor = jnp.exp(part_max - cache_max[None])
    cache_sum = jnp.sum(part_sum * factor, axis=0)
    cache_acc = jnp.sum(part_acc * factor[..., None], axis=0)
    own_rows = own_part.reshape(req_count, new_count, 3, own_heads, HEAD_DIM)
    own_prefix = jnp.transpose(
        lax.dynamic_slice_in_dim(prefix, head_start, own_heads, 2), (0, 2, 1)
    )
    fresh_logits = (
        jnp.einsum(
            "rmhd,rnhd->rhmn",
            own_rows[:, :, 0],
            own_rows[:, :, 1],
            preferred_element_type=jnp.float32,
        )
        * logit_scale
    )
    fresh_logits = fresh_logits + own_prefix[..., :, None] - own_prefix[..., None, :]
    step_ids = jnp.arange(new_count, dtype=jnp.int32)
    causal = (step_ids[None, :] <= step_ids[:, None])[None, None]
    joint_max = jnp.maximum(cache_max, jnp.max(jnp.where(causal, fresh_logits, neg_fill), axis=-1))
    new_weights = jnp.where(causal, jnp.exp(fresh_logits - joint_max[..., None]), 0.0)
    carried = jnp.exp(cache_max - joint_max)
    total_sum = cache_sum * carried + jnp.sum(new_weights, axis=-1)
    blend_weights = cache_acc * carried[..., None] + jnp.einsum(
        "rhmn,rnhd->rhmd",
        new_weights.astype(jnp.bfloat16),
        own_rows[:, :, 2],
        preferred_element_type=jnp.float32,
    )
    result = blend_weights / total_sum[..., None]
    live_rows = (step_ids[None, :] <= draft_counts[:, None])[:, None, :, None]
    result = jnp.where(live_rows, result, 0.0)
    return (
        jnp.transpose(result, (0, 2, 1, 3))
        .reshape(req_count, new_count, own_heads * HEAD_DIM)
        .astype(jnp.bfloat16)
    )


def solution(mesh):
    in_specs = (
        P("fsdp", None, None),
        P(),
        P(None, None, "seq", "fsdp"),
        P(),
        P(),
        P("fsdp", "seq", None),
        P("fsdp", "seq", None),
        P("fsdp", None, "seq"),
        P("fsdp"),
        P("fsdp", None),
        P("fsdp"),
    )
    out_specs = P("fsdp", None, "seq")
    return jax.shard_map(body, mesh=mesh, in_specs=in_specs, out_specs=out_specs, check_vma=False)
```

```python
import jax
import jax.numpy as jnp
from jax import lax
from jax.sharding import PartitionSpec as P

HEAD_DIM = 64


norm_eps = 1e-06
neg_fill = -1e30


def normalize(rows, gain):
    values = rows.astype(jnp.float32)
    mean_sq = jnp.mean(values * values, axis=-1, keepdims=True)
    return (values * lax.rsqrt(mean_sq + norm_eps) * gain).astype(jnp.bfloat16)


def body(
    hidden_in,
    norm_gain,
    w_qkv,
    w_forget,
    forget_bias,
    cache_keys,
    cache_values,
    cache_forget,
    cache_lengths,
    piece_map,
    draft_counts,
):
    req_count, new_count, width = hidden_in.shape
    head_count = w_forget.shape[1]
    seq_count = lax.axis_size("seq")
    fsdp_count = lax.axis_size("fsdp")
    own_heads = w_qkv.shape[2]
    own_dims = w_qkv.shape[3]
    piece_len = cache_forget.shape[2]
    logit_scale = HEAD_DIM ** (-0.5)
    seq_index = lax.axis_index("seq")
    head_start = seq_index * own_heads
    hidden_all = lax.all_to_all(
        jnp.broadcast_to(hidden_in[None], (fsdp_count, req_count, new_count, width)),
        "fsdp",
        0,
        0,
        tiled=True,
    )
    normed_all = normalize(hidden_all, norm_gain).reshape(fsdp_count * req_count * new_count, width)
    projected = jnp.einsum(
        "nd,dchk->nchk", normed_all, w_qkv, preferred_element_type=jnp.float32
    ).astype(jnp.bfloat16)
    projected = projected.reshape(fsdp_count, 1, req_count, new_count, 3, own_heads, own_dims)
    outgoing = jnp.broadcast_to(
        projected, (fsdp_count, seq_count, req_count, new_count, 3, own_heads, own_dims)
    ).reshape(fsdp_count * seq_count, req_count, new_count, 3, own_heads, own_dims)
    incoming = lax.all_to_all(outgoing, ("fsdp", "seq"), 0, 0, tiled=True)
    all_heads = (
        incoming.reshape(fsdp_count, seq_count, req_count, new_count, 3, own_heads, own_dims)
        .transpose(2, 3, 4, 1, 5, 0, 6)
        .reshape(req_count, new_count, 3, head_count, HEAD_DIM)
    )
    normed = normalize(hidden_in, norm_gain).reshape(req_count * new_count, width)
    gate_logit = (
        jnp.dot(normed, w_forget, preferred_element_type=jnp.float32).reshape(
            req_count, new_count, head_count
        )
        + forget_bias
    )
    prefix = jnp.cumsum(jax.nn.log_sigmoid(gate_logit), axis=1)
    slot_ids = jnp.arange(seq_count, dtype=jnp.int32)
    holders = piece_map[:, :, None] == slot_ids[None, None, :]
    piece_of_slot = jnp.sum(jnp.where(holders, slot_ids[None, :, None], 0), axis=1)
    own_piece = jnp.sum(jnp.where(piece_map == seq_index, slot_ids[None, :], 0), axis=1)
    steps = jnp.arange(piece_len, dtype=jnp.int32)
    positions = own_piece[:, None] * piece_len + steps[None, :]
    live_mask = positions < cache_lengths[:, None]
    masked = jnp.where(live_mask[:, None, :], cache_forget, 0.0)
    piece_total = jnp.sum(masked, axis=-1)
    later_step = (steps[:, None] > steps[None, :]).astype(jnp.float32)
    trailing_part = jnp.einsum(
        "rhl,lj->rhj", masked, later_step, precision=lax.Precision.HIGHEST,
        preferred_element_type=jnp.float32,
    )
    prefix_transposed = jnp.transpose(prefix, (0, 2, 1))
    head_eye = jnp.eye(head_count, dtype=jnp.bfloat16)
    query_rows = jnp.transpose(all_heads[:, :, 0], (0, 2, 1, 3))
    query_blocks = (
        query_rows[:, :, :, None, :] * head_eye[None, :, None, :, None]
    ).reshape(req_count, head_count * new_count, head_count * HEAD_DIM)
    scores = (
        jnp.einsum("rnc,rtc->rnt", query_blocks, cache_keys, preferred_element_type=jnp.float32)
        * logit_scale
    ).reshape(req_count, head_count, new_count, piece_len)
    scores = scores + trailing_part[:, :, None, :] + prefix_transposed[..., None]
    key_live = live_mask[:, None, None, :]
    row_max = jnp.max(jnp.where(key_live, scores, neg_fill), axis=-1)
    attn_weights = jnp.where(key_live, jnp.exp(scores - row_max[..., None]), 0.0)
    weight_sum = jnp.sum(attn_weights, axis=-1)
    accum_blocks = jnp.einsum(
        "rnt,rtc->rnc",
        attn_weights.astype(jnp.bfloat16).reshape(req_count, head_count * new_count, piece_len),
        cache_values,
        preferred_element_type=jnp.float32,
    ).reshape(req_count, head_count, new_count, head_count, HEAD_DIM)
    accum = jnp.sum(
        accum_blocks * head_eye.astype(jnp.float32)[None, :, None, :, None], axis=3
    )
    packed = jnp.concatenate(
        [
            accum,
            row_max[..., None],
            weight_sum[..., None],
            jnp.broadcast_to(piece_total[:, :, None, None], (req_count, head_count, new_count, 1)),
        ],
        axis=-1,
    )
    packed = packed.reshape(req_count, seq_count, own_heads, new_count, HEAD_DIM + 3).transpose(
        1, 0, 2, 3, 4
    )
    parts = lax.all_to_all(packed, "seq", 0, 0, tiled=True)
    part_acc = parts[..., :HEAD_DIM]
    part_max = parts[..., HEAD_DIM]
    part_sum = parts[..., HEAD_DIM + 1]
    part_total = parts[..., 0, HEAD_DIM + 2]
    later_piece = (piece_of_slot.T[None, :, :] > piece_of_slot.T[:, None, :])[..., None]
    later_sum = jnp.sum(jnp.where(later_piece, part_total[None], 0.0), axis=1)
    part_max = part_max + later_sum[..., None]
    cache_max = jnp.max(part_max, axis=0)
    factor = jnp.exp(part_max - cache_max[None])
    cache_sum = jnp.sum(part_sum * factor, axis=0)
    cache_acc = jnp.sum(part_acc * factor[..., None], axis=0)
    own_rows = lax.dynamic_slice_in_dim(all_heads, head_start, own_heads, 3)
    own_prefix = jnp.transpose(
        lax.dynamic_slice_in_dim(prefix, head_start, own_heads, 2), (0, 2, 1)
    )
    fresh_logits = (
        jnp.einsum(
            "rmhd,rnhd->rhmn",
            own_rows[:, :, 0],
            own_rows[:, :, 1],
            preferred_element_type=jnp.float32,
        )
        * logit_scale
    )
    fresh_logits = fresh_logits + own_prefix[..., :, None] - own_prefix[..., None, :]
    step_ids = jnp.arange(new_count, dtype=jnp.int32)
    causal = (step_ids[None, :] <= step_ids[:, None])[None, None]
    joint_max = jnp.maximum(cache_max, jnp.max(jnp.where(causal, fresh_logits, neg_fill), axis=-1))
    new_weights = jnp.where(causal, jnp.exp(fresh_logits - joint_max[..., None]), 0.0)
    carried = jnp.exp(cache_max - joint_max)
    total_sum = cache_sum * carried + jnp.sum(new_weights, axis=-1)
    blend_weights = cache_acc * carried[..., None] + jnp.einsum(
        "rhmn,rnhd->rhmd",
        new_weights.astype(jnp.bfloat16),
        own_rows[:, :, 2],
        preferred_element_type=jnp.float32,
    )
    result = blend_weights / total_sum[..., None]
    live_rows = (step_ids[None, :] <= draft_counts[:, None])[:, None, :, None]
    result = jnp.where(live_rows, result, 0.0)
    return (
        jnp.transpose(result, (0, 2, 1, 3))
        .reshape(req_count, new_count, own_heads * HEAD_DIM)
        .astype(jnp.bfloat16)
    )


def solution(mesh):
    in_specs = (
        P("fsdp", None, None),
        P(),
        P(None, None, "seq", "fsdp"),
        P(),
        P(),
        P("fsdp", "seq", None),
        P("fsdp", "seq", None),
        P("fsdp", None, "seq"),
        P("fsdp"),
        P("fsdp", None),
        P("fsdp"),
    )
    out_specs = P("fsdp", None, "seq")
    return jax.shard_map(body, mesh=mesh, in_specs=in_specs, out_specs=out_specs, check_vma=False)
```

```python
import jax
import jax.numpy as jnp
from jax import lax
from jax.sharding import PartitionSpec as P

HEAD_DIM = 64


norm_eps = 1e-06
neg_fill = -1e30


def normalize(rows, gain):
    values = rows.astype(jnp.float32)
    mean_sq = jnp.mean(values * values, axis=-1, keepdims=True)
    return (values * lax.rsqrt(mean_sq + norm_eps) * gain).astype(jnp.bfloat16)


def body(
    hidden_in,
    norm_gain,
    w_qkv,
    w_forget,
    forget_bias,
    cache_keys,
    cache_values,
    cache_forget,
    cache_lengths,
    piece_map,
    draft_counts,
):
    req_count, new_count, width = hidden_in.shape
    head_count = w_forget.shape[1]
    seq_count = lax.axis_size("seq")
    fsdp_count = lax.axis_size("fsdp")
    own_heads = w_qkv.shape[2]
    own_dims = w_qkv.shape[3]
    own_cols = 3 * own_heads * own_dims
    rows = req_count * new_count
    inner_width = head_count * HEAD_DIM
    piece_len = cache_forget.shape[2]
    logit_scale = HEAD_DIM ** (-0.5)
    seq_index = lax.axis_index("seq")
    head_start = seq_index * own_heads
    hidden_all = lax.all_to_all(
        jnp.broadcast_to(hidden_in[None], (fsdp_count, req_count, new_count, width)),
        "fsdp",
        0,
        0,
        tiled=True,
    )
    normed_all = normalize(hidden_all, norm_gain).reshape(fsdp_count * rows, width)
    projected = jnp.einsum(
        "dk,nd->kn",
        w_qkv.reshape(width, own_cols),
        normed_all,
        preferred_element_type=jnp.float32,
    ).astype(jnp.bfloat16)
    outgoing = (
        projected.reshape(3, own_heads * own_dims, fsdp_count, rows)
        .transpose(2, 1, 0, 3)
        .reshape(fsdp_count, 1, own_heads * own_dims * 3 * rows)
    )
    outgoing = jnp.broadcast_to(
        outgoing, (fsdp_count, seq_count, own_heads * own_dims * 3 * rows)
    ).reshape(fsdp_count * seq_count, own_heads * own_dims * 3 * rows)
    incoming = lax.all_to_all(outgoing, ("fsdp", "seq"), 0, 0, tiled=True)
    incoming = incoming.reshape(fsdp_count * seq_count * own_heads * own_dims, 3 * rows)
    src_row = jnp.arange(fsdp_count * seq_count * own_heads * own_dims, dtype=jnp.int32)
    src_dev = src_row // (own_heads * own_dims)
    src_head = (src_row // own_dims) % own_heads
    src_dim = src_row % own_dims
    target = ((src_dev % seq_count) * own_heads + src_head) * HEAD_DIM + (
        src_dev // seq_count
    ) * own_dims + src_dim
    placement = (target[:, None] == jnp.arange(inner_width, dtype=jnp.int32)[None, :]).astype(
        jnp.bfloat16
    )
    all_heads = jnp.einsum(
        "kx,kj->xj", incoming, placement, preferred_element_type=jnp.float32
    ).astype(jnp.bfloat16).reshape(3, req_count, new_count, inner_width)
    normed = normalize(hidden_in, norm_gain).reshape(rows, width)
    gate_logit = (
        jnp.dot(normed, w_forget, preferred_element_type=jnp.float32).reshape(
            req_count, new_count, head_count
        )
        + forget_bias
    )
    prefix = jnp.cumsum(jax.nn.log_sigmoid(gate_logit), axis=1)
    slot_ids = jnp.arange(seq_count, dtype=jnp.int32)
    holders = piece_map[:, :, None] == slot_ids[None, None, :]
    piece_of_slot = jnp.sum(jnp.where(holders, slot_ids[None, :, None], 0), axis=1)
    own_piece = jnp.sum(jnp.where(piece_map == seq_index, slot_ids[None, :], 0), axis=1)
    steps = jnp.arange(piece_len, dtype=jnp.int32)
    positions = own_piece[:, None] * piece_len + steps[None, :]
    live_mask = positions < cache_lengths[:, None]
    masked = jnp.where(live_mask[:, None, :], cache_forget, 0.0)
    piece_total = jnp.sum(masked, axis=-1)
    later_step = (steps[:, None] > steps[None, :]).astype(jnp.float32)
    trailing_part = jnp.einsum(
        "rhl,lj->rhj", masked, later_step, precision=lax.Precision.HIGHEST,
        preferred_element_type=jnp.float32,
    )
    col_head = jnp.arange(inner_width, dtype=jnp.int32) // HEAD_DIM
    head_mask = col_head[None, :] == jnp.arange(head_count, dtype=jnp.int32)[:, None]
    query_blocks = jnp.where(head_mask[None, None], all_heads[0][:, :, None, :], 0).reshape(
        req_count, new_count * head_count, inner_width
    )
    scores = (
        jnp.einsum("rnc,rtc->rnt", query_blocks, cache_keys, preferred_element_type=jnp.float32)
        * logit_scale
    ).reshape(req_count, new_count, head_count, piece_len)
    scores = scores + trailing_part[:, None, :, :] + prefix[..., None]
    key_live = live_mask[:, None, None, :]
    row_max = jnp.max(jnp.where(key_live, scores, neg_fill), axis=-1)
    attn_weights = jnp.where(key_live, jnp.exp(scores - row_max[..., None]), 0.0)
    weight_sum = jnp.sum(attn_weights, axis=-1)
    accum_blocks = jnp.einsum(
        "rnt,rtc->rnc",
        attn_weights.astype(jnp.bfloat16).reshape(req_count, new_count * head_count, piece_len),
        cache_values,
        preferred_element_type=jnp.float32,
    ).reshape(req_count, new_count, head_count, inner_width)
    fold = (
        (jnp.arange(inner_width, dtype=jnp.int32) % HEAD_DIM)[:, None]
        == jnp.arange(HEAD_DIM, dtype=jnp.int32)[None, :]
    ).astype(jnp.float32)
    accum = jnp.einsum(
        "rmhc,cd->rmhd",
        jnp.where(head_mask[None, None], accum_blocks, 0.0),
        fold,
        precision=lax.Precision.HIGHEST,
        preferred_element_type=jnp.float32,
    )
    packed = jnp.concatenate(
        [
            accum,
            row_max[..., None],
            weight_sum[..., None],
            jnp.broadcast_to(piece_total[:, None, :, None], (req_count, new_count, head_count, 1)),
        ],
        axis=-1,
    )
    packed = packed.reshape(req_count, new_count, seq_count, own_heads, HEAD_DIM + 3).transpose(
        2, 0, 1, 3, 4
    )
    parts = lax.all_to_all(packed, "seq", 0, 0, tiled=True)
    part_acc = parts[..., :HEAD_DIM]
    part_max = parts[..., HEAD_DIM]
    part_sum = parts[..., HEAD_DIM + 1]
    part_total = parts[:, :, 0, :, HEAD_DIM + 2]
    later_piece = (piece_of_slot.T[None, :, :] > piece_of_slot.T[:, None, :])[..., None]
    later_sum = jnp.sum(jnp.where(later_piece, part_total[None], 0.0), axis=1)
    part_max = part_max + later_sum[:, :, None, :]
    cache_max = jnp.max(part_max, axis=0)
    factor = jnp.exp(part_max - cache_max[None])
    cache_sum = jnp.sum(part_sum * factor, axis=0)
    cache_acc = jnp.sum(part_acc * factor[..., None], axis=0)
    own_rows = lax.dynamic_slice_in_dim(
        all_heads, head_start * HEAD_DIM, own_heads * HEAD_DIM, 3
    ).reshape(3, req_count, new_count, own_heads, HEAD_DIM)
    own_prefix = lax.dynamic_slice_in_dim(prefix, head_start, own_heads, 2)
    fresh_logits = (
        jnp.einsum(
            "rmhd,rnhd->rmhn",
            own_rows[0],
            own_rows[1],
            preferred_element_type=jnp.float32,
        )
        * logit_scale
    )
    fresh_logits = (
        fresh_logits + own_prefix[..., None] - jnp.transpose(own_prefix, (0, 2, 1))[:, None, :, :]
    )
    step_ids = jnp.arange(new_count, dtype=jnp.int32)
    causal = (step_ids[None, :] <= step_ids[:, None])[None, :, None, :]
    joint_max = jnp.maximum(cache_max, jnp.max(jnp.where(causal, fresh_logits, neg_fill), axis=-1))
    new_weights = jnp.where(causal, jnp.exp(fresh_logits - joint_max[..., None]), 0.0)
    carried = jnp.exp(cache_max - joint_max)
    total_sum = cache_sum * carried + jnp.sum(new_weights, axis=-1)
    blend_weights = cache_acc * carried[..., None] + jnp.einsum(
        "rmhn,rnhd->rmhd",
        new_weights.astype(jnp.bfloat16),
        own_rows[2],
        preferred_element_type=jnp.float32,
    )
    result = blend_weights / total_sum[..., None]
    live_rows = (step_ids[None, :] <= draft_counts[:, None])[:, :, None, None]
    result = jnp.where(live_rows, result, 0.0)
    return result.reshape(req_count, new_count, own_heads * HEAD_DIM).astype(jnp.bfloat16)


def solution(mesh):
    in_specs = (
        P("fsdp", None, None),
        P(),
        P(None, None, "seq", "fsdp"),
        P(),
        P(),
        P("fsdp", "seq", None),
        P("fsdp", "seq", None),
        P("fsdp", None, "seq"),
        P("fsdp"),
        P("fsdp", None),
        P("fsdp"),
    )
    out_specs = P("fsdp", None, "seq")
    return jax.shard_map(body, mesh=mesh, in_specs=in_specs, out_specs=out_specs, check_vma=False)
```

```python
import functools

import jax
import jax.numpy as jnp
from jax import lax
from jax.experimental import pallas as pl
from jax.experimental.pallas import tpu as pltpu
from jax.sharding import PartitionSpec as P

HEAD_DIM = 64


norm_eps = 1e-06
neg_fill = -1e30


def normalize(rows, gain):
    values = rows.astype(jnp.float32)
    mean_sq = jnp.mean(values * values, axis=-1, keepdims=True)
    return (values * lax.rsqrt(mean_sq + norm_eps) * gain).astype(jnp.bfloat16)


def attention_kernel(q_ref, k_ref, v_ref, bias_ref, live_ref, total_ref, out_ref, *, new_count):
    row_count = q_ref.shape[1]
    pair_count = v_ref.shape[2] // 128
    scores = lax.dot_general(
        q_ref[0], k_ref[0], (((1,), (1,)), ((), ())), preferred_element_type=jnp.float32
    )
    scores = scores * (HEAD_DIM ** (-0.5)) + bias_ref[0]
    live = live_ref[0] > 0.5
    row_max = jnp.max(jnp.where(live, scores, neg_fill), axis=1, keepdims=True)
    weights = jnp.where(live, jnp.exp(scores - row_max), 0.0)
    weight_sum = jnp.sum(weights, axis=1, keepdims=True)
    blocks = jnp.dot(weights.astype(jnp.bfloat16), v_ref[0], preferred_element_type=jnp.float32)
    row = lax.broadcasted_iota(jnp.int32, (row_count, 128), 0)
    picked = jnp.zeros((row_count, 128), jnp.float32)
    odd = row < 0
    for pair in range(pair_count):
        lo = 2 * pair * new_count
        picked = jnp.where(
            (row >= lo) & (row < lo + 2 * new_count), blocks[:, pair * 128 : (pair + 1) * 128], picked
        )
        odd = odd | ((row >= lo + new_count) & (row < lo + 2 * new_count))
    accum = jnp.where(odd, pltpu.roll(picked, 64, 1), picked)
    lane = lax.broadcasted_iota(jnp.int32, (row_count, 128), 1)
    packed = jnp.where(lane < HEAD_DIM, accum, 0.0)
    packed = jnp.where(lane == HEAD_DIM, row_max, packed)
    packed = jnp.where(lane == HEAD_DIM + 1, weight_sum, packed)
    packed = jnp.where(lane == HEAD_DIM + 2, total_ref[0], packed)
    out_ref[0] = packed


def piece_attention(query_blocks, keys, values, bias, live_row, total_row, new_count):
    req_count, row_count, inner_width = query_blocks.shape
    piece_len = keys.shape[1]
    return pl.pallas_call(
        functools.partial(attention_kernel, new_count=new_count),
        grid=(req_count,),
        in_specs=[
            pl.BlockSpec((1, row_count, inner_width), lambda r: (r, 0, 0)),
            pl.BlockSpec((1, piece_len, inner_width), lambda r: (r, 0, 0)),
            pl.BlockSpec((1, piece_len, inner_width), lambda r: (r, 0, 0)),
            pl.BlockSpec((1, row_count, piece_len), lambda r: (r, 0, 0)),
            pl.BlockSpec((1, 1, piece_len), lambda r: (r, 0, 0)),
            pl.BlockSpec((1, row_count, 1), lambda r: (r, 0, 0)),
        ],
        out_specs=pl.BlockSpec((1, row_count, 128), lambda r: (r, 0, 0)),
        out_shape=jax.ShapeDtypeStruct((req_count, row_count, 128), jnp.float32),
    )(query_blocks, keys, values, bias, live_row, total_row)


def body(
    hidden_in,
    norm_gain,
    w_qkv,
    w_forget,
    forget_bias,
    cache_keys,
    cache_values,
    cache_forget,
    cache_lengths,
    piece_map,
    draft_counts,
):
    req_count, new_count, width = hidden_in.shape
    head_count = w_forget.shape[1]
    seq_count = lax.axis_size("seq")
    fsdp_count = lax.axis_size("fsdp")
    own_heads = w_qkv.shape[2]
    own_dims = w_qkv.shape[3]
    own_cols = 3 * own_heads * own_dims
    rows = req_count * new_count
    inner_width = head_count * HEAD_DIM
    piece_len = cache_forget.shape[2]
    logit_scale = HEAD_DIM ** (-0.5)
    seq_index = lax.axis_index("seq")
    head_start = seq_index * own_heads
    hidden_all = lax.all_to_all(
        jnp.broadcast_to(hidden_in[None], (fsdp_count, req_count, new_count, width)),
        "fsdp",
        0,
        0,
        tiled=True,
    )
    normed_all = normalize(hidden_all, norm_gain).reshape(fsdp_count * rows, width)
    projected = jnp.einsum(
        "dk,nd->kn",
        w_qkv.reshape(width, own_cols),
        normed_all,
        preferred_element_type=jnp.float32,
    ).astype(jnp.bfloat16)
    outgoing = (
        projected.reshape(3, own_heads * own_dims, fsdp_count, rows)
        .transpose(2, 1, 0, 3)
        .reshape(fsdp_count, 1, own_heads * own_dims * 3 * rows)
    )
    outgoing = jnp.broadcast_to(
        outgoing, (fsdp_count, seq_count, own_heads * own_dims * 3 * rows)
    ).reshape(fsdp_count * seq_count, own_heads * own_dims * 3 * rows)
    incoming = lax.all_to_all(outgoing, ("fsdp", "seq"), 0, 0, tiled=True)
    incoming = incoming.reshape(fsdp_count * seq_count * own_heads * own_dims, 3 * rows)
    src_row = jnp.arange(fsdp_count * seq_count * own_heads * own_dims, dtype=jnp.int32)
    src_dev = src_row // (own_heads * own_dims)
    src_head = (src_row // own_dims) % own_heads
    src_dim = src_row % own_dims
    target = ((src_dev % seq_count) * own_heads + src_head) * HEAD_DIM + (
        src_dev // seq_count
    ) * own_dims + src_dim
    placement = (target[:, None] == jnp.arange(inner_width, dtype=jnp.int32)[None, :]).astype(
        jnp.bfloat16
    )
    all_heads = jnp.einsum(
        "kx,kj->xj", incoming, placement, preferred_element_type=jnp.float32
    ).astype(jnp.bfloat16).reshape(3, req_count, new_count, inner_width)
    normed = normalize(hidden_in, norm_gain).reshape(rows, width)
    gate_logit = (
        jnp.dot(normed, w_forget, preferred_element_type=jnp.float32).reshape(
            req_count, new_count, head_count
        )
        + forget_bias
    )
    prefix = jnp.cumsum(jax.nn.log_sigmoid(gate_logit), axis=1)
    slot_ids = jnp.arange(seq_count, dtype=jnp.int32)
    holders = piece_map[:, :, None] == slot_ids[None, None, :]
    piece_of_slot = jnp.sum(jnp.where(holders, slot_ids[None, :, None], 0), axis=1)
    own_piece = jnp.sum(jnp.where(piece_map == seq_index, slot_ids[None, :], 0), axis=1)
    steps = jnp.arange(piece_len, dtype=jnp.int32)
    positions = own_piece[:, None] * piece_len + steps[None, :]
    live_mask = positions < cache_lengths[:, None]
    masked = jnp.where(live_mask[:, None, :], cache_forget, 0.0)
    piece_total = jnp.sum(masked, axis=-1)
    later_step = (steps[:, None] > steps[None, :]).astype(jnp.float32)
    trailing_part = jnp.einsum(
        "rhl,lj->rhj", masked, later_step, precision=lax.Precision.HIGHEST,
        preferred_element_type=jnp.float32,
    )
    col_head = jnp.arange(inner_width, dtype=jnp.int32) // HEAD_DIM
    head_mask = col_head[None, :] == jnp.arange(head_count, dtype=jnp.int32)[:, None]
    query_blocks = jnp.where(
        head_mask[None, :, None, :], all_heads[0][:, None, :, :], 0
    ).reshape(req_count, head_count * new_count, inner_width)
    bias = (trailing_part[:, :, None, :] + jnp.transpose(prefix, (0, 2, 1))[..., None]).reshape(
        req_count, head_count * new_count, piece_len
    )
    live_row = live_mask.astype(jnp.float32)[:, None, :]
    total_row = jnp.broadcast_to(
        piece_total[:, :, None], (req_count, head_count, new_count)
    ).reshape(req_count, head_count * new_count, 1)
    packed = piece_attention(query_blocks, cache_keys, cache_values, bias, live_row, total_row, new_count)
    packed = packed.reshape(req_count, seq_count, own_heads, new_count, 128).transpose(1, 0, 2, 3, 4)
    parts = lax.all_to_all(packed, "seq", 0, 0, tiled=True)
    part_acc = parts[..., :HEAD_DIM]
    part_max = parts[..., HEAD_DIM]
    part_sum = parts[..., HEAD_DIM + 1]
    part_total = parts[:, :, :, 0, HEAD_DIM + 2]
    later_piece = (piece_of_slot.T[None, :, :] > piece_of_slot.T[:, None, :])[..., None]
    later_sum = jnp.sum(jnp.where(later_piece, part_total[None], 0.0), axis=1)
    part_max = part_max + later_sum[..., None]
    cache_max = jnp.max(part_max, axis=0)
    factor = jnp.exp(part_max - cache_max[None])
    cache_sum = jnp.sum(part_sum * factor, axis=0)
    cache_acc = jnp.sum(part_acc * factor[..., None], axis=0)
    own_rows = lax.dynamic_slice_in_dim(
        all_heads, head_start * HEAD_DIM, own_heads * HEAD_DIM, 3
    ).reshape(3, req_count, new_count, own_heads, HEAD_DIM)
    own_prefix = jnp.transpose(
        lax.dynamic_slice_in_dim(prefix, head_start, own_heads, 2), (0, 2, 1)
    )
    fresh_logits = (
        jnp.einsum(
            "rmhd,rnhd->rhmn",
            own_rows[0],
            own_rows[1],
            preferred_element_type=jnp.float32,
        )
        * logit_scale
    )
    fresh_logits = fresh_logits + own_prefix[..., :, None] - own_prefix[..., None, :]
    step_ids = jnp.arange(new_count, dtype=jnp.int32)
    causal = (step_ids[None, :] <= step_ids[:, None])[None, None]
    joint_max = jnp.maximum(cache_max, jnp.max(jnp.where(causal, fresh_logits, neg_fill), axis=-1))
    new_weights = jnp.where(causal, jnp.exp(fresh_logits - joint_max[..., None]), 0.0)
    carried = jnp.exp(cache_max - joint_max)
    total_sum = cache_sum * carried + jnp.sum(new_weights, axis=-1)
    blend_weights = cache_acc * carried[..., None] + jnp.einsum(
        "rhmn,rnhd->rhmd",
        new_weights.astype(jnp.bfloat16),
        own_rows[2],
        preferred_element_type=jnp.float32,
    )
    result = blend_weights / total_sum[..., None]
    live_rows = (step_ids[None, :] <= draft_counts[:, None])[:, None, :, None]
    result = jnp.where(live_rows, result, 0.0)
    return (
        jnp.transpose(result, (0, 2, 1, 3))
        .reshape(req_count, new_count, own_heads * HEAD_DIM)
        .astype(jnp.bfloat16)
    )


def solution(mesh):
    in_specs = (
        P("fsdp", None, None),
        P(),
        P(None, None, "seq", "fsdp"),
        P(),
        P(),
        P("fsdp", "seq", None),
        P("fsdp", "seq", None),
        P("fsdp", None, "seq"),
        P("fsdp"),
        P("fsdp", None),
        P("fsdp"),
    )
    out_specs = P("fsdp", None, "seq")
    return jax.shard_map(body, mesh=mesh, in_specs=in_specs, out_specs=out_specs, check_vma=False)
```

```python
import jax
import jax.numpy as jnp
from jax import lax
from jax.experimental import pallas as pl
from jax.experimental.pallas import tpu as pltpu
from jax.sharding import PartitionSpec as P

HEAD_DIM = 64


norm_eps = 1e-06
neg_fill = -1e30


def normalize(rows, gain):
    values = rows.astype(jnp.float32)
    mean_sq = jnp.mean(values * values, axis=-1, keepdims=True)
    return (values * lax.rsqrt(mean_sq + norm_eps) * gain).astype(jnp.bfloat16)


def attention_kernel(q_ref, k_ref, v_ref, trail_ref, prefix_ref, live_ref, total_ref, out_ref):
    step_rows = q_ref.shape[1]
    head_count = trail_ref.shape[1]
    piece_len = trail_ref.shape[2]
    inner_width = q_ref.shape[2]
    row_count = head_count * step_rows
    pair_count = inner_width // 128
    row_step = lax.broadcasted_iota(jnp.int32, (row_count, step_rows), 0) % step_rows
    spread = (row_step == lax.broadcasted_iota(jnp.int32, (row_count, step_rows), 1)).astype(jnp.bfloat16)
    repeated = jnp.dot(spread, q_ref[0], preferred_element_type=jnp.float32)
    row_head = lax.broadcasted_iota(jnp.int32, (row_count, inner_width), 0) // step_rows
    col_head = lax.broadcasted_iota(jnp.int32, (row_count, inner_width), 1) // HEAD_DIM
    query_blocks = jnp.where(row_head == col_head, repeated, 0.0).astype(jnp.bfloat16)
    scores = lax.dot_general(
        query_blocks, k_ref[0], (((1,), (1,)), ((), ())), preferred_element_type=jnp.float32
    )
    trailing = jnp.broadcast_to(
        trail_ref[0][:, None, :], (head_count, step_rows, piece_len)
    ).reshape(row_count, piece_len)
    scores = scores * (HEAD_DIM ** (-0.5)) + (trailing + prefix_ref[0])
    live = live_ref[0] > 0.5
    row_max = jnp.max(jnp.where(live, scores, neg_fill), axis=1, keepdims=True)
    weights = jnp.where(live, jnp.exp(scores - row_max), 0.0)
    weight_sum = jnp.sum(weights, axis=1, keepdims=True)
    blocks = jnp.dot(weights.astype(jnp.bfloat16), v_ref[0], preferred_element_type=jnp.float32)
    row = lax.broadcasted_iota(jnp.int32, (row_count, 128), 0)
    picked = jnp.zeros((row_count, 128), jnp.float32)
    for pair in range(pair_count):
        lo = 2 * pair * step_rows
        picked = jnp.where(
            (row >= lo) & (row < lo + 2 * step_rows), blocks[:, pair * 128 : (pair + 1) * 128], picked
        )
    odd = (row // step_rows) % 2 == 1
    accum = jnp.where(odd, pltpu.roll(picked, 64, 1), picked)
    lane = lax.broadcasted_iota(jnp.int32, (row_count, 128), 1)
    packed = jnp.where(lane < HEAD_DIM, accum, 0.0)
    packed = jnp.where(lane == HEAD_DIM, row_max, packed)
    packed = jnp.where(lane == HEAD_DIM + 1, weight_sum, packed)
    packed = jnp.where(lane == HEAD_DIM + 2, total_ref[0], packed)
    own_heads = out_ref.shape[2]
    for head in range(head_count):
        out_ref[head // own_heads, 0, head % own_heads] = packed[head * step_rows : (head + 1) * step_rows]


def piece_attention(query_rows, keys, values, trailing, prefix_rows, live_row, total_rows, seq_count):
    req_count, step_rows, inner_width = query_rows.shape
    head_count = trailing.shape[1]
    piece_len = keys.shape[1]
    row_count = head_count * step_rows
    own_heads = head_count // seq_count
    return pl.pallas_call(
        attention_kernel,
        grid=(req_count,),
        in_specs=[
            pl.BlockSpec((1, step_rows, inner_width), lambda r: (r, 0, 0)),
            pl.BlockSpec((1, piece_len, inner_width), lambda r: (r, 0, 0)),
            pl.BlockSpec((1, piece_len, inner_width), lambda r: (r, 0, 0)),
            pl.BlockSpec((1, head_count, piece_len), lambda r: (r, 0, 0)),
            pl.BlockSpec((1, row_count, 1), lambda r: (r, 0, 0)),
            pl.BlockSpec((1, 1, piece_len), lambda r: (r, 0, 0)),
            pl.BlockSpec((1, row_count, 1), lambda r: (r, 0, 0)),
        ],
        out_specs=pl.BlockSpec((seq_count, 1, own_heads, step_rows, 128), lambda r: (0, r, 0, 0, 0)),
        out_shape=jax.ShapeDtypeStruct((seq_count, req_count, own_heads, step_rows, 128), jnp.float32),
    )(query_rows, keys, values, trailing, prefix_rows, live_row, total_rows)


def body(
    hidden_in,
    norm_gain,
    w_qkv,
    w_forget,
    forget_bias,
    cache_keys,
    cache_values,
    cache_forget,
    cache_lengths,
    piece_map,
    draft_counts,
):
    req_count, new_count, width = hidden_in.shape
    head_count = w_forget.shape[1]
    seq_count = lax.axis_size("seq")
    fsdp_count = lax.axis_size("fsdp")
    own_heads = w_qkv.shape[2]
    own_dims = w_qkv.shape[3]
    own_cols = 3 * own_heads * own_dims
    rows = req_count * new_count
    inner_width = head_count * HEAD_DIM
    piece_len = cache_forget.shape[2]
    logit_scale = HEAD_DIM ** (-0.5)
    seq_index = lax.axis_index("seq")
    head_start = seq_index * own_heads
    hidden_all = lax.all_to_all(
        jnp.broadcast_to(hidden_in[None], (fsdp_count, req_count, new_count, width)),
        "fsdp",
        0,
        0,
        tiled=True,
    )
    normed_all = normalize(hidden_all, norm_gain).reshape(fsdp_count * rows, width)
    projected = jnp.einsum(
        "dk,nd->kn",
        w_qkv.reshape(width, own_cols),
        normed_all,
        preferred_element_type=jnp.float32,
    ).astype(jnp.bfloat16)
    outgoing = (
        projected.reshape(3, own_heads * own_dims, fsdp_count, rows)
        .transpose(2, 1, 0, 3)
        .reshape(fsdp_count, 1, own_heads * own_dims * 3 * rows)
    )
    outgoing = jnp.broadcast_to(
        outgoing, (fsdp_count, seq_count, own_heads * own_dims * 3 * rows)
    ).reshape(fsdp_count * seq_count, own_heads * own_dims * 3 * rows)
    incoming = lax.all_to_all(outgoing, ("fsdp", "seq"), 0, 0, tiled=True)
    incoming = incoming.reshape(fsdp_count * seq_count * own_heads * own_dims, 3 * rows)
    src_row = jnp.arange(fsdp_count * seq_count * own_heads * own_dims, dtype=jnp.int32)
    src_dev = src_row // (own_heads * own_dims)
    src_head = (src_row // own_dims) % own_heads
    src_dim = src_row % own_dims
    target = ((src_dev % seq_count) * own_heads + src_head) * HEAD_DIM + (
        src_dev // seq_count
    ) * own_dims + src_dim
    placement = (target[:, None] == jnp.arange(inner_width, dtype=jnp.int32)[None, :]).astype(
        jnp.bfloat16
    )
    all_heads = jnp.einsum(
        "kx,kj->xj", incoming, placement, preferred_element_type=jnp.float32
    ).astype(jnp.bfloat16).reshape(3, req_count, new_count, inner_width)
    normed = normalize(hidden_in, norm_gain).reshape(rows, width)
    gate_logit = (
        jnp.dot(normed, w_forget, preferred_element_type=jnp.float32).reshape(
            req_count, new_count, head_count
        )
        + forget_bias
    )
    prefix = jnp.cumsum(jax.nn.log_sigmoid(gate_logit), axis=1)
    slot_ids = jnp.arange(seq_count, dtype=jnp.int32)
    holders = piece_map[:, :, None] == slot_ids[None, None, :]
    piece_of_slot = jnp.sum(jnp.where(holders, slot_ids[None, :, None], 0), axis=1)
    own_piece = jnp.sum(jnp.where(piece_map == seq_index, slot_ids[None, :], 0), axis=1)
    steps = jnp.arange(piece_len, dtype=jnp.int32)
    positions = own_piece[:, None] * piece_len + steps[None, :]
    live_mask = positions < cache_lengths[:, None]
    masked = jnp.where(live_mask[:, None, :], cache_forget, 0.0)
    piece_total = jnp.sum(masked, axis=-1)
    later_step = (steps[:, None] > steps[None, :]).astype(jnp.float32)
    trailing_part = jnp.einsum(
        "rhl,lj->rhj", masked, later_step, precision=lax.Precision.HIGHEST,
        preferred_element_type=jnp.float32,
    )
    step_rows = 8
    pad_steps = ((0, 0), (0, step_rows - new_count))
    query_rows = jnp.pad(all_heads[0], pad_steps + ((0, 0),))
    prefix_rows = jnp.pad(jnp.transpose(prefix, (0, 2, 1)), ((0, 0),) + pad_steps).reshape(
        req_count, head_count * step_rows, 1
    )
    live_row = live_mask.astype(jnp.float32)[:, None, :]
    total_rows = jnp.broadcast_to(
        piece_total[:, :, None], (req_count, head_count, step_rows)
    ).reshape(req_count, head_count * step_rows, 1)
    packed = piece_attention(
        query_rows, cache_keys, cache_values, trailing_part, prefix_rows, live_row, total_rows, seq_count
    )
    parts = lax.all_to_all(packed, "seq", 0, 0, tiled=True)[:, :, :, :new_count]
    part_acc = parts[..., :HEAD_DIM]
    part_max = parts[..., HEAD_DIM]
    part_sum = parts[..., HEAD_DIM + 1]
    part_total = parts[:, :, :, 0, HEAD_DIM + 2]
    later_piece = (piece_of_slot.T[None, :, :] > piece_of_slot.T[:, None, :])[..., None]
    later_sum = jnp.sum(jnp.where(later_piece, part_total[None], 0.0), axis=1)
    part_max = part_max + later_sum[..., None]
    cache_max = jnp.max(part_max, axis=0)
    factor = jnp.exp(part_max - cache_max[None])
    cache_sum = jnp.sum(part_sum * factor, axis=0)
    cache_acc = jnp.sum(part_acc * factor[..., None], axis=0)
    own_rows = lax.dynamic_slice_in_dim(
        all_heads, head_start * HEAD_DIM, own_heads * HEAD_DIM, 3
    ).reshape(3, req_count, new_count, own_heads, HEAD_DIM)
    own_prefix = jnp.transpose(
        lax.dynamic_slice_in_dim(prefix, head_start, own_heads, 2), (0, 2, 1)
    )
    fresh_logits = (
        jnp.einsum(
            "rmhd,rnhd->rhmn",
            own_rows[0],
            own_rows[1],
            preferred_element_type=jnp.float32,
        )
        * logit_scale
    )
    fresh_logits = fresh_logits + own_prefix[..., :, None] - own_prefix[..., None, :]
    step_ids = jnp.arange(new_count, dtype=jnp.int32)
    causal = (step_ids[None, :] <= step_ids[:, None])[None, None]
    joint_max = jnp.maximum(cache_max, jnp.max(jnp.where(causal, fresh_logits, neg_fill), axis=-1))
    new_weights = jnp.where(causal, jnp.exp(fresh_logits - joint_max[..., None]), 0.0)
    carried = jnp.exp(cache_max - joint_max)
    total_sum = cache_sum * carried + jnp.sum(new_weights, axis=-1)
    blend_weights = cache_acc * carried[..., None] + jnp.einsum(
        "rhmn,rnhd->rhmd",
        new_weights.astype(jnp.bfloat16),
        own_rows[2],
        preferred_element_type=jnp.float32,
    )
    result = blend_weights / total_sum[..., None]
    live_rows = (step_ids[None, :] <= draft_counts[:, None])[:, None, :, None]
    result = jnp.where(live_rows, result, 0.0)
    return (
        jnp.transpose(result, (0, 2, 1, 3))
        .reshape(req_count, new_count, own_heads * HEAD_DIM)
        .astype(jnp.bfloat16)
    )


def solution(mesh):
    in_specs = (
        P("fsdp", None, None),
        P(),
        P(None, None, "seq", "fsdp"),
        P(),
        P(),
        P("fsdp", "seq", None),
        P("fsdp", "seq", None),
        P("fsdp", None, "seq"),
        P("fsdp"),
        P("fsdp", None),
        P("fsdp"),
    )
    out_specs = P("fsdp", None, "seq")
    return jax.shard_map(body, mesh=mesh, in_specs=in_specs, out_specs=out_specs, check_vma=False)
```

```python
import jax
import jax.numpy as jnp
from jax import lax
from jax.experimental import pallas as pl
from jax.experimental.pallas import tpu as pltpu
from jax.sharding import PartitionSpec as P

HEAD_DIM = 64


norm_eps = 1e-06
neg_fill = -1e30


def normalize(rows, gain):
    values = rows.astype(jnp.float32)
    mean_sq = jnp.mean(values * values, axis=-1, keepdims=True)
    return (values * lax.rsqrt(mean_sq + norm_eps) * gain).astype(jnp.bfloat16)


def attention_kernel(q_ref, k_ref, v_ref, trail_ref, prefix_ref, live_ref, total_ref, out_ref):
    step_rows = q_ref.shape[1]
    head_count = trail_ref.shape[1]
    piece_len = trail_ref.shape[2]
    inner_width = q_ref.shape[2]
    row_count = head_count * step_rows
    pair_count = inner_width // 128
    row_step = lax.broadcasted_iota(jnp.int32, (row_count, step_rows), 0) % step_rows
    spread = (row_step == lax.broadcasted_iota(jnp.int32, (row_count, step_rows), 1)).astype(jnp.bfloat16)
    repeated = jnp.dot(spread, q_ref[0], preferred_element_type=jnp.float32)
    row_head = lax.broadcasted_iota(jnp.int32, (row_count, inner_width), 0) // step_rows
    col_head = lax.broadcasted_iota(jnp.int32, (row_count, inner_width), 1) // HEAD_DIM
    query_blocks = jnp.where(row_head == col_head, repeated, 0.0).astype(jnp.bfloat16)
    scores = lax.dot_general(
        query_blocks, k_ref[0], (((1,), (1,)), ((), ())), preferred_element_type=jnp.float32
    )
    trailing = jnp.broadcast_to(
        trail_ref[0][:, None, :], (head_count, step_rows, piece_len)
    ).reshape(row_count, piece_len)
    scores = scores * (HEAD_DIM ** (-0.5)) + (trailing + prefix_ref[0])
    live = live_ref[0] > 0.5
    row_max = jnp.max(jnp.where(live, scores, neg_fill), axis=1, keepdims=True)
    weights = jnp.where(live, jnp.exp(scores - row_max), 0.0)
    weight_sum = jnp.sum(weights, axis=1, keepdims=True)
    blocks = jnp.dot(weights.astype(jnp.bfloat16), v_ref[0], preferred_element_type=jnp.float32)
    row = lax.broadcasted_iota(jnp.int32, (row_count, 128), 0)
    picked = jnp.zeros((row_count, 128), jnp.float32)
    for pair in range(pair_count):
        lo = 2 * pair * step_rows
        picked = jnp.where(
            (row >= lo) & (row < lo + 2 * step_rows), blocks[:, pair * 128 : (pair + 1) * 128], picked
        )
    odd = (row // step_rows) % 2 == 1
    accum = jnp.where(odd, pltpu.roll(picked, 64, 1), picked)
    lane = lax.broadcasted_iota(jnp.int32, (row_count, 128), 1)
    packed = jnp.where(lane < HEAD_DIM, accum, 0.0)
    packed = jnp.where(lane == HEAD_DIM, row_max, packed)
    packed = jnp.where(lane == HEAD_DIM + 1, weight_sum, packed)
    packed = jnp.where(lane == HEAD_DIM + 2, total_ref[0], packed)
    own_heads = out_ref.shape[2]
    for head in range(head_count):
        out_ref[head // own_heads, 0, head % own_heads] = packed[head * step_rows : (head + 1) * step_rows]


def piece_attention(query_rows, keys, values, trailing, prefix_rows, live_row, total_rows, seq_count):
    req_count, step_rows, inner_width = query_rows.shape
    head_count = trailing.shape[1]
    piece_len = keys.shape[1]
    row_count = head_count * step_rows
    own_heads = head_count // seq_count
    return pl.pallas_call(
        attention_kernel,
        grid=(req_count,),
        in_specs=[
            pl.BlockSpec((1, step_rows, inner_width), lambda r: (r, 0, 0)),
            pl.BlockSpec((1, piece_len, inner_width), lambda r: (r, 0, 0)),
            pl.BlockSpec((1, piece_len, inner_width), lambda r: (r, 0, 0)),
            pl.BlockSpec((1, head_count, piece_len), lambda r: (r, 0, 0)),
            pl.BlockSpec((1, row_count, 1), lambda r: (r, 0, 0)),
            pl.BlockSpec((1, 1, piece_len), lambda r: (r, 0, 0)),
            pl.BlockSpec((1, row_count, 1), lambda r: (r, 0, 0)),
        ],
        out_specs=pl.BlockSpec((seq_count, 1, own_heads, step_rows, 128), lambda r: (0, r, 0, 0, 0)),
        out_shape=jax.ShapeDtypeStruct((seq_count, req_count, own_heads, step_rows, 128), jnp.float32),
    )(query_rows, keys, values, trailing, prefix_rows, live_row, total_rows)


def body(
    hidden_in,
    norm_gain,
    w_qkv,
    w_forget,
    forget_bias,
    cache_keys,
    cache_values,
    cache_forget,
    cache_lengths,
    piece_map,
    draft_counts,
):
    req_count, new_count, width = hidden_in.shape
    head_count = w_forget.shape[1]
    seq_count = lax.axis_size("seq")
    fsdp_count = lax.axis_size("fsdp")
    own_heads = w_qkv.shape[2]
    own_dims = w_qkv.shape[3]
    own_cols = 3 * own_heads * own_dims
    rows = req_count * new_count
    inner_width = head_count * HEAD_DIM
    piece_len = cache_forget.shape[2]
    logit_scale = HEAD_DIM ** (-0.5)
    seq_index = lax.axis_index("seq")
    head_start = seq_index * own_heads
    normed = normalize(hidden_in, norm_gain).reshape(rows, width)
    normed_all = lax.all_to_all(
        jnp.broadcast_to(normed[None], (fsdp_count, rows, width)), "fsdp", 0, 0, tiled=True
    ).reshape(fsdp_count * rows, width)
    projected = jnp.einsum(
        "dk,nd->kn",
        w_qkv.reshape(width, own_cols),
        normed_all,
        preferred_element_type=jnp.float32,
    ).astype(jnp.bfloat16)
    outgoing = (
        projected.reshape(3, own_heads * own_dims, fsdp_count, rows)
        .transpose(2, 1, 0, 3)
        .reshape(fsdp_count, 1, own_heads * own_dims * 3 * rows)
    )
    outgoing = jnp.broadcast_to(
        outgoing, (fsdp_count, seq_count, own_heads * own_dims * 3 * rows)
    ).reshape(fsdp_count * seq_count, 2, own_heads * own_dims * 3 * rows // 2)
    incoming = lax.all_to_all(outgoing, ("fsdp", "seq"), 0, 0, tiled=True)
    incoming = incoming.reshape(fsdp_count * seq_count * own_heads * own_dims, 3 * rows)
    src_row = jnp.arange(fsdp_count * seq_count * own_heads * own_dims, dtype=jnp.int32)
    src_dev = src_row // (own_heads * own_dims)
    src_head = (src_row // own_dims) % own_heads
    src_dim = src_row % own_dims
    target = ((src_dev % seq_count) * own_heads + src_head) * HEAD_DIM + (
        src_dev // seq_count
    ) * own_dims + src_dim
    placement = (target[:, None] == jnp.arange(inner_width, dtype=jnp.int32)[None, :]).astype(
        jnp.bfloat16
    )
    all_heads = jnp.einsum(
        "kx,kj->xj", incoming, placement, preferred_element_type=jnp.float32
    ).astype(jnp.bfloat16).reshape(3, req_count, new_count, inner_width)
    gate_logit = (
        jnp.dot(normed, w_forget, preferred_element_type=jnp.float32).reshape(
            req_count, new_count, head_count
        )
        + forget_bias
    )
    prefix = jnp.cumsum(jax.nn.log_sigmoid(gate_logit), axis=1)
    slot_ids = jnp.arange(seq_count, dtype=jnp.int32)
    holders = piece_map[:, :, None] == slot_ids[None, None, :]
    piece_of_slot = jnp.sum(jnp.where(holders, slot_ids[None, :, None], 0), axis=1)
    own_piece = jnp.sum(jnp.where(piece_map == seq_index, slot_ids[None, :], 0), axis=1)
    steps = jnp.arange(piece_len, dtype=jnp.int32)
    positions = own_piece[:, None] * piece_len + steps[None, :]
    live_mask = positions < cache_lengths[:, None]
    masked = jnp.where(live_mask[:, None, :], cache_forget, 0.0)
    piece_total = jnp.sum(masked, axis=-1)
    later_step = (steps[:, None] > steps[None, :]).astype(jnp.float32)
    trailing_part = jnp.einsum(
        "rhl,lj->rhj", masked, later_step, precision=lax.Precision.HIGHEST,
        preferred_element_type=jnp.float32,
    )
    step_rows = 8
    pad_steps = ((0, 0), (0, step_rows - new_count))
    query_rows = jnp.pad(all_heads[0], pad_steps + ((0, 0),))
    prefix_rows = jnp.pad(jnp.transpose(prefix, (0, 2, 1)), ((0, 0),) + pad_steps).reshape(
        req_count, head_count * step_rows, 1
    )
    live_row = live_mask.astype(jnp.float32)[:, None, :]
    total_rows = jnp.broadcast_to(
        piece_total[:, :, None], (req_count, head_count, step_rows)
    ).reshape(req_count, head_count * step_rows, 1)
    packed = piece_attention(
        query_rows, cache_keys, cache_values, trailing_part, prefix_rows, live_row, total_rows, seq_count
    )
    parts = lax.all_to_all(packed, "seq", 0, 0, tiled=True)[:, :, :, :new_count]
    part_acc = parts[..., :HEAD_DIM]
    part_max = parts[..., HEAD_DIM]
    part_sum = parts[..., HEAD_DIM + 1]
    part_total = parts[:, :, :, 0, HEAD_DIM + 2]
    later_piece = (piece_of_slot.T[None, :, :] > piece_of_slot.T[:, None, :])[..., None]
    later_sum = jnp.sum(jnp.where(later_piece, part_total[None], 0.0), axis=1)
    part_max = part_max + later_sum[..., None]
    cache_max = jnp.max(part_max, axis=0)
    factor = jnp.exp(part_max - cache_max[None])
    cache_sum = jnp.sum(part_sum * factor, axis=0)
    cache_acc = jnp.sum(part_acc * factor[..., None], axis=0)
    own_rows = lax.dynamic_slice_in_dim(
        all_heads, head_start * HEAD_DIM, own_heads * HEAD_DIM, 3
    ).reshape(3, req_count, new_count, own_heads, HEAD_DIM)
    own_prefix = jnp.transpose(
        lax.dynamic_slice_in_dim(prefix, head_start, own_heads, 2), (0, 2, 1)
    )
    fresh_logits = (
        jnp.einsum(
            "rmhd,rnhd->rhmn",
            own_rows[0],
            own_rows[1],
            preferred_element_type=jnp.float32,
        )
        * logit_scale
    )
    fresh_logits = fresh_logits + own_prefix[..., :, None] - own_prefix[..., None, :]
    step_ids = jnp.arange(new_count, dtype=jnp.int32)
    causal = (step_ids[None, :] <= step_ids[:, None])[None, None]
    joint_max = jnp.maximum(cache_max, jnp.max(jnp.where(causal, fresh_logits, neg_fill), axis=-1))
    new_weights = jnp.where(causal, jnp.exp(fresh_logits - joint_max[..., None]), 0.0)
    carried = jnp.exp(cache_max - joint_max)
    total_sum = cache_sum * carried + jnp.sum(new_weights, axis=-1)
    blend_weights = cache_acc * carried[..., None] + jnp.einsum(
        "rhmn,rnhd->rhmd",
        new_weights.astype(jnp.bfloat16),
        own_rows[2],
        preferred_element_type=jnp.float32,
    )
    result = blend_weights / total_sum[..., None]
    live_rows = (step_ids[None, :] <= draft_counts[:, None])[:, None, :, None]
    result = jnp.where(live_rows, result, 0.0)
    return (
        jnp.transpose(result, (0, 2, 1, 3))
        .reshape(req_count, new_count, own_heads * HEAD_DIM)
        .astype(jnp.bfloat16)
    )


def solution(mesh):
    in_specs = (
        P("fsdp", None, None),
        P(),
        P(None, None, "seq", "fsdp"),
        P(),
        P(),
        P("fsdp", "seq", None),
        P("fsdp", "seq", None),
        P("fsdp", None, "seq"),
        P("fsdp"),
        P("fsdp", None),
        P("fsdp"),
    )
    out_specs = P("fsdp", None, "seq")
    return jax.shard_map(body, mesh=mesh, in_specs=in_specs, out_specs=out_specs, check_vma=False)
```

```python
import jax
import jax.numpy as jnp
from jax import lax
from jax.experimental import pallas as pl
from jax.experimental.pallas import tpu as pltpu
from jax.sharding import PartitionSpec as P

HEAD_DIM = 64


norm_eps = 1e-06
neg_fill = -1e30


def normalize(rows, gain):
    values = rows.astype(jnp.float32)
    mean_sq = jnp.mean(values * values, axis=-1, keepdims=True)
    return (values * lax.rsqrt(mean_sq + norm_eps) * gain).astype(jnp.bfloat16)


def normalize_kernel(rows_ref, gain_ref, out_ref):
    values = rows_ref[...].astype(jnp.float32)
    mean_sq = jnp.mean(values * values, axis=-1, keepdims=True)
    normed = (values * lax.rsqrt(mean_sq + norm_eps) * gain_ref[...]).astype(jnp.bfloat16)
    for copy in range(out_ref.shape[0]):
        out_ref[copy] = normed


def normalize_copies(rows, gain, copies):
    row_count, width = rows.shape
    return pl.pallas_call(
        normalize_kernel,
        out_shape=jax.ShapeDtypeStruct((copies, row_count, width), jnp.bfloat16),
    )(rows, gain.reshape(1, width))


def attention_kernel(q_ref, k_ref, v_ref, trail_ref, prefix_ref, live_ref, total_ref, out_ref):
    step_rows = q_ref.shape[1]
    head_count = trail_ref.shape[1]
    piece_len = trail_ref.shape[2]
    inner_width = q_ref.shape[2]
    row_count = head_count * step_rows
    pair_count = inner_width // 128
    row_step = lax.broadcasted_iota(jnp.int32, (row_count, step_rows), 0) % step_rows
    spread = (row_step == lax.broadcasted_iota(jnp.int32, (row_count, step_rows), 1)).astype(jnp.bfloat16)
    repeated = jnp.dot(spread, q_ref[0], preferred_element_type=jnp.float32)
    row_head = lax.broadcasted_iota(jnp.int32, (row_count, inner_width), 0) // step_rows
    col_head = lax.broadcasted_iota(jnp.int32, (row_count, inner_width), 1) // HEAD_DIM
    query_blocks = jnp.where(row_head == col_head, repeated, 0.0).astype(jnp.bfloat16)
    scores = lax.dot_general(
        query_blocks, k_ref[0], (((1,), (1,)), ((), ())), preferred_element_type=jnp.float32
    )
    trailing = jnp.broadcast_to(
        trail_ref[0][:, None, :], (head_count, step_rows, piece_len)
    ).reshape(row_count, piece_len)
    scores = scores * (HEAD_DIM ** (-0.5)) + (trailing + prefix_ref[0])
    live = live_ref[0] > 0.5
    row_max = jnp.max(jnp.where(live, scores, neg_fill), axis=1, keepdims=True)
    weights = jnp.where(live, jnp.exp(scores - row_max), 0.0)
    weight_sum = jnp.sum(weights, axis=1, keepdims=True)
    blocks = jnp.dot(weights.astype(jnp.bfloat16), v_ref[0], preferred_element_type=jnp.float32)
    row = lax.broadcasted_iota(jnp.int32, (row_count, 128), 0)
    picked = jnp.zeros((row_count, 128), jnp.float32)
    for pair in range(pair_count):
        lo = 2 * pair * step_rows
        picked = jnp.where(
            (row >= lo) & (row < lo + 2 * step_rows), blocks[:, pair * 128 : (pair + 1) * 128], picked
        )
    odd = (row // step_rows) % 2 == 1
    accum = jnp.where(odd, pltpu.roll(picked, 64, 1), picked)
    lane = lax.broadcasted_iota(jnp.int32, (row_count, 128), 1)
    packed = jnp.where(lane < HEAD_DIM, accum, 0.0)
    packed = jnp.where(lane == HEAD_DIM, row_max, packed)
    packed = jnp.where(lane == HEAD_DIM + 1, weight_sum, packed)
    packed = jnp.where(lane == HEAD_DIM + 2, total_ref[0], packed)
    own_heads = out_ref.shape[2]
    for head in range(head_count):
        out_ref[head // own_heads, 0, head % own_heads] = packed[head * step_rows : (head + 1) * step_rows]


def piece_attention(query_rows, keys, values, trailing, prefix_rows, live_row, total_rows, seq_count):
    req_count, step_rows, inner_width = query_rows.shape
    head_count = trailing.shape[1]
    piece_len = keys.shape[1]
    row_count = head_count * step_rows
    own_heads = head_count // seq_count
    return pl.pallas_call(
        attention_kernel,
        grid=(req_count,),
        in_specs=[
            pl.BlockSpec((1, step_rows, inner_width), lambda r: (r, 0, 0)),
            pl.BlockSpec((1, piece_len, inner_width), lambda r: (r, 0, 0)),
            pl.BlockSpec((1, piece_len, inner_width), lambda r: (r, 0, 0)),
            pl.BlockSpec((1, head_count, piece_len), lambda r: (r, 0, 0)),
            pl.BlockSpec((1, row_count, 1), lambda r: (r, 0, 0)),
            pl.BlockSpec((1, 1, piece_len), lambda r: (r, 0, 0)),
            pl.BlockSpec((1, row_count, 1), lambda r: (r, 0, 0)),
        ],
        out_specs=pl.BlockSpec((seq_count, 1, own_heads, step_rows, 128), lambda r: (0, r, 0, 0, 0)),
        out_shape=jax.ShapeDtypeStruct((seq_count, req_count, own_heads, step_rows, 128), jnp.float32),
    )(query_rows, keys, values, trailing, prefix_rows, live_row, total_rows)


def body(
    hidden_in,
    norm_gain,
    w_qkv,
    w_forget,
    forget_bias,
    cache_keys,
    cache_values,
    cache_forget,
    cache_lengths,
    piece_map,
    draft_counts,
):
    req_count, new_count, width = hidden_in.shape
    head_count = w_forget.shape[1]
    seq_count = lax.axis_size("seq")
    fsdp_count = lax.axis_size("fsdp")
    own_heads = w_qkv.shape[2]
    own_dims = w_qkv.shape[3]
    own_cols = 3 * own_heads * own_dims
    rows = req_count * new_count
    inner_width = head_count * HEAD_DIM
    piece_len = cache_forget.shape[2]
    logit_scale = HEAD_DIM ** (-0.5)
    seq_index = lax.axis_index("seq")
    head_start = seq_index * own_heads
    normed_copies = normalize_copies(hidden_in.reshape(rows, width), norm_gain, fsdp_count)
    normed = normed_copies[0]
    normed_all = lax.all_to_all(normed_copies, "fsdp", 0, 0, tiled=True).reshape(
        fsdp_count * rows, width
    )
    projected = jnp.einsum(
        "dk,nd->kn",
        w_qkv.reshape(width, own_cols),
        normed_all,
        preferred_element_type=jnp.float32,
    ).astype(jnp.bfloat16)
    outgoing = (
        projected.reshape(3, own_heads * own_dims, fsdp_count, rows)
        .transpose(2, 1, 0, 3)
        .reshape(fsdp_count, 1, own_heads * own_dims * 3 * rows)
    )
    outgoing = jnp.broadcast_to(
        outgoing, (fsdp_count, seq_count, own_heads * own_dims * 3 * rows)
    ).reshape(fsdp_count * seq_count, 2, own_heads * own_dims * 3 * rows // 2)
    incoming = lax.all_to_all(outgoing, ("fsdp", "seq"), 0, 0, tiled=True)
    incoming = incoming.reshape(fsdp_count * seq_count * own_heads * own_dims, 3 * rows)
    src_row = jnp.arange(fsdp_count * seq_count * own_heads * own_dims, dtype=jnp.int32)
    src_dev = src_row // (own_heads * own_dims)
    src_head = (src_row // own_dims) % own_heads
    src_dim = src_row % own_dims
    target = ((src_dev % seq_count) * own_heads + src_head) * HEAD_DIM + (
        src_dev // seq_count
    ) * own_dims + src_dim
    placement = (target[:, None] == jnp.arange(inner_width, dtype=jnp.int32)[None, :]).astype(
        jnp.bfloat16
    )
    all_heads = jnp.einsum(
        "kx,kj->xj", incoming, placement, preferred_element_type=jnp.float32
    ).astype(jnp.bfloat16).reshape(3, req_count, new_count, inner_width)
    gate_logit = (
        jnp.dot(normed, w_forget, preferred_element_type=jnp.float32).reshape(
            req_count, new_count, head_count
        )
        + forget_bias
    )
    prefix = jnp.cumsum(jax.nn.log_sigmoid(gate_logit), axis=1)
    slot_ids = jnp.arange(seq_count, dtype=jnp.int32)
    holders = piece_map[:, :, None] == slot_ids[None, None, :]
    piece_of_slot = jnp.sum(jnp.where(holders, slot_ids[None, :, None], 0), axis=1)
    own_piece = jnp.sum(jnp.where(piece_map == seq_index, slot_ids[None, :], 0), axis=1)
    steps = jnp.arange(piece_len, dtype=jnp.int32)
    positions = own_piece[:, None] * piece_len + steps[None, :]
    live_mask = positions < cache_lengths[:, None]
    masked = jnp.where(live_mask[:, None, :], cache_forget, 0.0)
    piece_total = jnp.sum(masked, axis=-1)
    later_step = (steps[:, None] > steps[None, :]).astype(jnp.float32)
    trailing_part = jnp.einsum(
        "rhl,lj->rhj", masked, later_step, precision=lax.Precision.HIGHEST,
        preferred_element_type=jnp.float32,
    )
    step_rows = 8
    pad_steps = ((0, 0), (0, step_rows - new_count))
    query_rows = jnp.pad(all_heads[0], pad_steps + ((0, 0),))
    prefix_rows = jnp.pad(jnp.transpose(prefix, (0, 2, 1)), ((0, 0),) + pad_steps).reshape(
        req_count, head_count * step_rows, 1
    )
    live_row = live_mask.astype(jnp.float32)[:, None, :]
    total_rows = jnp.broadcast_to(
        piece_total[:, :, None], (req_count, head_count, step_rows)
    ).reshape(req_count, head_count * step_rows, 1)
    packed = piece_attention(
        query_rows, cache_keys, cache_values, trailing_part, prefix_rows, live_row, total_rows, seq_count
    )
    parts = lax.all_to_all(packed, "seq", 0, 0, tiled=True)[:, :, :, :new_count]
    part_acc = parts[..., :HEAD_DIM]
    part_max = parts[..., HEAD_DIM]
    part_sum = parts[..., HEAD_DIM + 1]
    part_total = parts[:, :, :, 0, HEAD_DIM + 2]
    later_piece = (piece_of_slot.T[None, :, :] > piece_of_slot.T[:, None, :])[..., None]
    later_sum = jnp.sum(jnp.where(later_piece, part_total[None], 0.0), axis=1)
    part_max = part_max + later_sum[..., None]
    cache_max = jnp.max(part_max, axis=0)
    factor = jnp.exp(part_max - cache_max[None])
    cache_sum = jnp.sum(part_sum * factor, axis=0)
    cache_acc = jnp.sum(part_acc * factor[..., None], axis=0)
    own_rows = lax.dynamic_slice_in_dim(
        all_heads, head_start * HEAD_DIM, own_heads * HEAD_DIM, 3
    ).reshape(3, req_count, new_count, own_heads, HEAD_DIM)
    own_prefix = jnp.transpose(
        lax.dynamic_slice_in_dim(prefix, head_start, own_heads, 2), (0, 2, 1)
    )
    fresh_logits = (
        jnp.einsum(
            "rmhd,rnhd->rhmn",
            own_rows[0],
            own_rows[1],
            preferred_element_type=jnp.float32,
        )
        * logit_scale
    )
    fresh_logits = fresh_logits + own_prefix[..., :, None] - own_prefix[..., None, :]
    step_ids = jnp.arange(new_count, dtype=jnp.int32)
    causal = (step_ids[None, :] <= step_ids[:, None])[None, None]
    joint_max = jnp.maximum(cache_max, jnp.max(jnp.where(causal, fresh_logits, neg_fill), axis=-1))
    new_weights = jnp.where(causal, jnp.exp(fresh_logits - joint_max[..., None]), 0.0)
    carried = jnp.exp(cache_max - joint_max)
    total_sum = cache_sum * carried + jnp.sum(new_weights, axis=-1)
    blend_weights = cache_acc * carried[..., None] + jnp.einsum(
        "rhmn,rnhd->rhmd",
        new_weights.astype(jnp.bfloat16),
        own_rows[2],
        preferred_element_type=jnp.float32,
    )
    result = blend_weights / total_sum[..., None]
    live_rows = (step_ids[None, :] <= draft_counts[:, None])[:, None, :, None]
    result = jnp.where(live_rows, result, 0.0)
    return (
        jnp.transpose(result, (0, 2, 1, 3))
        .reshape(req_count, new_count, own_heads * HEAD_DIM)
        .astype(jnp.bfloat16)
    )


def solution(mesh):
    in_specs = (
        P("fsdp", None, None),
        P(),
        P(None, None, "seq", "fsdp"),
        P(),
        P(),
        P("fsdp", "seq", None),
        P("fsdp", "seq", None),
        P("fsdp", None, "seq"),
        P("fsdp"),
        P("fsdp", None),
        P("fsdp"),
    )
    out_specs = P("fsdp", None, "seq")
    return jax.shard_map(body, mesh=mesh, in_specs=in_specs, out_specs=out_specs, check_vma=False)
```

```python
import jax
import jax.numpy as jnp
from jax import lax
from jax.experimental import pallas as pl
from jax.experimental.pallas import tpu as pltpu
from jax.sharding import PartitionSpec as P

HEAD_DIM = 64


norm_eps = 1e-06
neg_fill = -1e30


def normalize(rows, gain):
    values = rows.astype(jnp.float32)
    mean_sq = jnp.mean(values * values, axis=-1, keepdims=True)
    return (values * lax.rsqrt(mean_sq + norm_eps) * gain).astype(jnp.bfloat16)


def attention_kernel(q_ref, k_ref, v_ref, trail_ref, prefix_ref, live_ref, total_ref, out_ref):
    step_rows = q_ref.shape[1]
    head_count = trail_ref.shape[1]
    piece_len = trail_ref.shape[2]
    inner_width = q_ref.shape[2]
    row_count = head_count * step_rows
    pair_count = inner_width // 128
    row_step = lax.broadcasted_iota(jnp.int32, (row_count, step_rows), 0) % step_rows
    spread = (row_step == lax.broadcasted_iota(jnp.int32, (row_count, step_rows), 1)).astype(jnp.bfloat16)
    repeated = jnp.dot(spread, q_ref[0], preferred_element_type=jnp.float32)
    row_head = lax.broadcasted_iota(jnp.int32, (row_count, inner_width), 0) // step_rows
    col_head = lax.broadcasted_iota(jnp.int32, (row_count, inner_width), 1) // HEAD_DIM
    query_blocks = jnp.where(row_head == col_head, repeated, 0.0).astype(jnp.bfloat16)
    scores = lax.dot_general(
        query_blocks, k_ref[0], (((1,), (1,)), ((), ())), preferred_element_type=jnp.float32
    )
    trailing = jnp.broadcast_to(
        trail_ref[0][:, None, :], (head_count, step_rows, piece_len)
    ).reshape(row_count, piece_len)
    scores = scores * (HEAD_DIM ** (-0.5)) + (trailing + prefix_ref[0])
    live = live_ref[0] > 0.5
    row_max = jnp.max(jnp.where(live, scores, neg_fill), axis=1, keepdims=True)
    weights = jnp.where(live, jnp.exp(scores - row_max), 0.0)
    weight_sum = jnp.sum(weights, axis=1, keepdims=True)
    blocks = jnp.dot(weights.astype(jnp.bfloat16), v_ref[0], preferred_element_type=jnp.float32)
    row = lax.broadcasted_iota(jnp.int32, (row_count, 128), 0)
    picked = jnp.zeros((row_count, 128), jnp.float32)
    for pair in range(pair_count):
        lo = 2 * pair * step_rows
        picked = jnp.where(
            (row >= lo) & (row < lo + 2 * step_rows), blocks[:, pair * 128 : (pair + 1) * 128], picked
        )
    odd = (row // step_rows) % 2 == 1
    accum = jnp.where(odd, pltpu.roll(picked, 64, 1), picked)
    lane = lax.broadcasted_iota(jnp.int32, (row_count, 128), 1)
    packed = jnp.where(lane < HEAD_DIM, accum, 0.0)
    packed = jnp.where(lane == HEAD_DIM, row_max, packed)
    packed = jnp.where(lane == HEAD_DIM + 1, weight_sum, packed)
    packed = jnp.where(lane == HEAD_DIM + 2, total_ref[0], packed)
    own_heads = out_ref.shape[2]
    for head in range(head_count):
        out_ref[head // own_heads, 0, head % own_heads] = packed[head * step_rows : (head + 1) * step_rows]


def piece_attention(query_rows, keys, values, trailing, prefix_rows, live_row, total_rows, seq_count):
    req_count, step_rows, inner_width = query_rows.shape
    head_count = trailing.shape[1]
    piece_len = keys.shape[1]
    row_count = head_count * step_rows
    own_heads = head_count // seq_count
    return pl.pallas_call(
        attention_kernel,
        grid=(req_count,),
        in_specs=[
            pl.BlockSpec((1, step_rows, inner_width), lambda r: (r, 0, 0)),
            pl.BlockSpec((1, piece_len, inner_width), lambda r: (r, 0, 0)),
            pl.BlockSpec((1, piece_len, inner_width), lambda r: (r, 0, 0)),
            pl.BlockSpec((1, head_count, piece_len), lambda r: (r, 0, 0)),
            pl.BlockSpec((1, row_count, 1), lambda r: (r, 0, 0)),
            pl.BlockSpec((1, 1, piece_len), lambda r: (r, 0, 0)),
            pl.BlockSpec((1, row_count, 1), lambda r: (r, 0, 0)),
        ],
        out_specs=pl.BlockSpec((seq_count, 1, own_heads, step_rows, 128), lambda r: (0, r, 0, 0, 0)),
        out_shape=jax.ShapeDtypeStruct((seq_count, req_count, own_heads, step_rows, 128), jnp.float32),
    )(query_rows, keys, values, trailing, prefix_rows, live_row, total_rows)


def body(
    hidden_in,
    norm_gain,
    w_qkv,
    w_forget,
    forget_bias,
    cache_keys,
    cache_values,
    cache_forget,
    cache_lengths,
    piece_map,
    draft_counts,
):
    req_count, new_count, width = hidden_in.shape
    head_count = w_forget.shape[1]
    seq_count = lax.axis_size("seq")
    fsdp_count = lax.axis_size("fsdp")
    own_heads = w_qkv.shape[2]
    own_dims = w_qkv.shape[3]
    own_cols = 3 * own_heads * own_dims
    rows = req_count * new_count
    inner_width = head_count * HEAD_DIM
    piece_len = cache_forget.shape[2]
    logit_scale = HEAD_DIM ** (-0.5)
    seq_index = lax.axis_index("seq")
    head_start = seq_index * own_heads
    normed = normalize(hidden_in, norm_gain).reshape(rows, width)
    normed_all = lax.all_to_all(
        jnp.broadcast_to(normed[None], (fsdp_count, rows, width)), "fsdp", 0, 0, tiled=True
    ).reshape(fsdp_count * rows, width)
    projected = jnp.einsum(
        "dk,nd->kn",
        w_qkv.reshape(width, own_cols),
        normed_all,
        preferred_element_type=jnp.float32,
    ).astype(jnp.bfloat16)
    outgoing = (
        projected.reshape(3, own_heads * own_dims, fsdp_count, rows)
        .transpose(2, 1, 0, 3)
        .reshape(fsdp_count, 1, own_heads * own_dims * 3 * rows)
    )
    outgoing = jnp.broadcast_to(
        outgoing, (fsdp_count, seq_count, own_heads * own_dims * 3 * rows)
    ).reshape(fsdp_count * seq_count, 2, own_heads * own_dims * 3 * rows // 2)
    incoming = lax.all_to_all(outgoing, ("fsdp", "seq"), 0, 0, tiled=True)
    incoming = incoming.reshape(fsdp_count * seq_count * own_heads * own_dims, 3 * rows)
    src_row = jnp.arange(fsdp_count * seq_count * own_heads * own_dims, dtype=jnp.int32)
    src_dev = src_row // (own_heads * own_dims)
    src_head = (src_row // own_dims) % own_heads
    src_dim = src_row % own_dims
    target = ((src_dev % seq_count) * own_heads + src_head) * HEAD_DIM + (
        src_dev // seq_count
    ) * own_dims + src_dim
    placement = (target[:, None] == jnp.arange(inner_width, dtype=jnp.int32)[None, :]).astype(
        jnp.bfloat16
    )
    all_heads = jnp.einsum(
        "kx,kj->xj", incoming, placement, preferred_element_type=jnp.float32
    ).astype(jnp.bfloat16).reshape(3, req_count, new_count, inner_width)
    gate_logit = (
        jnp.dot(normed, w_forget, preferred_element_type=jnp.float32).reshape(
            req_count, new_count, head_count
        )
        + forget_bias
    )
    prefix = jnp.cumsum(jax.nn.log_sigmoid(gate_logit), axis=1)
    slot_ids = jnp.arange(seq_count, dtype=jnp.int32)
    holders = piece_map[:, :, None] == slot_ids[None, None, :]
    piece_of_slot = jnp.sum(jnp.where(holders, slot_ids[None, :, None], 0), axis=1)
    own_piece = jnp.sum(jnp.where(piece_map == seq_index, slot_ids[None, :], 0), axis=1)
    steps = jnp.arange(piece_len, dtype=jnp.int32)
    positions = own_piece[:, None] * piece_len + steps[None, :]
    live_mask = positions < cache_lengths[:, None]
    masked = jnp.where(live_mask[:, None, :], cache_forget, 0.0)
    piece_total = jnp.sum(masked, axis=-1)
    later_step = (steps[:, None] > steps[None, :]).astype(jnp.float32)
    trailing_part = jnp.einsum(
        "rhl,lj->rhj", masked, later_step, precision=lax.Precision.HIGHEST,
        preferred_element_type=jnp.float32,
    )
    step_rows = 8
    pad_steps = ((0, 0), (0, step_rows - new_count))
    query_rows = jnp.pad(all_heads[0], pad_steps + ((0, 0),))
    prefix_rows = jnp.pad(jnp.transpose(prefix, (0, 2, 1)), ((0, 0),) + pad_steps).reshape(
        req_count, head_count * step_rows, 1
    )
    live_row = live_mask.astype(jnp.float32)[:, None, :]
    total_rows = jnp.broadcast_to(
        piece_total[:, :, None], (req_count, head_count, step_rows)
    ).reshape(req_count, head_count * step_rows, 1)
    packed = piece_attention(
        query_rows, cache_keys, cache_values, trailing_part, prefix_rows, live_row, total_rows, seq_count
    )
    own_rows = lax.dynamic_slice_in_dim(
        all_heads, head_start * HEAD_DIM, own_heads * HEAD_DIM, 3
    ).reshape(3, req_count, new_count, own_heads, HEAD_DIM)
    own_prefix = jnp.transpose(
        lax.dynamic_slice_in_dim(prefix, head_start, own_heads, 2), (0, 2, 1)
    )
    fresh_logits = (
        jnp.einsum(
            "rmhd,rnhd->rhmn",
            own_rows[0],
            own_rows[1],
            preferred_element_type=jnp.float32,
        )
        * logit_scale
    )
    fresh_logits = fresh_logits + own_prefix[..., :, None] - own_prefix[..., None, :]
    step_ids = jnp.arange(new_count, dtype=jnp.int32)
    causal = (step_ids[None, :] <= step_ids[:, None])[None, None]
    fresh_max = jnp.max(jnp.where(causal, fresh_logits, neg_fill), axis=-1)
    new_weights = jnp.where(causal, jnp.exp(fresh_logits - fresh_max[..., None]), 0.0)
    fresh_sum = jnp.sum(new_weights, axis=-1)
    fresh_acc = jnp.einsum(
        "rhmn,rnhd->rhmd",
        new_weights.astype(jnp.bfloat16),
        own_rows[2],
        preferred_element_type=jnp.float32,
    )
    parts = lax.all_to_all(packed, "seq", 0, 0, tiled=True)[:, :, :, :new_count]
    part_acc = parts[..., :HEAD_DIM]
    part_max = parts[..., HEAD_DIM]
    part_sum = parts[..., HEAD_DIM + 1]
    part_total = parts[:, :, :, 0, HEAD_DIM + 2]
    later_piece = (piece_of_slot.T[None, :, :] > piece_of_slot.T[:, None, :])[..., None]
    later_sum = jnp.sum(jnp.where(later_piece, part_total[None], 0.0), axis=1)
    part_max = part_max + later_sum[..., None]
    joint_max = jnp.maximum(jnp.max(part_max, axis=0), fresh_max)
    factor = jnp.exp(part_max - joint_max[None])
    carried = jnp.exp(fresh_max - joint_max)
    total_sum = jnp.sum(part_sum * factor, axis=0) + fresh_sum * carried
    blend_weights = jnp.sum(part_acc * factor[..., None], axis=0) + fresh_acc * carried[..., None]
    result = blend_weights / total_sum[..., None]
    live_rows = (step_ids[None, :] <= draft_counts[:, None])[:, None, :, None]
    result = jnp.where(live_rows, result, 0.0)
    return (
        jnp.transpose(result, (0, 2, 1, 3))
        .reshape(req_count, new_count, own_heads * HEAD_DIM)
        .astype(jnp.bfloat16)
    )


def solution(mesh):
    in_specs = (
        P("fsdp", None, None),
        P(),
        P(None, None, "seq", "fsdp"),
        P(),
        P(),
        P("fsdp", "seq", None),
        P("fsdp", "seq", None),
        P("fsdp", None, "seq"),
        P("fsdp"),
        P("fsdp", None),
        P("fsdp"),
    )
    out_specs = P("fsdp", None, "seq")
    return jax.shard_map(body, mesh=mesh, in_specs=in_specs, out_specs=out_specs, check_vma=False)
```

```python
import jax
import jax.numpy as jnp
from jax import lax
from jax.experimental import pallas as pl
from jax.experimental.pallas import tpu as pltpu
from jax.sharding import PartitionSpec as P

HEAD_DIM = 64


norm_eps = 1e-06
neg_fill = -1e30


def normalize(rows, gain):
    values = rows.astype(jnp.float32)
    mean_sq = jnp.mean(values * values, axis=-1, keepdims=True)
    return (values * lax.rsqrt(mean_sq + norm_eps) * gain).astype(jnp.bfloat16)


def fold_kernel(parts_ref, later_ref, fresh_ref, keep_ref, out_ref):
    source_count = parts_ref.shape[0]
    fresh = fresh_ref[...]
    raised = []
    for source in range(source_count):
        later = jnp.zeros_like(fresh[:, :1])
        for other in range(source_count):
            later = later + later_ref[source, other] * parts_ref[other][:, HEAD_DIM + 2 : HEAD_DIM + 3]
        raised.append(parts_ref[source][:, HEAD_DIM : HEAD_DIM + 1] + later)
    joint = fresh[:, HEAD_DIM : HEAD_DIM + 1]
    for value in raised:
        joint = jnp.maximum(joint, value)
    blend = fresh * jnp.exp(fresh[:, HEAD_DIM : HEAD_DIM + 1] - joint)
    for source in range(source_count):
        blend = blend + parts_ref[source] * jnp.exp(raised[source] - joint)
    result = blend[:, :HEAD_DIM] / blend[:, HEAD_DIM + 1 : HEAD_DIM + 2]
    out_ref[...] = jnp.where(keep_ref[...] > 0.5, result, 0.0).astype(out_ref.dtype)


def fold_partials(parts, later_rows, fresh_rows, keep_rows):
    return pl.pallas_call(
        fold_kernel,
        out_shape=jax.ShapeDtypeStruct((parts.shape[1], HEAD_DIM), jnp.bfloat16),
    )(parts, later_rows, fresh_rows, keep_rows)


def attention_kernel(q_ref, k_ref, v_ref, trail_ref, prefix_ref, live_ref, total_ref, out_ref):
    step_rows = q_ref.shape[1]
    head_count = trail_ref.shape[1]
    piece_len = trail_ref.shape[2]
    inner_width = q_ref.shape[2]
    row_count = head_count * step_rows
    pair_count = inner_width // 128
    row_step = lax.broadcasted_iota(jnp.int32, (row_count, step_rows), 0) % step_rows
    spread = (row_step == lax.broadcasted_iota(jnp.int32, (row_count, step_rows), 1)).astype(jnp.bfloat16)
    repeated = jnp.dot(spread, q_ref[0], preferred_element_type=jnp.float32)
    row_head = lax.broadcasted_iota(jnp.int32, (row_count, inner_width), 0) // step_rows
    col_head = lax.broadcasted_iota(jnp.int32, (row_count, inner_width), 1) // HEAD_DIM
    query_blocks = jnp.where(row_head == col_head, repeated, 0.0).astype(jnp.bfloat16)
    scores = lax.dot_general(
        query_blocks, k_ref[0], (((1,), (1,)), ((), ())), preferred_element_type=jnp.float32
    )
    trailing = jnp.broadcast_to(
        trail_ref[0][:, None, :], (head_count, step_rows, piece_len)
    ).reshape(row_count, piece_len)
    scores = scores * (HEAD_DIM ** (-0.5)) + (trailing + prefix_ref[0])
    live = live_ref[0] > 0.5
    row_max = jnp.max(jnp.where(live, scores, neg_fill), axis=1, keepdims=True)
    weights = jnp.where(live, jnp.exp(scores - row_max), 0.0)
    weight_sum = jnp.sum(weights, axis=1, keepdims=True)
    blocks = jnp.dot(weights.astype(jnp.bfloat16), v_ref[0], preferred_element_type=jnp.float32)
    row = lax.broadcasted_iota(jnp.int32, (row_count, 128), 0)
    picked = jnp.zeros((row_count, 128), jnp.float32)
    for pair in range(pair_count):
        lo = 2 * pair * step_rows
        picked = jnp.where(
            (row >= lo) & (row < lo + 2 * step_rows), blocks[:, pair * 128 : (pair + 1) * 128], picked
        )
    odd = (row // step_rows) % 2 == 1
    accum = jnp.where(odd, pltpu.roll(picked, 64, 1), picked)
    lane = lax.broadcasted_iota(jnp.int32, (row_count, 128), 1)
    packed = jnp.where(lane < HEAD_DIM, accum, 0.0)
    packed = jnp.where(lane == HEAD_DIM, row_max, packed)
    packed = jnp.where(lane == HEAD_DIM + 1, weight_sum, packed)
    packed = jnp.where(lane == HEAD_DIM + 2, total_ref[0], packed)
    own_heads = out_ref.shape[2]
    for head in range(head_count):
        out_ref[head // own_heads, 0, head % own_heads] = packed[head * step_rows : (head + 1) * step_rows]


def piece_attention(query_rows, keys, values, trailing, prefix_rows, live_row, total_rows, seq_count):
    req_count, step_rows, inner_width = query_rows.shape
    head_count = trailing.shape[1]
    piece_len = keys.shape[1]
    row_count = head_count * step_rows
    own_heads = head_count // seq_count
    return pl.pallas_call(
        attention_kernel,
        grid=(req_count,),
        in_specs=[
            pl.BlockSpec((1, step_rows, inner_width), lambda r: (r, 0, 0)),
            pl.BlockSpec((1, piece_len, inner_width), lambda r: (r, 0, 0)),
            pl.BlockSpec((1, piece_len, inner_width), lambda r: (r, 0, 0)),
            pl.BlockSpec((1, head_count, piece_len), lambda r: (r, 0, 0)),
            pl.BlockSpec((1, row_count, 1), lambda r: (r, 0, 0)),
            pl.BlockSpec((1, 1, piece_len), lambda r: (r, 0, 0)),
            pl.BlockSpec((1, row_count, 1), lambda r: (r, 0, 0)),
        ],
        out_specs=pl.BlockSpec((seq_count, 1, own_heads, step_rows, 128), lambda r: (0, r, 0, 0, 0)),
        out_shape=jax.ShapeDtypeStruct((seq_count, req_count, own_heads, step_rows, 128), jnp.float32),
    )(query_rows, keys, values, trailing, prefix_rows, live_row, total_rows)


def body(
    hidden_in,
    norm_gain,
    w_qkv,
    w_forget,
    forget_bias,
    cache_keys,
    cache_values,
    cache_forget,
    cache_lengths,
    piece_map,
    draft_counts,
):
    req_count, new_count, width = hidden_in.shape
    head_count = w_forget.shape[1]
    seq_count = lax.axis_size("seq")
    fsdp_count = lax.axis_size("fsdp")
    own_heads = w_qkv.shape[2]
    own_dims = w_qkv.shape[3]
    own_cols = 3 * own_heads * own_dims
    rows = req_count * new_count
    inner_width = head_count * HEAD_DIM
    piece_len = cache_forget.shape[2]
    logit_scale = HEAD_DIM ** (-0.5)
    seq_index = lax.axis_index("seq")
    head_start = seq_index * own_heads
    normed = normalize(hidden_in, norm_gain).reshape(rows, width)
    normed_all = lax.all_to_all(
        jnp.broadcast_to(normed[None], (fsdp_count, rows, width)), "fsdp", 0, 0, tiled=True
    ).reshape(fsdp_count * rows, width)
    projected = jnp.einsum(
        "dk,nd->kn",
        w_qkv.reshape(width, own_cols),
        normed_all,
        preferred_element_type=jnp.float32,
    ).astype(jnp.bfloat16)
    outgoing = (
        projected.reshape(3, own_heads * own_dims, fsdp_count, rows)
        .transpose(2, 1, 0, 3)
        .reshape(fsdp_count, 1, own_heads * own_dims * 3 * rows)
    )
    outgoing = jnp.broadcast_to(
        outgoing, (fsdp_count, seq_count, own_heads * own_dims * 3 * rows)
    ).reshape(fsdp_count * seq_count, 2, own_heads * own_dims * 3 * rows // 2)
    incoming = lax.all_to_all(outgoing, ("fsdp", "seq"), 0, 0, tiled=True)
    incoming = incoming.reshape(fsdp_count * seq_count * own_heads * own_dims, 3 * rows)
    src_row = jnp.arange(fsdp_count * seq_count * own_heads * own_dims, dtype=jnp.int32)
    src_dev = src_row // (own_heads * own_dims)
    src_head = (src_row // own_dims) % own_heads
    src_dim = src_row % own_dims
    target = ((src_dev % seq_count) * own_heads + src_head) * HEAD_DIM + (
        src_dev // seq_count
    ) * own_dims + src_dim
    placement = (target[:, None] == jnp.arange(inner_width, dtype=jnp.int32)[None, :]).astype(
        jnp.bfloat16
    )
    all_heads = jnp.einsum(
        "kx,kj->xj", incoming, placement, preferred_element_type=jnp.float32
    ).astype(jnp.bfloat16).reshape(3, req_count, new_count, inner_width)
    gate_logit = (
        jnp.dot(normed, w_forget, preferred_element_type=jnp.float32).reshape(
            req_count, new_count, head_count
        )
        + forget_bias
    )
    prefix = jnp.cumsum(jax.nn.log_sigmoid(gate_logit), axis=1)
    slot_ids = jnp.arange(seq_count, dtype=jnp.int32)
    holders = piece_map[:, :, None] == slot_ids[None, None, :]
    piece_of_slot = jnp.sum(jnp.where(holders, slot_ids[None, :, None], 0), axis=1)
    own_piece = jnp.sum(jnp.where(piece_map == seq_index, slot_ids[None, :], 0), axis=1)
    steps = jnp.arange(piece_len, dtype=jnp.int32)
    positions = own_piece[:, None] * piece_len + steps[None, :]
    live_mask = positions < cache_lengths[:, None]
    masked = jnp.where(live_mask[:, None, :], cache_forget, 0.0)
    piece_total = jnp.sum(masked, axis=-1)
    later_step = (steps[:, None] > steps[None, :]).astype(jnp.float32)
    trailing_part = jnp.einsum(
        "rhl,lj->rhj", masked, later_step, precision=lax.Precision.HIGHEST,
        preferred_element_type=jnp.float32,
    )
    step_rows = 8
    pad_steps = ((0, 0), (0, step_rows - new_count))
    query_rows = jnp.pad(all_heads[0], pad_steps + ((0, 0),))
    prefix_rows = jnp.pad(jnp.transpose(prefix, (0, 2, 1)), ((0, 0),) + pad_steps).reshape(
        req_count, head_count * step_rows, 1
    )
    live_row = live_mask.astype(jnp.float32)[:, None, :]
    total_rows = jnp.broadcast_to(
        piece_total[:, :, None], (req_count, head_count, step_rows)
    ).reshape(req_count, head_count * step_rows, 1)
    packed = piece_attention(
        query_rows, cache_keys, cache_values, trailing_part, prefix_rows, live_row, total_rows, seq_count
    )
    own_rows = lax.dynamic_slice_in_dim(
        all_heads, head_start * HEAD_DIM, own_heads * HEAD_DIM, 3
    ).reshape(3, req_count, new_count, own_heads, HEAD_DIM)
    own_prefix = jnp.transpose(
        lax.dynamic_slice_in_dim(prefix, head_start, own_heads, 2), (0, 2, 1)
    )
    fresh_logits = (
        jnp.einsum(
            "rmhd,rnhd->rhmn",
            own_rows[0],
            own_rows[1],
            preferred_element_type=jnp.float32,
        )
        * logit_scale
    )
    fresh_logits = fresh_logits + own_prefix[..., :, None] - own_prefix[..., None, :]
    step_ids = jnp.arange(new_count, dtype=jnp.int32)
    causal = (step_ids[None, :] <= step_ids[:, None])[None, None]
    fresh_max = jnp.max(jnp.where(causal, fresh_logits, neg_fill), axis=-1)
    new_weights = jnp.where(causal, jnp.exp(fresh_logits - fresh_max[..., None]), 0.0)
    fresh_sum = jnp.sum(new_weights, axis=-1)
    fresh_acc = jnp.einsum(
        "rhmn,rnhd->rhmd",
        new_weights.astype(jnp.bfloat16),
        own_rows[2],
        preferred_element_type=jnp.float32,
    )
    pad_rows = ((0, 0), (0, 0), (0, step_rows - new_count))
    fresh_rows = jnp.concatenate(
        [
            jnp.pad(fresh_acc, pad_rows + ((0, 0),)),
            jnp.pad(fresh_max, pad_rows)[..., None],
            jnp.pad(fresh_sum, pad_rows)[..., None],
            jnp.zeros((req_count, own_heads, step_rows, 128 - HEAD_DIM - 2), jnp.float32),
        ],
        axis=-1,
    ).reshape(req_count * own_heads * step_rows, 128)
    later_piece = (piece_of_slot.T[:, None, :] < piece_of_slot.T[None, :, :]).astype(jnp.float32)
    later_rows = jnp.broadcast_to(
        later_piece[:, :, :, None, None], (seq_count, seq_count, req_count, own_heads, step_rows)
    ).reshape(seq_count, seq_count, req_count * own_heads * step_rows, 1)
    pad_ids = jnp.arange(step_rows, dtype=jnp.int32)
    keep_rows = jnp.broadcast_to(
        (pad_ids[None, :] <= draft_counts[:, None]).astype(jnp.float32)[:, None, :],
        (req_count, own_heads, step_rows),
    ).reshape(req_count * own_heads * step_rows, 1)
    parts = lax.all_to_all(packed, "seq", 0, 0, tiled=True).reshape(
        seq_count, req_count * own_heads * step_rows, 128
    )
    folded = fold_partials(parts, later_rows, fresh_rows, keep_rows)
    result = folded.reshape(req_count, own_heads, step_rows, HEAD_DIM)[:, :, :new_count]
    return (
        jnp.transpose(result, (0, 2, 1, 3))
        .reshape(req_count, new_count, own_heads * HEAD_DIM)
    )


def solution(mesh):
    in_specs = (
        P("fsdp", None, None),
        P(),
        P(None, None, "seq", "fsdp"),
        P(),
        P(),
        P("fsdp", "seq", None),
        P("fsdp", "seq", None),
        P("fsdp", None, "seq"),
        P("fsdp"),
        P("fsdp", None),
        P("fsdp"),
    )
    out_specs = P("fsdp", None, "seq")
    return jax.shard_map(body, mesh=mesh, in_specs=in_specs, out_specs=out_specs, check_vma=False)
```

```python
import jax
import jax.numpy as jnp
from jax import lax
from jax.experimental import pallas as pl
from jax.experimental.pallas import tpu as pltpu
from jax.sharding import PartitionSpec as P

HEAD_DIM = 64


norm_eps = 1e-06
neg_fill = -1e30


def normalize(rows, gain):
    values = rows.astype(jnp.float32)
    mean_sq = jnp.mean(values * values, axis=-1, keepdims=True)
    return (values * lax.rsqrt(mean_sq + norm_eps) * gain).astype(jnp.bfloat16)


def attention_kernel(q_ref, k_ref, v_ref, trail_ref, prefix_ref, live_ref, total_ref, out_ref):
    head_count = trail_ref.shape[1]
    piece_len = trail_ref.shape[2]
    row_count = prefix_ref.shape[1]
    step_rows = row_count // head_count
    query_count, inner_width = q_ref.shape
    new_count = query_count // 3 // pl.num_programs(0)
    pair_count = inner_width // 128
    row_step = lax.broadcasted_iota(jnp.int32, (row_count, query_count), 0) % step_rows
    source = lax.broadcasted_iota(jnp.int32, (row_count, query_count), 1)
    spread = (
        (source == pl.program_id(0) * new_count + row_step) & (row_step < new_count)
    ).astype(jnp.bfloat16)
    repeated = jnp.dot(spread, q_ref[...], preferred_element_type=jnp.float32)
    row_head = lax.broadcasted_iota(jnp.int32, (row_count, inner_width), 0) // step_rows
    col_head = lax.broadcasted_iota(jnp.int32, (row_count, inner_width), 1) // HEAD_DIM
    query_blocks = jnp.where(row_head == col_head, repeated, 0.0).astype(jnp.bfloat16)
    scores = lax.dot_general(
        query_blocks, k_ref[0], (((1,), (1,)), ((), ())), preferred_element_type=jnp.float32
    )
    trailing = jnp.broadcast_to(
        trail_ref[0][:, None, :], (head_count, step_rows, piece_len)
    ).reshape(row_count, piece_len)
    scores = scores * (HEAD_DIM ** (-0.5)) + (trailing + prefix_ref[0])
    live = live_ref[0] > 0.5
    row_max = jnp.max(jnp.where(live, scores, neg_fill), axis=1, keepdims=True)
    weights = jnp.where(live, jnp.exp(scores - row_max), 0.0)
    weight_sum = jnp.sum(weights, axis=1, keepdims=True)
    blocks = jnp.dot(weights.astype(jnp.bfloat16), v_ref[0], preferred_element_type=jnp.float32)
    row = lax.broadcasted_iota(jnp.int32, (row_count, 128), 0)
    picked = jnp.zeros((row_count, 128), jnp.float32)
    for pair in range(pair_count):
        lo = 2 * pair * step_rows
        picked = jnp.where(
            (row >= lo) & (row < lo + 2 * step_rows), blocks[:, pair * 128 : (pair + 1) * 128], picked
        )
    odd = (row // step_rows) % 2 == 1
    accum = jnp.where(odd, pltpu.roll(picked, 64, 1), picked)
    lane = lax.broadcasted_iota(jnp.int32, (row_count, 128), 1)
    packed = jnp.where(lane < HEAD_DIM, accum, 0.0)
    packed = jnp.where(lane == HEAD_DIM, row_max, packed)
    packed = jnp.where(lane == HEAD_DIM + 1, weight_sum, packed)
    packed = jnp.where(lane == HEAD_DIM + 2, total_ref[0], packed)
    own_heads = out_ref.shape[2]
    for head in range(head_count):
        out_ref[head // own_heads, 0, head % own_heads] = packed[head * step_rows : (head + 1) * step_rows]


def piece_attention(query_rows, keys, values, trailing, prefix_rows, live_row, total_rows, seq_count):
    query_count, inner_width = query_rows.shape
    req_count = keys.shape[0]
    head_count = trailing.shape[1]
    piece_len = keys.shape[1]
    row_count = prefix_rows.shape[1]
    step_rows = row_count // head_count
    own_heads = head_count // seq_count
    return pl.pallas_call(
        attention_kernel,
        grid=(req_count,),
        in_specs=[
            pl.BlockSpec((query_count, inner_width), lambda r: (0, 0)),
            pl.BlockSpec((1, piece_len, inner_width), lambda r: (r, 0, 0)),
            pl.BlockSpec((1, piece_len, inner_width), lambda r: (r, 0, 0)),
            pl.BlockSpec((1, head_count, piece_len), lambda r: (r, 0, 0)),
            pl.BlockSpec((1, row_count, 1), lambda r: (r, 0, 0)),
            pl.BlockSpec((1, 1, piece_len), lambda r: (r, 0, 0)),
            pl.BlockSpec((1, row_count, 1), lambda r: (r, 0, 0)),
        ],
        out_specs=pl.BlockSpec((seq_count, 1, own_heads, step_rows, 128), lambda r: (0, r, 0, 0, 0)),
        out_shape=jax.ShapeDtypeStruct((seq_count, req_count, own_heads, step_rows, 128), jnp.float32),
    )(query_rows, keys, values, trailing, prefix_rows, live_row, total_rows)


def body(
    hidden_in,
    norm_gain,
    w_qkv,
    w_forget,
    forget_bias,
    cache_keys,
    cache_values,
    cache_forget,
    cache_lengths,
    piece_map,
    draft_counts,
):
    req_count, new_count, width = hidden_in.shape
    head_count = w_forget.shape[1]
    seq_count = lax.axis_size("seq")
    fsdp_count = lax.axis_size("fsdp")
    own_heads = w_qkv.shape[2]
    own_dims = w_qkv.shape[3]
    own_cols = 3 * own_heads * own_dims
    rows = req_count * new_count
    inner_width = head_count * HEAD_DIM
    piece_len = cache_forget.shape[2]
    logit_scale = HEAD_DIM ** (-0.5)
    seq_index = lax.axis_index("seq")
    head_start = seq_index * own_heads
    normed = normalize(hidden_in, norm_gain).reshape(rows, width)
    normed_all = lax.all_to_all(
        jnp.broadcast_to(normed[None], (fsdp_count, rows, width)), "fsdp", 0, 0, tiled=True
    ).reshape(fsdp_count * rows, width)
    projected = jnp.einsum(
        "dk,nd->kn",
        w_qkv.reshape(width, own_cols),
        normed_all,
        preferred_element_type=jnp.float32,
    ).astype(jnp.bfloat16)
    outgoing = (
        projected.reshape(3, own_heads * own_dims, fsdp_count, rows)
        .transpose(2, 1, 0, 3)
        .reshape(fsdp_count, 1, own_heads * own_dims * 3 * rows)
    )
    outgoing = jnp.broadcast_to(
        outgoing, (fsdp_count, seq_count, own_heads * own_dims * 3 * rows)
    ).reshape(fsdp_count * seq_count, 2, own_heads * own_dims * 3 * rows // 2)
    incoming = lax.all_to_all(outgoing, ("fsdp", "seq"), 0, 0, tiled=True)
    incoming = incoming.reshape(fsdp_count * seq_count * own_heads * own_dims, 3 * rows)
    src_row = jnp.arange(fsdp_count * seq_count * own_heads * own_dims, dtype=jnp.int32)
    src_dev = src_row // (own_heads * own_dims)
    src_head = (src_row // own_dims) % own_heads
    src_dim = src_row % own_dims
    target = ((src_dev % seq_count) * own_heads + src_head) * HEAD_DIM + (
        src_dev // seq_count
    ) * own_dims + src_dim
    placement = (target[:, None] == jnp.arange(inner_width, dtype=jnp.int32)[None, :]).astype(
        jnp.bfloat16
    )
    head_rows = jnp.einsum(
        "kx,kj->xj", incoming, placement, preferred_element_type=jnp.float32
    ).astype(jnp.bfloat16)
    all_heads = head_rows.reshape(3, req_count, new_count, inner_width)
    gate_logit = (
        jnp.dot(normed, w_forget, preferred_element_type=jnp.float32).reshape(
            req_count, new_count, head_count
        )
        + forget_bias
    )
    prefix = jnp.cumsum(jax.nn.log_sigmoid(gate_logit), axis=1)
    slot_ids = jnp.arange(seq_count, dtype=jnp.int32)
    holders = piece_map[:, :, None] == slot_ids[None, None, :]
    piece_of_slot = jnp.sum(jnp.where(holders, slot_ids[None, :, None], 0), axis=1)
    own_piece = jnp.sum(jnp.where(piece_map == seq_index, slot_ids[None, :], 0), axis=1)
    steps = jnp.arange(piece_len, dtype=jnp.int32)
    positions = own_piece[:, None] * piece_len + steps[None, :]
    live_mask = positions < cache_lengths[:, None]
    masked = jnp.where(live_mask[:, None, :], cache_forget, 0.0)
    piece_total = jnp.sum(masked, axis=-1)
    later_step = (steps[:, None] > steps[None, :]).astype(jnp.float32)
    trailing_part = jnp.einsum(
        "rhl,lj->rhj", masked, later_step, precision=lax.Precision.HIGHEST,
        preferred_element_type=jnp.float32,
    )
    step_rows = 8
    pad_steps = ((0, 0), (0, step_rows - new_count))
    prefix_rows = jnp.pad(jnp.transpose(prefix, (0, 2, 1)), ((0, 0),) + pad_steps).reshape(
        req_count, head_count * step_rows, 1
    )
    live_row = live_mask.astype(jnp.float32)[:, None, :]
    total_rows = jnp.broadcast_to(
        piece_total[:, :, None], (req_count, head_count, step_rows)
    ).reshape(req_count, head_count * step_rows, 1)
    packed = piece_attention(
        head_rows, cache_keys, cache_values, trailing_part, prefix_rows, live_row, total_rows, seq_count
    )
    parts = lax.all_to_all(packed, "seq", 0, 0, tiled=True)[:, :, :, :new_count]
    part_acc = parts[..., :HEAD_DIM]
    part_max = parts[..., HEAD_DIM]
    part_sum = parts[..., HEAD_DIM + 1]
    part_total = parts[:, :, :, 0, HEAD_DIM + 2]
    later_piece = (piece_of_slot.T[None, :, :] > piece_of_slot.T[:, None, :])[..., None]
    later_sum = jnp.sum(jnp.where(later_piece, part_total[None], 0.0), axis=1)
    part_max = part_max + later_sum[..., None]
    cache_max = jnp.max(part_max, axis=0)
    factor = jnp.exp(part_max - cache_max[None])
    cache_sum = jnp.sum(part_sum * factor, axis=0)
    cache_acc = jnp.sum(part_acc * factor[..., None], axis=0)
    own_rows = lax.dynamic_slice_in_dim(
        all_heads, head_start * HEAD_DIM, own_heads * HEAD_DIM, 3
    ).reshape(3, req_count, new_count, own_heads, HEAD_DIM)
    own_prefix = jnp.transpose(
        lax.dynamic_slice_in_dim(prefix, head_start, own_heads, 2), (0, 2, 1)
    )
    fresh_logits = (
        jnp.einsum(
            "rmhd,rnhd->rhmn",
            own_rows[0],
            own_rows[1],
            preferred_element_type=jnp.float32,
        )
        * logit_scale
    )
    fresh_logits = fresh_logits + own_prefix[..., :, None] - own_prefix[..., None, :]
    step_ids = jnp.arange(new_count, dtype=jnp.int32)
    causal = (step_ids[None, :] <= step_ids[:, None])[None, None]
    joint_max = jnp.maximum(cache_max, jnp.max(jnp.where(causal, fresh_logits, neg_fill), axis=-1))
    new_weights = jnp.where(causal, jnp.exp(fresh_logits - joint_max[..., None]), 0.0)
    carried = jnp.exp(cache_max - joint_max)
    total_sum = cache_sum * carried + jnp.sum(new_weights, axis=-1)
    blend_weights = cache_acc * carried[..., None] + jnp.einsum(
        "rhmn,rnhd->rhmd",
        new_weights.astype(jnp.bfloat16),
        own_rows[2],
        preferred_element_type=jnp.float32,
    )
    result = blend_weights / total_sum[..., None]
    live_rows = (step_ids[None, :] <= draft_counts[:, None])[:, None, :, None]
    result = jnp.where(live_rows, result, 0.0)
    return (
        jnp.transpose(result, (0, 2, 1, 3))
        .reshape(req_count, new_count, own_heads * HEAD_DIM)
        .astype(jnp.bfloat16)
    )


def solution(mesh):
    in_specs = (
        P("fsdp", None, None),
        P(),
        P(None, None, "seq", "fsdp"),
        P(),
        P(),
        P("fsdp", "seq", None),
        P("fsdp", "seq", None),
        P("fsdp", None, "seq"),
        P("fsdp"),
        P("fsdp", None),
        P("fsdp"),
    )
    out_specs = P("fsdp", None, "seq")
    return jax.shard_map(body, mesh=mesh, in_specs=in_specs, out_specs=out_specs, check_vma=False)
```

```python
import jax
import jax.numpy as jnp
from jax import lax
from jax.experimental import pallas as pl
from jax.experimental.pallas import tpu as pltpu
from jax.sharding import PartitionSpec as P

HEAD_DIM = 64


norm_eps = 1e-06
neg_fill = -1e30


def normalize(rows, gain):
    values = rows.astype(jnp.float32)
    mean_sq = jnp.mean(values * values, axis=-1, keepdims=True)
    return (values * lax.rsqrt(mean_sq + norm_eps) * gain).astype(jnp.bfloat16)


def attention_kernel(q_ref, k_ref, v_ref, trail_ref, prefix_ref, live_ref, total_ref, out_ref):
    step_rows = q_ref.shape[1]
    head_count = trail_ref.shape[1]
    piece_len = trail_ref.shape[2]
    inner_width = q_ref.shape[2]
    row_count = head_count * step_rows
    pair_count = inner_width // 128
    row_step = lax.broadcasted_iota(jnp.int32, (row_count, step_rows), 0) % step_rows
    spread = (row_step == lax.broadcasted_iota(jnp.int32, (row_count, step_rows), 1)).astype(jnp.bfloat16)
    repeated = jnp.dot(spread, q_ref[0], preferred_element_type=jnp.float32)
    row_head = lax.broadcasted_iota(jnp.int32, (row_count, inner_width), 0) // step_rows
    col_head = lax.broadcasted_iota(jnp.int32, (row_count, inner_width), 1) // HEAD_DIM
    query_blocks = jnp.where(row_head == col_head, repeated, 0.0).astype(jnp.bfloat16)
    scores = lax.dot_general(
        query_blocks, k_ref[0], (((1,), (1,)), ((), ())), preferred_element_type=jnp.float32
    )
    trailing = jnp.broadcast_to(
        trail_ref[0][:, None, :], (head_count, step_rows, piece_len)
    ).reshape(row_count, piece_len)
    scores = scores * (HEAD_DIM ** (-0.5)) + (trailing + prefix_ref[0])
    live = live_ref[0] > 0.5
    row_max = jnp.max(jnp.where(live, scores, neg_fill), axis=1, keepdims=True)
    weights = jnp.where(live, jnp.exp(scores - row_max), 0.0)
    weight_sum = jnp.sum(weights, axis=1, keepdims=True)
    blocks = jnp.dot(weights.astype(jnp.bfloat16), v_ref[0], preferred_element_type=jnp.float32)
    row = lax.broadcasted_iota(jnp.int32, (row_count, 128), 0)
    picked = jnp.zeros((row_count, 128), jnp.float32)
    for pair in range(pair_count):
        lo = 2 * pair * step_rows
        picked = jnp.where(
            (row >= lo) & (row < lo + 2 * step_rows), blocks[:, pair * 128 : (pair + 1) * 128], picked
        )
    odd = (row // step_rows) % 2 == 1
    accum = jnp.where(odd, pltpu.roll(picked, 64, 1), picked)
    lane = lax.broadcasted_iota(jnp.int32, (row_count, 128), 1)
    packed = jnp.where(lane < HEAD_DIM, accum, 0.0)
    packed = jnp.where(lane == HEAD_DIM, row_max, packed)
    packed = jnp.where(lane == HEAD_DIM + 1, weight_sum, packed)
    packed = jnp.where(lane == HEAD_DIM + 2, total_ref[0], packed)
    own_heads = out_ref.shape[2]
    for head in range(head_count):
        out_ref[head // own_heads, 0, head % own_heads] = packed[head * step_rows : (head + 1) * step_rows]


def piece_attention(query_rows, keys, values, trailing, prefix_rows, live_row, total_rows, seq_count):
    req_count, step_rows, inner_width = query_rows.shape
    head_count = trailing.shape[1]
    piece_len = keys.shape[1]
    row_count = head_count * step_rows
    own_heads = head_count // seq_count
    return pl.pallas_call(
        attention_kernel,
        grid=(req_count,),
        in_specs=[
            pl.BlockSpec((1, step_rows, inner_width), lambda r: (r, 0, 0)),
            pl.BlockSpec((1, piece_len, inner_width), lambda r: (r, 0, 0)),
            pl.BlockSpec((1, piece_len, inner_width), lambda r: (r, 0, 0)),
            pl.BlockSpec((1, head_count, piece_len), lambda r: (r, 0, 0)),
            pl.BlockSpec((1, row_count, 1), lambda r: (r, 0, 0)),
            pl.BlockSpec((1, 1, piece_len), lambda r: (r, 0, 0)),
            pl.BlockSpec((1, row_count, 1), lambda r: (r, 0, 0)),
        ],
        out_specs=pl.BlockSpec((seq_count, 1, own_heads, step_rows, 128), lambda r: (0, r, 0, 0, 0)),
        out_shape=jax.ShapeDtypeStruct((seq_count, req_count, own_heads, step_rows, 128), jnp.float32),
    )(query_rows, keys, values, trailing, prefix_rows, live_row, total_rows)


def body(
    hidden_in,
    norm_gain,
    w_qkv,
    w_forget,
    forget_bias,
    cache_keys,
    cache_values,
    cache_forget,
    cache_lengths,
    piece_map,
    draft_counts,
):
    req_count, new_count, width = hidden_in.shape
    head_count = w_forget.shape[1]
    seq_count = lax.axis_size("seq")
    fsdp_count = lax.axis_size("fsdp")
    own_heads = w_qkv.shape[2]
    own_dims = w_qkv.shape[3]
    own_cols = 3 * own_heads * own_dims
    rows = req_count * new_count
    inner_width = head_count * HEAD_DIM
    piece_len = cache_forget.shape[2]
    logit_scale = HEAD_DIM ** (-0.5)
    seq_index = lax.axis_index("seq")
    head_start = seq_index * own_heads
    normed = normalize(hidden_in, norm_gain).reshape(rows, width)
    normed_all = lax.all_to_all(
        jnp.broadcast_to(normed[None], (fsdp_count, rows, width)), "fsdp", 0, 0, tiled=True
    ).reshape(fsdp_count * rows, width)
    projected = jnp.einsum(
        "dk,nd->kn",
        w_qkv.reshape(width, own_cols),
        normed_all,
        preferred_element_type=jnp.float32,
    ).astype(jnp.bfloat16)
    outgoing = (
        projected.reshape(3, own_heads * own_dims, fsdp_count, rows)
        .transpose(2, 1, 0, 3)
        .reshape(fsdp_count, 1, own_heads * own_dims * 3 * rows)
    )
    outgoing = jnp.broadcast_to(
        outgoing, (fsdp_count, seq_count, own_heads * own_dims * 3 * rows)
    ).reshape(fsdp_count * seq_count, 2, own_heads * own_dims * 3 * rows // 2)
    outgoing, cache_forget, normed = lax.optimization_barrier((outgoing, cache_forget, normed))
    incoming = lax.all_to_all(outgoing, ("fsdp", "seq"), 0, 0, tiled=True)
    incoming = incoming.reshape(fsdp_count * seq_count * own_heads * own_dims, 3 * rows)
    src_row = jnp.arange(fsdp_count * seq_count * own_heads * own_dims, dtype=jnp.int32)
    src_dev = src_row // (own_heads * own_dims)
    src_head = (src_row // own_dims) % own_heads
    src_dim = src_row % own_dims
    target = ((src_dev % seq_count) * own_heads + src_head) * HEAD_DIM + (
        src_dev // seq_count
    ) * own_dims + src_dim
    placement = (target[:, None] == jnp.arange(inner_width, dtype=jnp.int32)[None, :]).astype(
        jnp.bfloat16
    )
    all_heads = jnp.einsum(
        "kx,kj->xj", incoming, placement, preferred_element_type=jnp.float32
    ).astype(jnp.bfloat16).reshape(3, req_count, new_count, inner_width)
    gate_logit = (
        jnp.dot(normed, w_forget, preferred_element_type=jnp.float32).reshape(
            req_count, new_count, head_count
        )
        + forget_bias
    )
    prefix = jnp.cumsum(jax.nn.log_sigmoid(gate_logit), axis=1)
    slot_ids = jnp.arange(seq_count, dtype=jnp.int32)
    holders = piece_map[:, :, None] == slot_ids[None, None, :]
    piece_of_slot = jnp.sum(jnp.where(holders, slot_ids[None, :, None], 0), axis=1)
    own_piece = jnp.sum(jnp.where(piece_map == seq_index, slot_ids[None, :], 0), axis=1)
    steps = jnp.arange(piece_len, dtype=jnp.int32)
    positions = own_piece[:, None] * piece_len + steps[None, :]
    live_mask = positions < cache_lengths[:, None]
    masked = jnp.where(live_mask[:, None, :], cache_forget, 0.0)
    piece_total = jnp.sum(masked, axis=-1)
    later_step = (steps[:, None] > steps[None, :]).astype(jnp.float32)
    trailing_part = jnp.einsum(
        "rhl,lj->rhj", masked, later_step, precision=lax.Precision.HIGHEST,
        preferred_element_type=jnp.float32,
    )
    step_rows = 8
    pad_steps = ((0, 0), (0, step_rows - new_count))
    query_rows = jnp.pad(all_heads[0], pad_steps + ((0, 0),))
    prefix_rows = jnp.pad(jnp.transpose(prefix, (0, 2, 1)), ((0, 0),) + pad_steps).reshape(
        req_count, head_count * step_rows, 1
    )
    live_row = live_mask.astype(jnp.float32)[:, None, :]
    total_rows = jnp.broadcast_to(
        piece_total[:, :, None], (req_count, head_count, step_rows)
    ).reshape(req_count, head_count * step_rows, 1)
    packed = piece_attention(
        query_rows, cache_keys, cache_values, trailing_part, prefix_rows, live_row, total_rows, seq_count
    )
    parts = lax.all_to_all(packed, "seq", 0, 0, tiled=True)[:, :, :, :new_count]
    part_acc = parts[..., :HEAD_DIM]
    part_max = parts[..., HEAD_DIM]
    part_sum = parts[..., HEAD_DIM + 1]
    part_total = parts[:, :, :, 0, HEAD_DIM + 2]
    later_piece = (piece_of_slot.T[None, :, :] > piece_of_slot.T[:, None, :])[..., None]
    later_sum = jnp.sum(jnp.where(later_piece, part_total[None], 0.0), axis=1)
    part_max = part_max + later_sum[..., None]
    cache_max = jnp.max(part_max, axis=0)
    factor = jnp.exp(part_max - cache_max[None])
    cache_sum = jnp.sum(part_sum * factor, axis=0)
    cache_acc = jnp.sum(part_acc * factor[..., None], axis=0)
    own_rows = lax.dynamic_slice_in_dim(
        all_heads, head_start * HEAD_DIM, own_heads * HEAD_DIM, 3
    ).reshape(3, req_count, new_count, own_heads, HEAD_DIM)
    own_prefix = jnp.transpose(
        lax.dynamic_slice_in_dim(prefix, head_start, own_heads, 2), (0, 2, 1)
    )
    fresh_logits = (
        jnp.einsum(
            "rmhd,rnhd->rhmn",
            own_rows[0],
            own_rows[1],
            preferred_element_type=jnp.float32,
        )
        * logit_scale
    )
    fresh_logits = fresh_logits + own_prefix[..., :, None] - own_prefix[..., None, :]
    step_ids = jnp.arange(new_count, dtype=jnp.int32)
    causal = (step_ids[None, :] <= step_ids[:, None])[None, None]
    joint_max = jnp.maximum(cache_max, jnp.max(jnp.where(causal, fresh_logits, neg_fill), axis=-1))
    new_weights = jnp.where(causal, jnp.exp(fresh_logits - joint_max[..., None]), 0.0)
    carried = jnp.exp(cache_max - joint_max)
    total_sum = cache_sum * carried + jnp.sum(new_weights, axis=-1)
    blend_weights = cache_acc * carried[..., None] + jnp.einsum(
        "rhmn,rnhd->rhmd",
        new_weights.astype(jnp.bfloat16),
        own_rows[2],
        preferred_element_type=jnp.float32,
    )
    result = blend_weights / total_sum[..., None]
    live_rows = (step_ids[None, :] <= draft_counts[:, None])[:, None, :, None]
    result = jnp.where(live_rows, result, 0.0)
    return (
        jnp.transpose(result, (0, 2, 1, 3))
        .reshape(req_count, new_count, own_heads * HEAD_DIM)
        .astype(jnp.bfloat16)
    )


def solution(mesh):
    in_specs = (
        P("fsdp", None, None),
        P(),
        P(None, None, "seq", "fsdp"),
        P(),
        P(),
        P("fsdp", "seq", None),
        P("fsdp", "seq", None),
        P("fsdp", None, "seq"),
        P("fsdp"),
        P("fsdp", None),
        P("fsdp"),
    )
    out_specs = P("fsdp", None, "seq")
    return jax.shard_map(body, mesh=mesh, in_specs=in_specs, out_specs=out_specs, check_vma=False)
```

```python
import jax
import jax.numpy as jnp
from jax import lax
from jax.experimental import pallas as pl
from jax.experimental.pallas import tpu as pltpu
from jax.sharding import PartitionSpec as P

HEAD_DIM = 64


norm_eps = 1e-06
neg_fill = -1e30


def normalize(rows, gain):
    values = rows.astype(jnp.float32)
    mean_sq = jnp.mean(values * values, axis=-1, keepdims=True)
    return (values * lax.rsqrt(mean_sq + norm_eps) * gain).astype(jnp.bfloat16)


def attention_kernel(q_ref, k_ref, v_ref, trail_ref, prefix_ref, live_ref, total_ref, out_ref):
    step_rows = q_ref.shape[1]
    head_count = trail_ref.shape[1]
    piece_len = trail_ref.shape[2]
    inner_width = q_ref.shape[2]
    row_count = head_count * step_rows
    pair_count = inner_width // 128
    row_step = lax.broadcasted_iota(jnp.int32, (row_count, step_rows), 0) % step_rows
    spread = (row_step == lax.broadcasted_iota(jnp.int32, (row_count, step_rows), 1)).astype(jnp.bfloat16)
    repeated = jnp.dot(spread, q_ref[0], preferred_element_type=jnp.float32)
    row_head = lax.broadcasted_iota(jnp.int32, (row_count, inner_width), 0) // step_rows
    col_head = lax.broadcasted_iota(jnp.int32, (row_count, inner_width), 1) // HEAD_DIM
    query_blocks = jnp.where(row_head == col_head, repeated, 0.0).astype(jnp.bfloat16)
    scores = lax.dot_general(
        query_blocks, k_ref[0], (((1,), (1,)), ((), ())), preferred_element_type=jnp.float32
    )
    trailing = jnp.broadcast_to(
        trail_ref[0][:, None, :], (head_count, step_rows, piece_len)
    ).reshape(row_count, piece_len)
    scores = scores * (HEAD_DIM ** (-0.5)) + (trailing + prefix_ref[0])
    live = live_ref[0] > 0.5
    row_max = jnp.max(jnp.where(live, scores, neg_fill), axis=1, keepdims=True)
    weights = jnp.where(live, jnp.exp(scores - row_max), 0.0)
    weight_sum = jnp.sum(weights, axis=1, keepdims=True)
    blocks = jnp.dot(weights.astype(jnp.bfloat16), v_ref[0], preferred_element_type=jnp.float32)
    row = lax.broadcasted_iota(jnp.int32, (row_count, 128), 0)
    picked = jnp.zeros((row_count, 128), jnp.float32)
    for pair in range(pair_count):
        lo = 2 * pair * step_rows
        picked = jnp.where(
            (row >= lo) & (row < lo + 2 * step_rows), blocks[:, pair * 128 : (pair + 1) * 128], picked
        )
    odd = (row // step_rows) % 2 == 1
    accum = jnp.where(odd, pltpu.roll(picked, 64, 1), picked)
    lane = lax.broadcasted_iota(jnp.int32, (row_count, 128), 1)
    packed = jnp.where(lane < HEAD_DIM, accum, 0.0)
    packed = jnp.where(lane == HEAD_DIM, row_max, packed)
    packed = jnp.where(lane == HEAD_DIM + 1, weight_sum, packed)
    packed = jnp.where(lane == HEAD_DIM + 2, total_ref[0], packed)
    own_heads = out_ref.shape[2]
    for head in range(head_count):
        out_ref[head // own_heads, 0, head % own_heads] = packed[head * step_rows : (head + 1) * step_rows]


def piece_attention(query_rows, keys, values, trailing, prefix_rows, live_row, total_rows, seq_count):
    req_count, step_rows, inner_width = query_rows.shape
    head_count = trailing.shape[1]
    piece_len = keys.shape[1]
    row_count = head_count * step_rows
    own_heads = head_count // seq_count
    return pl.pallas_call(
        attention_kernel,
        grid=(req_count,),
        in_specs=[
            pl.BlockSpec((1, step_rows, inner_width), lambda r: (r, 0, 0)),
            pl.BlockSpec((1, piece_len, inner_width), lambda r: (r, 0, 0)),
            pl.BlockSpec((1, piece_len, inner_width), lambda r: (r, 0, 0)),
            pl.BlockSpec((1, head_count, piece_len), lambda r: (r, 0, 0)),
            pl.BlockSpec((1, row_count, 1), lambda r: (r, 0, 0)),
            pl.BlockSpec((1, 1, piece_len), lambda r: (r, 0, 0)),
            pl.BlockSpec((1, row_count, 1), lambda r: (r, 0, 0)),
        ],
        out_specs=pl.BlockSpec((seq_count, 1, own_heads, step_rows, 128), lambda r: (0, r, 0, 0, 0)),
        out_shape=jax.ShapeDtypeStruct((seq_count, req_count, own_heads, step_rows, 128), jnp.float32),
    )(query_rows, keys, values, trailing, prefix_rows, live_row, total_rows)


def body(
    hidden_in,
    norm_gain,
    w_qkv,
    w_forget,
    forget_bias,
    cache_keys,
    cache_values,
    cache_forget,
    cache_lengths,
    piece_map,
    draft_counts,
):
    req_count, new_count, width = hidden_in.shape
    head_count = w_forget.shape[1]
    seq_count = lax.axis_size("seq")
    fsdp_count = lax.axis_size("fsdp")
    own_heads = w_qkv.shape[2]
    own_dims = w_qkv.shape[3]
    own_cols = 3 * own_heads * own_dims
    rows = req_count * new_count
    inner_width = head_count * HEAD_DIM
    piece_len = cache_forget.shape[2]
    logit_scale = HEAD_DIM ** (-0.5)
    seq_index = lax.axis_index("seq")
    head_start = seq_index * own_heads
    hidden_rows = hidden_in.reshape(rows, width)
    hidden_all = lax.all_to_all(
        jnp.broadcast_to(hidden_rows[None], (fsdp_count, rows, width)), "fsdp", 0, 0, tiled=True
    )
    normed_all = normalize(hidden_all, norm_gain).reshape(fsdp_count * rows, width)
    normed = normalize(hidden_rows, norm_gain)
    projected = jnp.einsum(
        "dk,nd->kn",
        w_qkv.reshape(width, own_cols),
        normed_all,
        preferred_element_type=jnp.float32,
    ).astype(jnp.bfloat16)
    outgoing = (
        projected.reshape(3, own_heads * own_dims, fsdp_count, rows)
        .transpose(2, 1, 0, 3)
        .reshape(fsdp_count, 1, own_heads * own_dims * 3 * rows)
    )
    outgoing = jnp.broadcast_to(
        outgoing, (fsdp_count, seq_count, own_heads * own_dims * 3 * rows)
    ).reshape(fsdp_count * seq_count, 2, own_heads * own_dims * 3 * rows // 2)
    incoming = lax.all_to_all(outgoing, ("fsdp", "seq"), 0, 0, tiled=True)
    incoming = incoming.reshape(fsdp_count * seq_count * own_heads * own_dims, 3 * rows)
    src_row = jnp.arange(fsdp_count * seq_count * own_heads * own_dims, dtype=jnp.int32)
    src_dev = src_row // (own_heads * own_dims)
    src_head = (src_row // own_dims) % own_heads
    src_dim = src_row % own_dims
    target = ((src_dev % seq_count) * own_heads + src_head) * HEAD_DIM + (
        src_dev // seq_count
    ) * own_dims + src_dim
    placement = (target[:, None] == jnp.arange(inner_width, dtype=jnp.int32)[None, :]).astype(
        jnp.bfloat16
    )
    all_heads = jnp.einsum(
        "kx,kj->xj", incoming, placement, preferred_element_type=jnp.float32
    ).astype(jnp.bfloat16).reshape(3, req_count, new_count, inner_width)
    gate_logit = (
        jnp.dot(normed, w_forget, preferred_element_type=jnp.float32).reshape(
            req_count, new_count, head_count
        )
        + forget_bias
    )
    prefix = jnp.cumsum(jax.nn.log_sigmoid(gate_logit), axis=1)
    slot_ids = jnp.arange(seq_count, dtype=jnp.int32)
    holders = piece_map[:, :, None] == slot_ids[None, None, :]
    piece_of_slot = jnp.sum(jnp.where(holders, slot_ids[None, :, None], 0), axis=1)
    own_piece = jnp.sum(jnp.where(piece_map == seq_index, slot_ids[None, :], 0), axis=1)
    steps = jnp.arange(piece_len, dtype=jnp.int32)
    positions = own_piece[:, None] * piece_len + steps[None, :]
    live_mask = positions < cache_lengths[:, None]
    masked = jnp.where(live_mask[:, None, :], cache_forget, 0.0)
    piece_total = jnp.sum(masked, axis=-1)
    later_step = (steps[:, None] > steps[None, :]).astype(jnp.float32)
    trailing_part = jnp.einsum(
        "rhl,lj->rhj", masked, later_step, precision=lax.Precision.HIGHEST,
        preferred_element_type=jnp.float32,
    )
    step_rows = 8
    pad_steps = ((0, 0), (0, step_rows - new_count))
    query_rows = jnp.pad(all_heads[0], pad_steps + ((0, 0),))
    prefix_rows = jnp.pad(jnp.transpose(prefix, (0, 2, 1)), ((0, 0),) + pad_steps).reshape(
        req_count, head_count * step_rows, 1
    )
    live_row = live_mask.astype(jnp.float32)[:, None, :]
    total_rows = jnp.broadcast_to(
        piece_total[:, :, None], (req_count, head_count, step_rows)
    ).reshape(req_count, head_count * step_rows, 1)
    packed = piece_attention(
        query_rows, cache_keys, cache_values, trailing_part, prefix_rows, live_row, total_rows, seq_count
    )
    parts = lax.all_to_all(packed, "seq", 0, 0, tiled=True)[:, :, :, :new_count]
    part_acc = parts[..., :HEAD_DIM]
    part_max = parts[..., HEAD_DIM]
    part_sum = parts[..., HEAD_DIM + 1]
    part_total = parts[:, :, :, 0, HEAD_DIM + 2]
    later_piece = (piece_of_slot.T[None, :, :] > piece_of_slot.T[:, None, :])[..., None]
    later_sum = jnp.sum(jnp.where(later_piece, part_total[None], 0.0), axis=1)
    part_max = part_max + later_sum[..., None]
    cache_max = jnp.max(part_max, axis=0)
    factor = jnp.exp(part_max - cache_max[None])
    cache_sum = jnp.sum(part_sum * factor, axis=0)
    cache_acc = jnp.sum(part_acc * factor[..., None], axis=0)
    own_rows = lax.dynamic_slice_in_dim(
        all_heads, head_start * HEAD_DIM, own_heads * HEAD_DIM, 3
    ).reshape(3, req_count, new_count, own_heads, HEAD_DIM)
    own_prefix = jnp.transpose(
        lax.dynamic_slice_in_dim(prefix, head_start, own_heads, 2), (0, 2, 1)
    )
    fresh_logits = (
        jnp.einsum(
            "rmhd,rnhd->rhmn",
            own_rows[0],
            own_rows[1],
            preferred_element_type=jnp.float32,
        )
        * logit_scale
    )
    fresh_logits = fresh_logits + own_prefix[..., :, None] - own_prefix[..., None, :]
    step_ids = jnp.arange(new_count, dtype=jnp.int32)
    causal = (step_ids[None, :] <= step_ids[:, None])[None, None]
    joint_max = jnp.maximum(cache_max, jnp.max(jnp.where(causal, fresh_logits, neg_fill), axis=-1))
    new_weights = jnp.where(causal, jnp.exp(fresh_logits - joint_max[..., None]), 0.0)
    carried = jnp.exp(cache_max - joint_max)
    total_sum = cache_sum * carried + jnp.sum(new_weights, axis=-1)
    blend_weights = cache_acc * carried[..., None] + jnp.einsum(
        "rhmn,rnhd->rhmd",
        new_weights.astype(jnp.bfloat16),
        own_rows[2],
        preferred_element_type=jnp.float32,
    )
    result = blend_weights / total_sum[..., None]
    live_rows = (step_ids[None, :] <= draft_counts[:, None])[:, None, :, None]
    result = jnp.where(live_rows, result, 0.0)
    return (
        jnp.transpose(result, (0, 2, 1, 3))
        .reshape(req_count, new_count, own_heads * HEAD_DIM)
        .astype(jnp.bfloat16)
    )


def solution(mesh):
    in_specs = (
        P("fsdp", None, None),
        P(),
        P(None, None, "seq", "fsdp"),
        P(),
        P(),
        P("fsdp", "seq", None),
        P("fsdp", "seq", None),
        P("fsdp", None, "seq"),
        P("fsdp"),
        P("fsdp", None),
        P("fsdp"),
    )
    out_specs = P("fsdp", None, "seq")
    return jax.shard_map(body, mesh=mesh, in_specs=in_specs, out_specs=out_specs, check_vma=False)
```

```python
import jax
import jax.numpy as jnp
from jax import lax
from jax.experimental import pallas as pl
from jax.experimental.pallas import tpu as pltpu
from jax.sharding import PartitionSpec as P

HEAD_DIM = 64


norm_eps = 1e-06
neg_fill = -1e30


def normalize(rows, gain):
    values = rows.astype(jnp.float32)
    mean_sq = jnp.mean(values * values, axis=-1, keepdims=True)
    return (values * lax.rsqrt(mean_sq + norm_eps) * gain).astype(jnp.bfloat16)


def attention_kernel(q_ref, k_ref, v_ref, trail_ref, prefix_ref, live_ref, total_ref, out_ref):
    step_rows = q_ref.shape[1]
    head_count = trail_ref.shape[1]
    piece_len = trail_ref.shape[2]
    inner_width = q_ref.shape[2]
    row_count = head_count * step_rows
    pair_count = inner_width // 128
    row_step = lax.broadcasted_iota(jnp.int32, (row_count, step_rows), 0) % step_rows
    spread = (row_step == lax.broadcasted_iota(jnp.int32, (row_count, step_rows), 1)).astype(jnp.bfloat16)
    repeated = jnp.dot(spread, q_ref[0], preferred_element_type=jnp.float32)
    row_head = lax.broadcasted_iota(jnp.int32, (row_count, inner_width), 0) // step_rows
    col_head = lax.broadcasted_iota(jnp.int32, (row_count, inner_width), 1) // HEAD_DIM
    query_blocks = jnp.where(row_head == col_head, repeated, 0.0).astype(jnp.bfloat16)
    scores = lax.dot_general(
        query_blocks, k_ref[0], (((1,), (1,)), ((), ())), preferred_element_type=jnp.float32
    )
    trailing = jnp.broadcast_to(
        trail_ref[0][:, None, :], (head_count, step_rows, piece_len)
    ).reshape(row_count, piece_len)
    scores = scores * (HEAD_DIM ** (-0.5)) + (trailing + prefix_ref[0])
    live = live_ref[0] > 0.5
    row_max = jnp.max(jnp.where(live, scores, neg_fill), axis=1, keepdims=True)
    weights = jnp.where(live, jnp.exp(scores - row_max), 0.0)
    weight_sum = jnp.sum(weights, axis=1, keepdims=True)
    blocks = jnp.dot(weights.astype(jnp.bfloat16), v_ref[0], preferred_element_type=jnp.float32)
    row = lax.broadcasted_iota(jnp.int32, (row_count, 128), 0)
    picked = jnp.zeros((row_count, 128), jnp.float32)
    for pair in range(pair_count):
        lo = 2 * pair * step_rows
        picked = jnp.where(
            (row >= lo) & (row < lo + 2 * step_rows), blocks[:, pair * 128 : (pair + 1) * 128], picked
        )
    odd = (row // step_rows) % 2 == 1
    accum = jnp.where(odd, pltpu.roll(picked, 64, 1), picked)
    lane = lax.broadcasted_iota(jnp.int32, (row_count, 128), 1)
    packed = jnp.where(lane < HEAD_DIM, accum, 0.0)
    packed = jnp.where(lane == HEAD_DIM, row_max, packed)
    packed = jnp.where(lane == HEAD_DIM + 1, weight_sum, packed)
    packed = jnp.where(lane == HEAD_DIM + 2, total_ref[0], packed)
    own_heads = out_ref.shape[2]
    for head in range(head_count):
        out_ref[head // own_heads, 0, head % own_heads] = packed[head * step_rows : (head + 1) * step_rows]


def piece_attention(query_rows, keys, values, trailing, prefix_rows, live_row, total_rows, seq_count):
    req_count, step_rows, inner_width = query_rows.shape
    head_count = trailing.shape[1]
    piece_len = keys.shape[1]
    row_count = head_count * step_rows
    own_heads = head_count // seq_count
    return pl.pallas_call(
        attention_kernel,
        grid=(req_count,),
        in_specs=[
            pl.BlockSpec((1, step_rows, inner_width), lambda r: (r, 0, 0)),
            pl.BlockSpec((1, piece_len, inner_width), lambda r: (r, 0, 0)),
            pl.BlockSpec((1, piece_len, inner_width), lambda r: (r, 0, 0)),
            pl.BlockSpec((1, head_count, piece_len), lambda r: (r, 0, 0)),
            pl.BlockSpec((1, row_count, 1), lambda r: (r, 0, 0)),
            pl.BlockSpec((1, 1, piece_len), lambda r: (r, 0, 0)),
            pl.BlockSpec((1, row_count, 1), lambda r: (r, 0, 0)),
        ],
        out_specs=pl.BlockSpec((seq_count, 1, own_heads, step_rows, 128), lambda r: (0, r, 0, 0, 0)),
        out_shape=jax.ShapeDtypeStruct((seq_count, req_count, own_heads, step_rows, 128), jnp.float32),
    )(query_rows, keys, values, trailing, prefix_rows, live_row, total_rows)


def body(
    hidden_in,
    norm_gain,
    w_qkv,
    w_forget,
    forget_bias,
    cache_keys,
    cache_values,
    cache_forget,
    cache_lengths,
    piece_map,
    draft_counts,
):
    req_count, new_count, width = hidden_in.shape
    head_count = w_forget.shape[1]
    seq_count = lax.axis_size("seq")
    fsdp_count = lax.axis_size("fsdp")
    own_heads = w_qkv.shape[2]
    own_dims = w_qkv.shape[3]
    own_cols = 3 * own_heads * own_dims
    rows = req_count * new_count
    inner_width = head_count * HEAD_DIM
    piece_len = cache_forget.shape[2]
    logit_scale = HEAD_DIM ** (-0.5)
    seq_index = lax.axis_index("seq")
    head_start = seq_index * own_heads
    hidden_all = lax.all_to_all(
        jnp.broadcast_to(hidden_in[None], (fsdp_count, req_count, new_count, width)),
        "fsdp",
        0,
        0,
        tiled=True,
    )
    normed_all = normalize(hidden_all, norm_gain).reshape(fsdp_count * rows, width)
    normed = normalize(hidden_in, norm_gain).reshape(rows, width)
    projected = jnp.einsum(
        "dk,nd->kn",
        w_qkv.reshape(width, own_cols),
        normed_all,
        preferred_element_type=jnp.float32,
    ).astype(jnp.bfloat16)
    outgoing = (
        projected.reshape(3, own_heads * own_dims, fsdp_count, rows)
        .transpose(2, 1, 0, 3)
        .reshape(fsdp_count, 1, own_heads * own_dims * 3 * rows)
    )
    outgoing = jnp.broadcast_to(
        outgoing, (fsdp_count, seq_count, own_heads * own_dims * 3 * rows)
    ).reshape(fsdp_count * seq_count, 2, own_heads * own_dims * 3 * rows // 2)
    incoming = lax.all_to_all(outgoing, ("fsdp", "seq"), 0, 0, tiled=True)
    incoming = incoming.reshape(fsdp_count * seq_count * own_heads * own_dims, 3 * rows)
    src_row = jnp.arange(fsdp_count * seq_count * own_heads * own_dims, dtype=jnp.int32)
    src_dev = src_row // (own_heads * own_dims)
    src_head = (src_row // own_dims) % own_heads
    src_dim = src_row % own_dims
    target = ((src_dev % seq_count) * own_heads + src_head) * HEAD_DIM + (
        src_dev // seq_count
    ) * own_dims + src_dim
    placement = (target[:, None] == jnp.arange(inner_width, dtype=jnp.int32)[None, :]).astype(
        jnp.bfloat16
    )
    all_heads = jnp.einsum(
        "kx,kj->xj", incoming, placement, preferred_element_type=jnp.float32
    ).astype(jnp.bfloat16).reshape(3, req_count, new_count, inner_width)
    gate_logit = (
        jnp.dot(normed, w_forget, preferred_element_type=jnp.float32).reshape(
            req_count, new_count, head_count
        )
        + forget_bias
    )
    prefix = jnp.cumsum(jax.nn.log_sigmoid(gate_logit), axis=1)
    slot_ids = jnp.arange(seq_count, dtype=jnp.int32)
    holders = piece_map[:, :, None] == slot_ids[None, None, :]
    piece_of_slot = jnp.sum(jnp.where(holders, slot_ids[None, :, None], 0), axis=1)
    own_piece = jnp.sum(jnp.where(piece_map == seq_index, slot_ids[None, :], 0), axis=1)
    steps = jnp.arange(piece_len, dtype=jnp.int32)
    positions = own_piece[:, None] * piece_len + steps[None, :]
    live_mask = positions < cache_lengths[:, None]
    masked = jnp.where(live_mask[:, None, :], cache_forget, 0.0)
    piece_total = jnp.sum(masked, axis=-1)
    later_step = (steps[:, None] > steps[None, :]).astype(jnp.float32)
    trailing_part = jnp.einsum(
        "rhl,lj->rhj", masked, later_step, precision=lax.Precision.HIGHEST,
        preferred_element_type=jnp.float32,
    )
    step_rows = 8
    pad_steps = ((0, 0), (0, step_rows - new_count))
    query_rows = jnp.pad(all_heads[0], pad_steps + ((0, 0),))
    prefix_rows = jnp.pad(jnp.transpose(prefix, (0, 2, 1)), ((0, 0),) + pad_steps).reshape(
        req_count, head_count * step_rows, 1
    )
    live_row = live_mask.astype(jnp.float32)[:, None, :]
    total_rows = jnp.broadcast_to(
        piece_total[:, :, None], (req_count, head_count, step_rows)
    ).reshape(req_count, head_count * step_rows, 1)
    packed = piece_attention(
        query_rows, cache_keys, cache_values, trailing_part, prefix_rows, live_row, total_rows, seq_count
    )
    parts = lax.all_to_all(packed, "seq", 0, 0, tiled=True)[:, :, :, :new_count]
    part_acc = parts[..., :HEAD_DIM]
    part_max = parts[..., HEAD_DIM]
    part_sum = parts[..., HEAD_DIM + 1]
    part_total = parts[:, :, :, 0, HEAD_DIM + 2]
    later_piece = (piece_of_slot.T[None, :, :] > piece_of_slot.T[:, None, :])[..., None]
    later_sum = jnp.sum(jnp.where(later_piece, part_total[None], 0.0), axis=1)
    part_max = part_max + later_sum[..., None]
    cache_max = jnp.max(part_max, axis=0)
    factor = jnp.exp(part_max - cache_max[None])
    cache_sum = jnp.sum(part_sum * factor, axis=0)
    cache_acc = jnp.sum(part_acc * factor[..., None], axis=0)
    own_rows = lax.dynamic_slice_in_dim(
        all_heads, head_start * HEAD_DIM, own_heads * HEAD_DIM, 3
    ).reshape(3, req_count, new_count, own_heads, HEAD_DIM)
    own_prefix = jnp.transpose(
        lax.dynamic_slice_in_dim(prefix, head_start, own_heads, 2), (0, 2, 1)
    )
    fresh_logits = (
        jnp.einsum(
            "rmhd,rnhd->rhmn",
            own_rows[0],
            own_rows[1],
            preferred_element_type=jnp.float32,
        )
        * logit_scale
    )
    fresh_logits = fresh_logits + own_prefix[..., :, None] - own_prefix[..., None, :]
    step_ids = jnp.arange(new_count, dtype=jnp.int32)
    causal = (step_ids[None, :] <= step_ids[:, None])[None, None]
    joint_max = jnp.maximum(cache_max, jnp.max(jnp.where(causal, fresh_logits, neg_fill), axis=-1))
    new_weights = jnp.where(causal, jnp.exp(fresh_logits - joint_max[..., None]), 0.0)
    carried = jnp.exp(cache_max - joint_max)
    total_sum = cache_sum * carried + jnp.sum(new_weights, axis=-1)
    blend_weights = cache_acc * carried[..., None] + jnp.einsum(
        "rhmn,rnhd->rhmd",
        new_weights.astype(jnp.bfloat16),
        own_rows[2],
        preferred_element_type=jnp.float32,
    )
    result = blend_weights / total_sum[..., None]
    live_rows = (step_ids[None, :] <= draft_counts[:, None])[:, None, :, None]
    result = jnp.where(live_rows, result, 0.0)
    return (
        jnp.transpose(result, (0, 2, 1, 3))
        .reshape(req_count, new_count, own_heads * HEAD_DIM)
        .astype(jnp.bfloat16)
    )


def solution(mesh):
    in_specs = (
        P("fsdp", None, None),
        P(),
        P(None, None, "seq", "fsdp"),
        P(),
        P(),
        P("fsdp", "seq", None),
        P("fsdp", "seq", None),
        P("fsdp", None, "seq"),
        P("fsdp"),
        P("fsdp", None),
        P("fsdp"),
    )
    out_specs = P("fsdp", None, "seq")
    return jax.shard_map(body, mesh=mesh, in_specs=in_specs, out_specs=out_specs, check_vma=False)
```

```python
import jax
import jax.numpy as jnp
from jax import lax
from jax.experimental import pallas as pl
from jax.experimental.pallas import tpu as pltpu
from jax.sharding import PartitionSpec as P

HEAD_DIM = 64


norm_eps = 1e-06
neg_fill = -1e30


def normalize(rows, gain):
    values = rows.astype(jnp.float32)
    mean_sq = jnp.mean(values * values, axis=-1, keepdims=True)
    return (values * lax.rsqrt(mean_sq + norm_eps) * gain).astype(jnp.bfloat16)


def attention_kernel(q_ref, k_ref, v_ref, trail_ref, prefix_ref, live_ref, total_ref, out_ref):
    step_rows = q_ref.shape[1]
    head_count = trail_ref.shape[1]
    piece_len = trail_ref.shape[2]
    inner_width = q_ref.shape[2]
    row_count = head_count * step_rows
    pair_count = inner_width // 128
    row_step = lax.broadcasted_iota(jnp.int32, (row_count, step_rows), 0) % step_rows
    spread = (row_step == lax.broadcasted_iota(jnp.int32, (row_count, step_rows), 1)).astype(jnp.bfloat16)
    repeated = jnp.dot(spread, q_ref[0], preferred_element_type=jnp.float32)
    row_head = lax.broadcasted_iota(jnp.int32, (row_count, inner_width), 0) // step_rows
    col_head = lax.broadcasted_iota(jnp.int32, (row_count, inner_width), 1) // HEAD_DIM
    query_blocks = jnp.where(row_head == col_head, repeated, 0.0).astype(jnp.bfloat16)
    scores = lax.dot_general(
        query_blocks, k_ref[0], (((1,), (1,)), ((), ())), preferred_element_type=jnp.float32
    )
    trailing = jnp.broadcast_to(
        trail_ref[0][:, None, :], (head_count, step_rows, piece_len)
    ).reshape(row_count, piece_len)
    scores = scores * (HEAD_DIM ** (-0.5)) + (trailing + prefix_ref[0])
    live = live_ref[0] > 0.5
    row_max = jnp.max(jnp.where(live, scores, neg_fill), axis=1, keepdims=True)
    weights = jnp.where(live, jnp.exp(scores - row_max), 0.0)
    weight_sum = jnp.sum(weights, axis=1, keepdims=True)
    blocks = jnp.dot(weights.astype(jnp.bfloat16), v_ref[0], preferred_element_type=jnp.float32)
    row = lax.broadcasted_iota(jnp.int32, (row_count, 128), 0)
    picked = jnp.zeros((row_count, 128), jnp.float32)
    for pair in range(pair_count):
        lo = 2 * pair * step_rows
        picked = jnp.where(
            (row >= lo) & (row < lo + 2 * step_rows), blocks[:, pair * 128 : (pair + 1) * 128], picked
        )
    odd = (row // step_rows) % 2 == 1
    accum = jnp.where(odd, pltpu.roll(picked, 64, 1), picked)
    lane = lax.broadcasted_iota(jnp.int32, (row_count, 128), 1)
    packed = jnp.where(lane < HEAD_DIM, accum, 0.0)
    packed = jnp.where(lane == HEAD_DIM, row_max, packed)
    packed = jnp.where(lane == HEAD_DIM + 1, weight_sum, packed)
    packed = jnp.where(lane == HEAD_DIM + 2, total_ref[0], packed)
    own_heads = out_ref.shape[2]
    for head in range(head_count):
        out_ref[head // own_heads, 0, head % own_heads] = packed[head * step_rows : (head + 1) * step_rows]


def piece_attention(query_rows, keys, values, trailing, prefix_rows, live_row, total_rows, seq_count):
    req_count, step_rows, inner_width = query_rows.shape
    head_count = trailing.shape[1]
    piece_len = keys.shape[1]
    row_count = head_count * step_rows
    own_heads = head_count // seq_count
    return pl.pallas_call(
        attention_kernel,
        grid=(req_count,),
        in_specs=[
            pl.BlockSpec((1, step_rows, inner_width), lambda r: (r, 0, 0)),
            pl.BlockSpec((1, piece_len, inner_width), lambda r: (r, 0, 0)),
            pl.BlockSpec((1, piece_len, inner_width), lambda r: (r, 0, 0)),
            pl.BlockSpec((1, head_count, piece_len), lambda r: (r, 0, 0)),
            pl.BlockSpec((1, row_count, 1), lambda r: (r, 0, 0)),
            pl.BlockSpec((1, 1, piece_len), lambda r: (r, 0, 0)),
            pl.BlockSpec((1, row_count, 1), lambda r: (r, 0, 0)),
        ],
        out_specs=pl.BlockSpec((seq_count, 1, own_heads, step_rows, 128), lambda r: (0, r, 0, 0, 0)),
        out_shape=jax.ShapeDtypeStruct((seq_count, req_count, own_heads, step_rows, 128), jnp.float32),
    )(query_rows, keys, values, trailing, prefix_rows, live_row, total_rows)


def body(
    hidden_in,
    norm_gain,
    w_qkv,
    w_forget,
    forget_bias,
    cache_keys,
    cache_values,
    cache_forget,
    cache_lengths,
    piece_map,
    draft_counts,
):
    req_count, new_count, width = hidden_in.shape
    head_count = w_forget.shape[1]
    seq_count = lax.axis_size("seq")
    fsdp_count = lax.axis_size("fsdp")
    own_heads = w_qkv.shape[2]
    own_dims = w_qkv.shape[3]
    own_cols = 3 * own_heads * own_dims
    rows = req_count * new_count
    inner_width = head_count * HEAD_DIM
    piece_len = cache_forget.shape[2]
    logit_scale = HEAD_DIM ** (-0.5)
    seq_index = lax.axis_index("seq")
    head_start = seq_index * own_heads
    hidden_all = lax.all_to_all(
        jnp.broadcast_to(hidden_in[None], (fsdp_count, req_count, new_count, width)),
        "fsdp",
        0,
        0,
        tiled=True,
    )
    normed_all = normalize(hidden_all, norm_gain).reshape(fsdp_count * rows, width)
    normed = normalize(hidden_in, norm_gain).reshape(rows, width)
    projected = jnp.einsum(
        "dk,nd->kn",
        w_qkv.reshape(width, own_cols),
        normed_all,
        preferred_element_type=jnp.float32,
    ).astype(jnp.bfloat16)
    outgoing = (
        projected.reshape(3, own_heads * own_dims, fsdp_count, rows)
        .transpose(2, 1, 0, 3)
        .reshape(fsdp_count, 1, own_heads * own_dims * 3 * rows)
    )
    outgoing = jnp.broadcast_to(
        outgoing, (fsdp_count, seq_count, own_heads * own_dims * 3 * rows)
    ).reshape(fsdp_count * seq_count, 2, own_heads * own_dims * 3 * rows // 2)
    incoming = lax.all_to_all(outgoing, ("fsdp", "seq"), 0, 0, tiled=True)
    incoming = incoming.reshape(fsdp_count * seq_count * own_heads * own_dims, 3 * rows)
    src_row = jnp.arange(fsdp_count * seq_count * own_heads * own_dims, dtype=jnp.int32)
    src_dev = src_row // (own_heads * own_dims)
    src_head = (src_row // own_dims) % own_heads
    src_dim = src_row % own_dims
    target = ((src_dev % seq_count) * own_heads + src_head) * HEAD_DIM + (
        src_dev // seq_count
    ) * own_dims + src_dim
    placement = (target[:, None] == jnp.arange(inner_width, dtype=jnp.int32)[None, :]).astype(
        jnp.bfloat16
    )
    all_heads = jnp.einsum(
        "kx,kj->xj", incoming, placement, preferred_element_type=jnp.float32
    ).astype(jnp.bfloat16).reshape(3, req_count, new_count, inner_width)
    gate_logit = (
        jnp.dot(normed, w_forget, preferred_element_type=jnp.float32).reshape(
            req_count, new_count, head_count
        )
        + forget_bias
    )
    prefix = jnp.cumsum(jax.nn.log_sigmoid(gate_logit), axis=1)
    slot_ids = jnp.arange(seq_count, dtype=jnp.int32)
    holders = piece_map[:, :, None] == slot_ids[None, None, :]
    piece_of_slot = jnp.sum(jnp.where(holders, slot_ids[None, :, None], 0), axis=1)
    own_piece = jnp.sum(jnp.where(piece_map == seq_index, slot_ids[None, :], 0), axis=1)
    steps = jnp.arange(piece_len, dtype=jnp.int32)
    positions = own_piece[:, None] * piece_len + steps[None, :]
    live_mask = positions < cache_lengths[:, None]
    masked = jnp.where(live_mask[:, None, :], cache_forget, 0.0)
    piece_total = jnp.sum(masked, axis=-1)
    later_step = (steps[:, None] > steps[None, :]).astype(jnp.float32)
    trailing_part = jnp.einsum(
        "rhl,lj->rhj", masked, later_step, precision=lax.Precision.HIGHEST,
        preferred_element_type=jnp.float32,
    )
    step_rows = 8
    pad_steps = ((0, 0), (0, step_rows - new_count))
    query_rows = jnp.pad(all_heads[0], pad_steps + ((0, 0),))
    prefix_rows = jnp.pad(jnp.transpose(prefix, (0, 2, 1)), ((0, 0),) + pad_steps).reshape(
        req_count, head_count * step_rows, 1
    )
    live_row = live_mask.astype(jnp.float32)[:, None, :]
    total_rows = jnp.broadcast_to(
        piece_total[:, :, None], (req_count, head_count, step_rows)
    ).reshape(req_count, head_count * step_rows, 1)
    packed = piece_attention(
        query_rows, cache_keys, cache_values, trailing_part, prefix_rows, live_row, total_rows, seq_count
    )
    own_rows = lax.dynamic_slice_in_dim(
        all_heads, head_start * HEAD_DIM, own_heads * HEAD_DIM, 3
    ).reshape(3, req_count, new_count, own_heads, HEAD_DIM)
    own_prefix = jnp.transpose(
        lax.dynamic_slice_in_dim(prefix, head_start, own_heads, 2), (0, 2, 1)
    )
    fresh_logits = (
        jnp.einsum(
            "rmhd,rnhd->rhmn",
            own_rows[0],
            own_rows[1],
            preferred_element_type=jnp.float32,
        )
        * logit_scale
    )
    fresh_logits = fresh_logits + own_prefix[..., :, None] - own_prefix[..., None, :]
    step_ids = jnp.arange(new_count, dtype=jnp.int32)
    causal = (step_ids[None, :] <= step_ids[:, None])[None, None]
    fresh_max = jnp.max(jnp.where(causal, fresh_logits, neg_fill), axis=-1)
    new_weights = jnp.where(causal, jnp.exp(fresh_logits - fresh_max[..., None]), 0.0)
    fresh_sum = jnp.sum(new_weights, axis=-1)
    fresh_acc = jnp.einsum(
        "rhmn,rnhd->rhmd",
        new_weights.astype(jnp.bfloat16),
        own_rows[2],
        preferred_element_type=jnp.float32,
    )
    parts = lax.all_to_all(packed, "seq", 0, 0, tiled=True)[:, :, :, :new_count]
    part_acc = parts[..., :HEAD_DIM]
    part_max = parts[..., HEAD_DIM]
    part_sum = parts[..., HEAD_DIM + 1]
    part_total = parts[:, :, :, 0, HEAD_DIM + 2]
    later_piece = (piece_of_slot.T[None, :, :] > piece_of_slot.T[:, None, :])[..., None]
    later_sum = jnp.sum(jnp.where(later_piece, part_total[None], 0.0), axis=1)
    part_max = part_max + later_sum[..., None]
    joint_max = jnp.maximum(jnp.max(part_max, axis=0), fresh_max)
    factor = jnp.exp(part_max - joint_max[None])
    carried = jnp.exp(fresh_max - joint_max)
    total_sum = jnp.sum(part_sum * factor, axis=0) + fresh_sum * carried
    blend_weights = jnp.sum(part_acc * factor[..., None], axis=0) + fresh_acc * carried[..., None]
    result = blend_weights / total_sum[..., None]
    live_rows = (step_ids[None, :] <= draft_counts[:, None])[:, None, :, None]
    result = jnp.where(live_rows, result, 0.0)
    return (
        jnp.transpose(result, (0, 2, 1, 3))
        .reshape(req_count, new_count, own_heads * HEAD_DIM)
        .astype(jnp.bfloat16)
    )


def solution(mesh):
    in_specs = (
        P("fsdp", None, None),
        P(),
        P(None, None, "seq", "fsdp"),
        P(),
        P(),
        P("fsdp", "seq", None),
        P("fsdp", "seq", None),
        P("fsdp", None, "seq"),
        P("fsdp"),
        P("fsdp", None),
        P("fsdp"),
    )
    out_specs = P("fsdp", None, "seq")
    return jax.shard_map(body, mesh=mesh, in_specs=in_specs, out_specs=out_specs, check_vma=False)
```

```python
import jax
import jax.numpy as jnp
from jax import lax
from jax.experimental import pallas as pl
from jax.experimental.pallas import tpu as pltpu
from jax.sharding import PartitionSpec as P

HEAD_DIM = 64


norm_eps = 1e-06
neg_fill = -1e30


def normalize(rows, gain):
    values = rows.astype(jnp.float32)
    mean_sq = jnp.mean(values * values, axis=-1, keepdims=True)
    return (values * lax.rsqrt(mean_sq + norm_eps) * gain).astype(jnp.bfloat16)


def attention_kernel(q_ref, k_ref, v_ref, trail_ref, prefix_ref, live_ref, total_ref, out_ref):
    step_rows = q_ref.shape[1]
    head_count = trail_ref.shape[1]
    piece_len = trail_ref.shape[2]
    inner_width = q_ref.shape[2]
    row_count = head_count * step_rows
    pair_count = inner_width // 128
    row_step = lax.broadcasted_iota(jnp.int32, (row_count, step_rows), 0) % step_rows
    spread = (row_step == lax.broadcasted_iota(jnp.int32, (row_count, step_rows), 1)).astype(jnp.bfloat16)
    repeated = jnp.dot(spread, q_ref[0], preferred_element_type=jnp.float32)
    row_head = lax.broadcasted_iota(jnp.int32, (row_count, inner_width), 0) // step_rows
    col_head = lax.broadcasted_iota(jnp.int32, (row_count, inner_width), 1) // HEAD_DIM
    query_blocks = jnp.where(row_head == col_head, repeated, 0.0).astype(jnp.bfloat16)
    scores = lax.dot_general(
        query_blocks, k_ref[0], (((1,), (1,)), ((), ())), preferred_element_type=jnp.float32
    )
    trailing = jnp.broadcast_to(
        trail_ref[0][:, None, :], (head_count, step_rows, piece_len)
    ).reshape(row_count, piece_len)
    scores = scores * (HEAD_DIM ** (-0.5)) + (trailing + prefix_ref[0])
    live = live_ref[0] > 0.5
    row_max = jnp.max(jnp.where(live, scores, neg_fill), axis=1, keepdims=True)
    weights = jnp.where(live, jnp.exp(scores - row_max), 0.0)
    weight_sum = jnp.sum(weights, axis=1, keepdims=True)
    blocks = jnp.dot(weights.astype(jnp.bfloat16), v_ref[0], preferred_element_type=jnp.float32)
    row = lax.broadcasted_iota(jnp.int32, (row_count, 128), 0)
    picked = jnp.zeros((row_count, 128), jnp.float32)
    for pair in range(pair_count):
        lo = 2 * pair * step_rows
        picked = jnp.where(
            (row >= lo) & (row < lo + 2 * step_rows), blocks[:, pair * 128 : (pair + 1) * 128], picked
        )
    odd = (row // step_rows) % 2 == 1
    accum = jnp.where(odd, pltpu.roll(picked, 64, 1), picked)
    lane = lax.broadcasted_iota(jnp.int32, (row_count, 128), 1)
    packed = jnp.where(lane < HEAD_DIM, accum, 0.0)
    packed = jnp.where(lane == HEAD_DIM, row_max, packed)
    packed = jnp.where(lane == HEAD_DIM + 1, weight_sum, packed)
    packed = jnp.where(lane == HEAD_DIM + 2, total_ref[0], packed)
    own_heads = out_ref.shape[2]
    for head in range(head_count):
        out_ref[head // own_heads, 0, head % own_heads] = packed[head * step_rows : (head + 1) * step_rows]


def piece_attention(query_rows, keys, values, trailing, prefix_rows, live_row, total_rows, seq_count):
    req_count, step_rows, inner_width = query_rows.shape
    head_count = trailing.shape[1]
    piece_len = keys.shape[1]
    row_count = head_count * step_rows
    own_heads = head_count // seq_count
    return pl.pallas_call(
        attention_kernel,
        grid=(req_count,),
        in_specs=[
            pl.BlockSpec((1, step_rows, inner_width), lambda r: (r, 0, 0)),
            pl.BlockSpec((1, piece_len, inner_width), lambda r: (r, 0, 0)),
            pl.BlockSpec((1, piece_len, inner_width), lambda r: (r, 0, 0)),
            pl.BlockSpec((1, head_count, piece_len), lambda r: (r, 0, 0)),
            pl.BlockSpec((1, row_count, 1), lambda r: (r, 0, 0)),
            pl.BlockSpec((1, 1, piece_len), lambda r: (r, 0, 0)),
            pl.BlockSpec((1, row_count, 1), lambda r: (r, 0, 0)),
        ],
        out_specs=pl.BlockSpec((seq_count, 1, own_heads, step_rows, 128), lambda r: (0, r, 0, 0, 0)),
        out_shape=jax.ShapeDtypeStruct((seq_count, req_count, own_heads, step_rows, 128), jnp.float32),
    )(query_rows, keys, values, trailing, prefix_rows, live_row, total_rows)


def body(
    hidden_in,
    norm_gain,
    w_qkv,
    w_forget,
    forget_bias,
    cache_keys,
    cache_values,
    cache_forget,
    cache_lengths,
    piece_map,
    draft_counts,
):
    req_count, new_count, width = hidden_in.shape
    head_count = w_forget.shape[1]
    seq_count = lax.axis_size("seq")
    fsdp_count = lax.axis_size("fsdp")
    own_heads = w_qkv.shape[2]
    own_dims = w_qkv.shape[3]
    own_cols = 3 * own_heads * own_dims
    rows = req_count * new_count
    inner_width = head_count * HEAD_DIM
    piece_len = cache_forget.shape[2]
    logit_scale = HEAD_DIM ** (-0.5)
    seq_index = lax.axis_index("seq")
    head_start = seq_index * own_heads
    hidden_all = lax.all_to_all(
        jnp.broadcast_to(hidden_in[None], (fsdp_count, req_count, new_count, width)),
        "fsdp",
        0,
        0,
        tiled=True,
    )
    normed_all = normalize(hidden_all, norm_gain).reshape(fsdp_count * rows, width)
    normed = normalize(hidden_in, norm_gain).reshape(rows, width)
    projected = jnp.einsum(
        "dk,nd->kn",
        w_qkv.reshape(width, own_cols),
        normed_all,
        preferred_element_type=jnp.float32,
    ).astype(jnp.bfloat16)
    outgoing = (
        projected.reshape(3, own_heads * own_dims, fsdp_count, rows)
        .transpose(2, 1, 0, 3)
        .reshape(fsdp_count, 1, own_heads * own_dims * 3 * rows)
    )
    outgoing = jnp.broadcast_to(
        outgoing, (fsdp_count, seq_count, own_heads * own_dims * 3 * rows)
    ).reshape(fsdp_count * seq_count, 2, own_heads * own_dims * 3 * rows // 2)
    incoming = lax.all_to_all(outgoing, ("fsdp", "seq"), 0, 0, tiled=True)
    incoming = incoming.reshape(fsdp_count * seq_count * own_heads * own_dims, 3 * rows)
    src_row = jnp.arange(fsdp_count * seq_count * own_heads * own_dims, dtype=jnp.int32)
    src_dev = src_row // (own_heads * own_dims)
    src_head = (src_row // own_dims) % own_heads
    src_dim = src_row % own_dims
    target = ((src_dev % seq_count) * own_heads + src_head) * HEAD_DIM + (
        src_dev // seq_count
    ) * own_dims + src_dim
    placement = (target[:, None] == jnp.arange(inner_width, dtype=jnp.int32)[None, :]).astype(
        jnp.bfloat16
    )
    all_heads = jnp.einsum(
        "kx,kj->xj", incoming, placement, preferred_element_type=jnp.float32
    ).astype(jnp.bfloat16).reshape(3, req_count, new_count, inner_width)
    gate_logit = (
        jnp.dot(normed, w_forget, preferred_element_type=jnp.float32).reshape(
            req_count, new_count, head_count
        )
        + forget_bias
    )
    prefix = jnp.cumsum(jax.nn.log_sigmoid(gate_logit), axis=1)
    slot_ids = jnp.arange(seq_count, dtype=jnp.int32)
    holders = piece_map[:, :, None] == slot_ids[None, None, :]
    piece_of_slot = jnp.sum(jnp.where(holders, slot_ids[None, :, None], 0), axis=1)
    own_piece = jnp.sum(jnp.where(piece_map == seq_index, slot_ids[None, :], 0), axis=1)
    steps = jnp.arange(piece_len, dtype=jnp.int32)
    positions = own_piece[:, None] * piece_len + steps[None, :]
    live_mask = positions < cache_lengths[:, None]
    masked = jnp.where(live_mask[:, None, :], cache_forget, 0.0)
    piece_total = jnp.sum(masked, axis=-1)
    later_step = (steps[:, None] > steps[None, :]).astype(jnp.float32)
    trailing_part = jnp.einsum(
        "rhl,lj->rhj", masked, later_step, precision=lax.Precision.HIGHEST,
        preferred_element_type=jnp.float32,
    )
    step_rows = 8
    pad_steps = ((0, 0), (0, step_rows - new_count))
    query_rows = jnp.pad(all_heads[0], pad_steps + ((0, 0),))
    prefix_rows = jnp.pad(jnp.transpose(prefix, (0, 2, 1)), ((0, 0),) + pad_steps).reshape(
        req_count, head_count * step_rows, 1
    )
    live_row = live_mask.astype(jnp.float32)[:, None, :]
    total_rows = jnp.broadcast_to(
        piece_total[:, :, None], (req_count, head_count, step_rows)
    ).reshape(req_count, head_count * step_rows, 1)
    packed = piece_attention(
        query_rows, cache_keys, cache_values, trailing_part, prefix_rows, live_row, total_rows, seq_count
    )
    parts = lax.all_to_all(packed, "seq", 0, 0, tiled=True)[:, :, :, :new_count]
    part_acc = parts[..., :HEAD_DIM]
    part_max = parts[..., HEAD_DIM]
    part_sum = parts[..., HEAD_DIM + 1]
    part_total = parts[:, :, :, 0, HEAD_DIM + 2]
    later_piece = (piece_of_slot.T[None, :, :] > piece_of_slot.T[:, None, :])[..., None]
    later_sum = jnp.sum(jnp.where(later_piece, part_total[None], 0.0), axis=1)
    part_max = part_max + later_sum[..., None]
    cache_max = jnp.max(part_max, axis=0)
    factor = jnp.exp(part_max - cache_max[None])
    cache_sum = jnp.sum(part_sum * factor, axis=0)
    cache_acc = jnp.sum(part_acc * factor[..., None], axis=0)
    own_rows = lax.dynamic_slice_in_dim(
        all_heads, head_start * HEAD_DIM, own_heads * HEAD_DIM, 3
    ).reshape(3, req_count, new_count, own_heads, HEAD_DIM)
    own_prefix = jnp.transpose(
        lax.dynamic_slice_in_dim(prefix, head_start, own_heads, 2), (0, 2, 1)
    )
    fresh_logits = (
        jnp.einsum(
            "rmhd,rnhd->rhmn",
            own_rows[0],
            own_rows[1],
            preferred_element_type=jnp.float32,
        )
        * logit_scale
    )
    fresh_logits = fresh_logits + own_prefix[..., :, None] - own_prefix[..., None, :]
    step_ids = jnp.arange(new_count, dtype=jnp.int32)
    causal = (step_ids[None, :] <= step_ids[:, None])[None, None]
    joint_max = jnp.maximum(cache_max, jnp.max(jnp.where(causal, fresh_logits, neg_fill), axis=-1))
    new_weights = jnp.where(causal, jnp.exp(fresh_logits - joint_max[..., None]), 0.0)
    carried = jnp.exp(cache_max - joint_max)
    total_sum = cache_sum * carried + jnp.sum(new_weights, axis=-1)
    blend_weights = cache_acc * carried[..., None] + jnp.einsum(
        "rhmn,rnhd->rhmd",
        new_weights.astype(jnp.bfloat16),
        own_rows[2],
        preferred_element_type=jnp.float32,
    )
    result = blend_weights / total_sum[..., None]
    live_rows = (step_ids[None, :] <= draft_counts[:, None])[:, None, :, None]
    result = jnp.where(live_rows, result, 0.0)
    step_major = (
        jnp.transpose(result, (2, 0, 1, 3))
        .reshape(new_count, req_count, own_heads * HEAD_DIM)
        .astype(jnp.bfloat16)
    )
    return jnp.transpose(step_major, (1, 0, 2))


def solution(mesh):
    in_specs = (
        P("fsdp", None, None),
        P(),
        P(None, None, "seq", "fsdp"),
        P(),
        P(),
        P("fsdp", "seq", None),
        P("fsdp", "seq", None),
        P("fsdp", None, "seq"),
        P("fsdp"),
        P("fsdp", None),
        P("fsdp"),
    )
    out_specs = P("fsdp", None, "seq")
    return jax.shard_map(body, mesh=mesh, in_specs=in_specs, out_specs=out_specs, check_vma=False)
```

```python
import jax
import jax.numpy as jnp
from jax import lax
from jax.experimental import pallas as pl
from jax.experimental.pallas import tpu as pltpu
from jax.sharding import PartitionSpec as P

HEAD_DIM = 64


norm_eps = 1e-06
neg_fill = -1e30


def normalize(rows, gain):
    values = rows.astype(jnp.float32)
    mean_sq = jnp.mean(values * values, axis=-1, keepdims=True)
    return (values * lax.rsqrt(mean_sq + norm_eps) * gain).astype(jnp.bfloat16)


def attention_kernel(q_ref, k_ref, v_ref, trail_ref, prefix_ref, live_ref, total_ref, out_ref):
    step_rows = q_ref.shape[1]
    head_count = trail_ref.shape[1]
    piece_len = trail_ref.shape[2]
    inner_width = q_ref.shape[2]
    row_count = head_count * step_rows
    pair_count = inner_width // 128
    row_step = lax.broadcasted_iota(jnp.int32, (row_count, step_rows), 0) % step_rows
    spread = (row_step == lax.broadcasted_iota(jnp.int32, (row_count, step_rows), 1)).astype(jnp.bfloat16)
    repeated = jnp.dot(spread, q_ref[0], preferred_element_type=jnp.float32)
    row_head = lax.broadcasted_iota(jnp.int32, (row_count, inner_width), 0) // step_rows
    col_head = lax.broadcasted_iota(jnp.int32, (row_count, inner_width), 1) // HEAD_DIM
    query_blocks = jnp.where(row_head == col_head, repeated, 0.0).astype(jnp.bfloat16)
    scores = lax.dot_general(
        query_blocks, k_ref[0], (((1,), (1,)), ((), ())), preferred_element_type=jnp.float32
    )
    trailing = jnp.broadcast_to(
        trail_ref[0][:, None, :], (head_count, step_rows, piece_len)
    ).reshape(row_count, piece_len)
    scores = scores * (HEAD_DIM ** (-0.5)) + (trailing + prefix_ref[0])
    live = live_ref[0] > 0.5
    row_max = jnp.max(jnp.where(live, scores, neg_fill), axis=1, keepdims=True)
    weights = jnp.where(live, jnp.exp(scores - row_max), 0.0)
    weight_sum = jnp.sum(weights, axis=1, keepdims=True)
    blocks = jnp.dot(weights.astype(jnp.bfloat16), v_ref[0], preferred_element_type=jnp.float32)
    row = lax.broadcasted_iota(jnp.int32, (row_count, 128), 0)
    picked = jnp.zeros((row_count, 128), jnp.float32)
    for pair in range(pair_count):
        lo = 2 * pair * step_rows
        picked = jnp.where(
            (row >= lo) & (row < lo + 2 * step_rows), blocks[:, pair * 128 : (pair + 1) * 128], picked
        )
    odd = (row // step_rows) % 2 == 1
    accum = jnp.where(odd, pltpu.roll(picked, 64, 1), picked)
    lane = lax.broadcasted_iota(jnp.int32, (row_count, 128), 1)
    packed = jnp.where(lane < HEAD_DIM, accum, 0.0)
    packed = jnp.where(lane == HEAD_DIM, row_max, packed)
    packed = jnp.where(lane == HEAD_DIM + 1, weight_sum, packed)
    packed = jnp.where(lane == HEAD_DIM + 2, total_ref[0], packed)
    own_heads = out_ref.shape[2]
    for head in range(head_count):
        out_ref[head // own_heads, 0, head % own_heads] = packed[head * step_rows : (head + 1) * step_rows]


def piece_attention(query_rows, keys, values, trailing, prefix_rows, live_row, total_rows, seq_count):
    req_count, step_rows, inner_width = query_rows.shape
    head_count = trailing.shape[1]
    piece_len = keys.shape[1]
    row_count = head_count * step_rows
    own_heads = head_count // seq_count
    return pl.pallas_call(
        attention_kernel,
        grid=(req_count,),
        in_specs=[
            pl.BlockSpec((1, step_rows, inner_width), lambda r: (r, 0, 0)),
            pl.BlockSpec((1, piece_len, inner_width), lambda r: (r, 0, 0)),
            pl.BlockSpec((1, piece_len, inner_width), lambda r: (r, 0, 0)),
            pl.BlockSpec((1, head_count, piece_len), lambda r: (r, 0, 0)),
            pl.BlockSpec((1, row_count, 1), lambda r: (r, 0, 0)),
            pl.BlockSpec((1, 1, piece_len), lambda r: (r, 0, 0)),
            pl.BlockSpec((1, row_count, 1), lambda r: (r, 0, 0)),
        ],
        out_specs=pl.BlockSpec((seq_count, 1, own_heads, step_rows, 128), lambda r: (0, r, 0, 0, 0)),
        out_shape=jax.ShapeDtypeStruct((seq_count, req_count, own_heads, step_rows, 128), jnp.float32),
    )(query_rows, keys, values, trailing, prefix_rows, live_row, total_rows)


def body(
    hidden_in,
    norm_gain,
    w_qkv,
    w_forget,
    forget_bias,
    cache_keys,
    cache_values,
    cache_forget,
    cache_lengths,
    piece_map,
    draft_counts,
):
    req_count, new_count, width = hidden_in.shape
    head_count = w_forget.shape[1]
    seq_count = lax.axis_size("seq")
    fsdp_count = lax.axis_size("fsdp")
    own_heads = w_qkv.shape[2]
    own_dims = w_qkv.shape[3]
    own_cols = 3 * own_heads * own_dims
    rows = req_count * new_count
    inner_width = head_count * HEAD_DIM
    piece_len = cache_forget.shape[2]
    logit_scale = HEAD_DIM ** (-0.5)
    seq_index = lax.axis_index("seq")
    head_start = seq_index * own_heads
    hidden_all = lax.all_to_all(
        jnp.broadcast_to(hidden_in[None], (fsdp_count, req_count, new_count, width)),
        "fsdp",
        0,
        0,
        tiled=True,
    )
    normed_all = normalize(hidden_all, norm_gain).reshape(fsdp_count * rows, width)
    normed = normalize(hidden_in, norm_gain).reshape(rows, width)
    projected = jnp.einsum(
        "dk,nd->kn",
        w_qkv.reshape(width, own_cols),
        normed_all,
        preferred_element_type=jnp.float32,
    ).astype(jnp.bfloat16)
    outgoing = (
        projected.reshape(3, own_heads * own_dims, fsdp_count, rows)
        .transpose(2, 1, 0, 3)
        .reshape(fsdp_count, 1, own_heads * own_dims * 3 * rows)
    )
    outgoing = jnp.broadcast_to(
        outgoing, (fsdp_count, seq_count, own_heads * own_dims * 3 * rows)
    ).reshape(fsdp_count * seq_count, 6, own_heads * own_dims * 3 * rows // 6)
    incoming = lax.all_to_all(outgoing, ("fsdp", "seq"), 0, 0, tiled=True)
    incoming = incoming.reshape(fsdp_count * seq_count * own_heads * own_dims, 3 * rows)
    src_row = jnp.arange(fsdp_count * seq_count * own_heads * own_dims, dtype=jnp.int32)
    src_dev = src_row // (own_heads * own_dims)
    src_head = (src_row // own_dims) % own_heads
    src_dim = src_row % own_dims
    target = ((src_dev % seq_count) * own_heads + src_head) * HEAD_DIM + (
        src_dev // seq_count
    ) * own_dims + src_dim
    placement = (target[:, None] == jnp.arange(inner_width, dtype=jnp.int32)[None, :]).astype(
        jnp.bfloat16
    )
    all_heads = jnp.einsum(
        "kx,kj->xj", incoming, placement, preferred_element_type=jnp.float32
    ).astype(jnp.bfloat16).reshape(3, req_count, new_count, inner_width)
    gate_logit = (
        jnp.dot(normed, w_forget, preferred_element_type=jnp.float32).reshape(
            req_count, new_count, head_count
        )
        + forget_bias
    )
    prefix = jnp.cumsum(jax.nn.log_sigmoid(gate_logit), axis=1)
    slot_ids = jnp.arange(seq_count, dtype=jnp.int32)
    holders = piece_map[:, :, None] == slot_ids[None, None, :]
    piece_of_slot = jnp.sum(jnp.where(holders, slot_ids[None, :, None], 0), axis=1)
    own_piece = jnp.sum(jnp.where(piece_map == seq_index, slot_ids[None, :], 0), axis=1)
    steps = jnp.arange(piece_len, dtype=jnp.int32)
    positions = own_piece[:, None] * piece_len + steps[None, :]
    live_mask = positions < cache_lengths[:, None]
    masked = jnp.where(live_mask[:, None, :], cache_forget, 0.0)
    piece_total = jnp.sum(masked, axis=-1)
    later_step = (steps[:, None] > steps[None, :]).astype(jnp.float32)
    trailing_part = jnp.einsum(
        "rhl,lj->rhj", masked, later_step, precision=lax.Precision.HIGHEST,
        preferred_element_type=jnp.float32,
    )
    step_rows = 8
    pad_steps = ((0, 0), (0, step_rows - new_count))
    query_rows = jnp.pad(all_heads[0], pad_steps + ((0, 0),))
    prefix_rows = jnp.pad(jnp.transpose(prefix, (0, 2, 1)), ((0, 0),) + pad_steps).reshape(
        req_count, head_count * step_rows, 1
    )
    live_row = live_mask.astype(jnp.float32)[:, None, :]
    total_rows = jnp.broadcast_to(
        piece_total[:, :, None], (req_count, head_count, step_rows)
    ).reshape(req_count, head_count * step_rows, 1)
    packed = piece_attention(
        query_rows, cache_keys, cache_values, trailing_part, prefix_rows, live_row, total_rows, seq_count
    )
    parts = lax.all_to_all(packed, "seq", 0, 0, tiled=True)[:, :, :, :new_count]
    part_acc = parts[..., :HEAD_DIM]
    part_max = parts[..., HEAD_DIM]
    part_sum = parts[..., HEAD_DIM + 1]
    part_total = parts[:, :, :, 0, HEAD_DIM + 2]
    later_piece = (piece_of_slot.T[None, :, :] > piece_of_slot.T[:, None, :])[..., None]
    later_sum = jnp.sum(jnp.where(later_piece, part_total[None], 0.0), axis=1)
    part_max = part_max + later_sum[..., None]
    cache_max = jnp.max(part_max, axis=0)
    factor = jnp.exp(part_max - cache_max[None])
    cache_sum = jnp.sum(part_sum * factor, axis=0)
    cache_acc = jnp.sum(part_acc * factor[..., None], axis=0)
    own_rows = lax.dynamic_slice_in_dim(
        all_heads, head_start * HEAD_DIM, own_heads * HEAD_DIM, 3
    ).reshape(3, req_count, new_count, own_heads, HEAD_DIM)
    own_prefix = jnp.transpose(
        lax.dynamic_slice_in_dim(prefix, head_start, own_heads, 2), (0, 2, 1)
    )
    fresh_logits = (
        jnp.einsum(
            "rmhd,rnhd->rhmn",
            own_rows[0],
            own_rows[1],
            preferred_element_type=jnp.float32,
        )
        * logit_scale
    )
    fresh_logits = fresh_logits + own_prefix[..., :, None] - own_prefix[..., None, :]
    step_ids = jnp.arange(new_count, dtype=jnp.int32)
    causal = (step_ids[None, :] <= step_ids[:, None])[None, None]
    joint_max = jnp.maximum(cache_max, jnp.max(jnp.where(causal, fresh_logits, neg_fill), axis=-1))
    new_weights = jnp.where(causal, jnp.exp(fresh_logits - joint_max[..., None]), 0.0)
    carried = jnp.exp(cache_max - joint_max)
    total_sum = cache_sum * carried + jnp.sum(new_weights, axis=-1)
    blend_weights = cache_acc * carried[..., None] + jnp.einsum(
        "rhmn,rnhd->rhmd",
        new_weights.astype(jnp.bfloat16),
        own_rows[2],
        preferred_element_type=jnp.float32,
    )
    result = blend_weights / total_sum[..., None]
    live_rows = (step_ids[None, :] <= draft_counts[:, None])[:, None, :, None]
    result = jnp.where(live_rows, result, 0.0)
    return (
        jnp.transpose(result, (0, 2, 1, 3))
        .reshape(req_count, new_count, own_heads * HEAD_DIM)
        .astype(jnp.bfloat16)
    )


def solution(mesh):
    in_specs = (
        P("fsdp", None, None),
        P(),
        P(None, None, "seq", "fsdp"),
        P(),
        P(),
        P("fsdp", "seq", None),
        P("fsdp", "seq", None),
        P("fsdp", None, "seq"),
        P("fsdp"),
        P("fsdp", None),
        P("fsdp"),
    )
    out_specs = P("fsdp", None, "seq")
    return jax.shard_map(body, mesh=mesh, in_specs=in_specs, out_specs=out_specs, check_vma=False)
```
